32 devices in a mesh: groups: 2 (over y), tp: 16 (over z, x, core).
Axes of the slice: x: 2, y: 2, z: 4, core: 2. Of those that a mesh axis runs over, the one named last changes fastest.
Arguments:
- hidden_in: bfloat16 [32, 8, 512], P(('groups', 'tp')), parts along dimension 0, may hold values from -6 to 6
- norm_gain: float32 [8192], replicated, may hold values from 0.1 to 1.9
- q_blocks: bfloat16 [16, 16, 128, 2048], P('tp'), may hold values from -0.0625 to 0.0625
- o_blocks: bfloat16 [16, 2048, 16, 128], P('tp'), may hold values from -1.5 to 1.5
- kv_blocks: bfloat16 [2, 1024, 8192], P(None, None, 'tp'), may hold values from -0.0625 to 0.0625
- kv_assign: int32 [16], replicated, may hold values from 0 to 7, as said below
- key_cache: bfloat16 [32, 8, 2048, 128], P(('groups', 'tp')), parts along dimension 0, may hold values from -240 to 240
- value_cache: bfloat16 [32, 8, 2048, 128], P(('groups', 'tp')), parts along dimension 0, may hold values from -6 to 6
- lengths: int32 [32, 8], P(('groups', 'tp')), parts along dimension 0, may hold values from 1 to 2048, as said below
Outputs:
- attn_out: bfloat16 [32, 8, 512], P(('groups', 'tp')), parts along dimension 0
The draws below stay inside these ranges and needn't reach their ends.
There are 2 independent parts, one for each index of `groups`. The reference program is written for one: setup_inputs(seed, part) draws one part's arguments, and reference() takes and returns one part's arrays. A program takes and returns all parts, laid end to end along the dimension named above; an argument that names none is the same for every part. Nothing has to cross between parts.
Inputs may be any that keep to these rules, and one draw needn't show every extreme that they name: `kv_assign`: entries 2m and 2m + 1 are equal, and each of the 8 key-value heads is named by exactly two entries. `lengths`: in every rank one row has all 2048 positions valid.
All inputs are finite; a program needn't handle non-finite values.
Results may differ from the reference program's by a relative error of at most 0.011.
The reference program's roundings to bfloat16 on the way count: a program that leaves them out, or rounds other values in their place, can miss the bound.
Values may be sent and summed in bfloat16 or wider, within the bound.
No kernel may reach another device: no remote copies, remote signals or barrier semaphores. Data moves between devices by JAX's collectives and lax.ppermute only.
A program may use at most 128 MiB of HBM per device.

```python
import jax
import jax.numpy as jnp
from jax import lax

D = 8192
QH = 64
KVH = 8
HD = 128
ROLL = 16
ROWS = 8
RANKS = 16
GR = 4
QG = 16
GC = 4
DS = 512
CTXH = 2048


def draw_kv_assign(key, part):
    order = jax.random.permutation(jax.random.fold_in(key, 11), KVH)
    return jnp.repeat(order, 2).astype(jnp.int32)


def draw_lengths(key, part):
    base = jax.random.randint(jax.random.fold_in(key, 21), (RANKS, ROWS), 1, CTXH + 1)
    chosen = jax.random.randint(jax.random.fold_in(key, 22), (RANKS, 1), 0, ROWS)
    positions = jnp.arange(ROWS, dtype=jnp.int32)[None, :]
    return jnp.where(positions == chosen, CTXH, base).astype(jnp.int32)


def draw_key_cache(key, part):
    base = jnp.clip(jax.random.normal(jax.random.fold_in(key, 31), (RANKS, ROWS, CTXH, HD), jnp.float32), -6.0, 6.0)
    return base.astype(jnp.bfloat16)


def levels(rng, dims, shards, least, high):
    factor_of, own = 1.0, jax.random.fold_in(rng, 6)
    for dim, blocks in shards:
        steps = jnp.exp(jax.random.uniform(jax.random.fold_in(own, dim), (blocks,), jnp.float32, least / len(shards), high / len(shards)))
        factor_of = factor_of * jnp.repeat(steps, dims[dim] // blocks).reshape([-1 if axis == dim else 1 for axis in range(len(dims))])
    return factor_of


def noise(key, dims, width, reach, split=(), kind=jnp.bfloat16):
    array = width * jax.random.normal(key, dims, jnp.float32)
    if split:
        array = array * levels(key, dims, split, -0.22, 0.18)
    return jnp.clip(array, -reach, reach).astype(kind)


def setup_inputs(seed: int = 0, part: int = 0) -> dict:
    splits = jax.random.split(jax.random.key(seed), 10)
    part_keys = jax.random.split(jax.random.fold_in(splits[9], part), 10)
    hidden_in = noise(part_keys[0], (RANKS, ROWS, DS), 1.0, 6.0, ((0, 16),))
    norm_gain = jnp.clip(1.0 + 0.18 * jax.random.normal(splits[1], (D,), jnp.float32), 0.1, 1.9)
    q_blocks = noise(splits[2], (RANKS, QG, HD, D // GC), D ** -0.5, 0.0625, ((0, 16),))
    o_blocks = noise(splits[3], (RANKS, D // GC, QG, HD), (QH * HD // 512) ** -0.5, 1.5, ((0, 16),))
    kv_blocks = noise(splits[4], (2, KVH * HD, D), D ** -0.5, 0.0625, ((2, 16),))
    kv_assign = draw_kv_assign(jax.random.fold_in(splits[9], 71), part)
    key_cache = draw_key_cache(jax.random.fold_in(jax.random.fold_in(splits[9], part), 71), part)
    value_cache = noise(part_keys[7], (RANKS, ROWS, CTXH, HD), 1.0, 6.0, ((0, 16),))
    lengths = draw_lengths(jax.random.fold_in(jax.random.fold_in(splits[9], part), 71), part)
    return dict(hidden_in=hidden_in, norm_gain=norm_gain, q_blocks=q_blocks, o_blocks=o_blocks, kv_blocks=kv_blocks, kv_assign=kv_assign, key_cache=key_cache, value_cache=value_cache, lengths=lengths)


def half_partial(queries, keys, values, valid, key_new, value_new, with_new):
    scale = 1.0 / HD ** 0.5
    scores = jnp.einsum('bmhe,mbte->mbht', queries.astype(jnp.float32), keys.astype(jnp.float32)) * scale
    positions = jnp.arange(CTXH, dtype=jnp.int32)
    masked = positions[None, None, None, :] < valid[:, :, None, None]
    new_score = jnp.einsum('bmhe,bme->mbh', queries.astype(jnp.float32), key_new.astype(jnp.float32)) * scale
    new_score = jnp.where(with_new, new_score, jnp.float32(-1e+30))
    top = jnp.maximum(lax.optimization_barrier(jnp.max(jnp.where(masked, scores, jnp.float32(-1e+30)), axis=-1)), new_score)
    weights = jnp.where(masked, jnp.exp(scores - top[..., None]), jnp.float32(0.0))
    new_weight = jnp.exp(new_score - top)
    total = lax.optimization_barrier(jnp.sum(weights, axis=-1)) + new_weight
    rounded = lax.optimization_barrier(weights.astype(jnp.bfloat16)).astype(jnp.float32)
    new_rounded = lax.optimization_barrier(new_weight.astype(jnp.bfloat16)).astype(jnp.float32)
    summed = jnp.einsum('mbht,mbte->mbhe', rounded, values.astype(jnp.float32))
    summed = summed + new_rounded[..., None] * value_new.astype(jnp.float32).transpose(1, 0, 2)[:, :, None, :]
    return (top, total, summed)

def reference(hidden_in, norm_gain, q_blocks, o_blocks, kv_blocks, kv_assign, key_cache, value_cache, lengths):
    ranks = hidden_in.shape[0]
    groups_count = ranks // ROLL
    grid_cols = ranks // GR
    w_query = q_blocks.reshape(GR, grid_cols, QG, HD, D // grid_cols).transpose(2, 0, 3, 1, 4).reshape(QH * HD, D)
    w_out = o_blocks.reshape(GR, grid_cols, D // grid_cols, QG, HD).transpose(3, 0, 4, 1, 2).reshape(QH * HD, D)
    w_key = kv_blocks[0]
    w_value = kv_blocks[1]
    rows_all = hidden_in.reshape(groups_count, ROLL, ROWS, DS).transpose(0, 2, 1, 3).reshape(groups_count * ROWS, D)
    rows_float = rows_all.astype(jnp.float32)
    mean_square = lax.optimization_barrier(jnp.mean(rows_float * rows_float, axis=-1, keepdims=True))
    normed = (rows_float * lax.rsqrt(mean_square + 1e-05) * norm_gain[None, :]).astype(jnp.bfloat16)
    queries = jnp.dot(normed, w_query.T, preferred_element_type=jnp.float32).astype(jnp.bfloat16)
    key_new = jnp.dot(normed, w_key.T, preferred_element_type=jnp.float32).astype(jnp.bfloat16)
    value_new = jnp.dot(normed, w_value.T, preferred_element_type=jnp.float32).astype(jnp.bfloat16)
    per_group = QH // KVH
    pair_heads = kv_assign[0::2].astype(jnp.int32)
    query_pairs = queries.reshape(groups_count * ROWS, KVH, per_group, HD)[:, pair_heads]
    key_pairs = key_new.reshape(groups_count * ROWS, KVH, HD)[:, pair_heads]
    value_pairs = value_new.reshape(groups_count * ROWS, KVH, HD)[:, pair_heads]
    key_split = key_cache.reshape(groups_count, KVH, 2, ROWS, CTXH, HD)
    value_split = value_cache.reshape(groups_count, KVH, 2, ROWS, CTXH, HD)
    length_split = lengths.reshape(groups_count, KVH, 2, ROWS)

    def one_group(inputs):
        group_queries, group_keys, group_values, group_lengths, group_knew, group_vnew = inputs
        first = half_partial(group_queries, group_keys[:, 0], group_values[:, 0], group_lengths[:, 0], group_knew, group_vnew, True)
        second = half_partial(group_queries, group_keys[:, 1], group_values[:, 1], group_lengths[:, 1], group_knew, group_vnew, False)
        joint = jnp.maximum(first[0], second[0])
        factor_a = jnp.exp(first[0] - joint)
        factor_b = jnp.exp(second[0] - joint)
        numer = first[2] * factor_a[..., None] + second[2] * factor_b[..., None]
        denom = first[1] * factor_a + second[1] * factor_b
        return (numer / denom[..., None]).transpose(1, 0, 2, 3)
    grouped = lax.map(one_group, (query_pairs.reshape(groups_count, ROWS, KVH, per_group, HD), key_split, value_split, length_split, key_pairs.reshape(groups_count, ROWS, KVH, HD), value_pairs.reshape(groups_count, ROWS, KVH, HD)))
    attention = grouped.reshape(groups_count * ROWS, KVH, per_group, HD).astype(jnp.bfloat16)
    head_ids = jnp.arange(KVH, dtype=jnp.int32)
    inverse = lax.optimization_barrier(jnp.sum(head_ids[None, :] * (pair_heads[None, :] == head_ids[:, None]).astype(jnp.int32), axis=1))
    ordered = attention[:, inverse].reshape(groups_count * ROWS, QH * HD)
    result = jnp.dot(ordered, w_out, preferred_element_type=jnp.float32).astype(jnp.bfloat16)
    return result.reshape(groups_count, ROWS, ROLL, DS).transpose(0, 2, 1, 3).reshape(ranks, ROWS, DS)
```

```python
import jax
import jax.numpy as jnp
from jax import lax
from jax.sharding import PartitionSpec as P

D = 8192
KVH = 8
HD = 128
ROLL = 16
ROWS = 8
GR = 4
QG = 16
DS = 512


def from_partner(value, axis, bit):
    mask = 2**bit
    pairs = [(source, source ^ mask) for source in range(lax.axis_size(axis))]
    return lax.ppermute(value, axis, pairs)


def xor_swap(value, axis, bit):
    return from_partner(value, axis, bit)


def gather_xor(value, axis):
    n = lax.axis_size(axis)
    me = lax.axis_index(axis)
    held = value
    for bit in range(n.bit_length() - 1):
        other = xor_swap(held, axis, bit)
        low = ((me >> bit) & 1) == 0
        held = jnp.where(low, jnp.concatenate([held, other], 0), jnp.concatenate([other, held], 0))
    return held


def scatter_sum_xor(pieces, axis):
    n = lax.axis_size(axis)
    bits = n.bit_length() - 1
    me = lax.axis_index(axis)
    held = pieces.reshape((2,) * bits + pieces.shape[1:])
    order = list(range(bits - 1, -1, -1))
    for bit in range(bits):
        pos = order.index(bit)
        order.pop(pos)
        low = ((me >> bit) & 1) == 0
        first = lax.index_in_dim(held, 0, pos, keepdims=False)
        second = lax.index_in_dim(held, 1, pos, keepdims=False)
        keep = jnp.where(low, first, second)
        give = jnp.where(low, second, first)
        held = keep + xor_swap(give, axis, bit)
    return held[None]


def norm_rows(rows_float, norm_gain):
    mean_square = jnp.mean(rows_float * rows_float, axis=-1, keepdims=True)
    return (rows_float * lax.rsqrt(mean_square + 1e-05) * norm_gain[None, :]).astype(jnp.bfloat16)


def local(
    hidden_in, norm_gain, q_blocks, o_blocks, kv_blocks, kv_assign, key_cache, value_cache, lengths
):
    ranks = lax.axis_size("tp")
    my_index = lax.axis_index("tp")
    my_rank = my_index % ROLL
    my_half = my_rank % 2
    grid_cols = ranks // GR
    group_count = ranks // ROLL
    col_width = q_blocks.shape[3]
    key_width = kv_blocks.shape[2]
    grid_row = my_index // grid_cols
    grid_col = my_index % grid_cols
    dest_ids = jnp.arange(ranks, dtype=jnp.int32)
    dest_rank = dest_ids % ROLL
    dest_head = kv_assign[dest_rank]
    dest_group = 2 * dest_head + dest_rank % 2
    dest_copy = dest_ids // ROLL
    every_rows = gather_xor(hidden_in, "tp")
    rows_float = (
        every_rows.reshape(group_count, ROLL, ROWS, DS)
        .transpose(0, 2, 1, 3)
        .reshape(group_count * ROWS, D)
        .astype(jnp.float32)
    )
    normed_every = norm_rows(rows_float, norm_gain)
    col_rows = lax.dynamic_slice_in_dim(normed_every, grid_col * col_width, col_width, 1)
    query_part = jnp.einsum(
        "rc,aec->rae", col_rows, q_blocks[0], preferred_element_type=jnp.float32
    )
    query_part = (
        query_part.reshape(group_count, ROWS, QG, HD)
        .transpose(0, 2, 1, 3)
        .reshape(group_count * QG, ROWS, HD)
    )
    query_pick = jnp.take(query_part, dest_copy * QG + dest_group, axis=0)
    slot_mask = (jnp.arange(GR, dtype=jnp.int32) == grid_row).astype(jnp.float32)
    query_term = (query_pick[:, :, None, :] * slot_mask[None, None, :, None]).reshape(
        ranks, ROWS, GR * HD
    )
    key_rows = lax.dynamic_slice_in_dim(normed_every, my_index * key_width, key_width, 1)
    keyval_part = jnp.einsum("rc,kfc->rkf", key_rows, kv_blocks, preferred_element_type=jnp.float32)
    keyval_part = (
        keyval_part.reshape(group_count, ROWS, 2, KVH, HD)
        .transpose(0, 3, 1, 2, 4)
        .reshape(group_count * KVH, ROWS, 2 * HD)
    )
    keyval_term = jnp.take(keyval_part, dest_copy * KVH + dest_head, axis=0)
    proj_term = jnp.concatenate([query_term, keyval_term], -1).reshape(ranks * ROWS, (GR + 2) * HD)
    projected = scatter_sum_xor(proj_term.reshape(ranks, ROWS, (GR + 2) * HD), "tp")[0]
    queries = projected[:, : GR * HD].astype(jnp.bfloat16)
    keyval_new = projected[:, GR * HD :].astype(jnp.bfloat16)
    key_new = keyval_new[:, :HD]
    value_new = keyval_new[:, HD:]
    partner_queries = from_partner(queries, "tp", 0)
    both_queries = jnp.where(
        my_half == 0,
        jnp.concatenate([queries, partner_queries], 1),
        jnp.concatenate([partner_queries, queries], 1),
    )
    both_queries = both_queries.reshape(ROWS, 2 * GR, HD)
    scale = 1.0 / HD**0.5
    scores = (
        jnp.einsum("bhe,bte->bht", both_queries, key_cache[0], preferred_element_type=jnp.float32)
        * scale
    )
    positions = jnp.arange(scores.shape[2], dtype=jnp.int32)
    masked = positions[None, None, :] < lengths[0][:, None, None]
    new_score = (
        jnp.einsum("bhe,be->bh", both_queries, key_new, preferred_element_type=jnp.float32) * scale
    )
    new_score = jnp.where(my_half == 0, new_score, jnp.float32(-1e30))
    top = jnp.maximum(jnp.max(jnp.where(masked, scores, jnp.float32(-1e30)), axis=-1), new_score)
    weights = jnp.where(masked, jnp.exp(scores - top[..., None]), jnp.float32(0.0))
    new_weight = jnp.exp(new_score - top)
    total = jnp.sum(weights, axis=-1) + new_weight
    summed = jnp.einsum(
        "bht,bte->bhe",
        weights.astype(jnp.bfloat16),
        value_cache[0],
        preferred_element_type=jnp.float32,
    )
    new_rounded = lax.optimization_barrier(new_weight.astype(jnp.bfloat16)).astype(jnp.float32)
    summed = summed + new_rounded[..., None] * value_new.astype(jnp.float32)[:, None, :]
    top_split = top.reshape(ROWS, 2, GR)
    total_split = total.reshape(ROWS, 2, GR)
    summed_split = summed.reshape(ROWS, 2, GR, HD)
    first_half = my_half == 0
    own_top = jnp.where(first_half, top_split[:, 0], top_split[:, 1])
    own_total = jnp.where(first_half, total_split[:, 0], total_split[:, 1])
    own_summed = jnp.where(first_half, summed_split[:, 0], summed_split[:, 1])
    give_top = jnp.where(first_half, top_split[:, 1], top_split[:, 0])
    give_total = jnp.where(first_half, total_split[:, 1], total_split[:, 0])
    give_summed = jnp.where(first_half, summed_split[:, 1], summed_split[:, 0])
    got_top, got_total, got_summed = from_partner((give_top, give_total, give_summed), "tp", 0)
    joint = jnp.maximum(own_top, got_top)
    factor_own = jnp.exp(own_top - joint)
    factor_got = jnp.exp(got_top - joint)
    numer = own_summed * factor_own[..., None] + got_summed * factor_got[..., None]
    denom = own_total * factor_own + got_total * factor_got
    attention = (numer / denom[..., None]).astype(jnp.bfloat16).reshape(ROWS, GR * HD)
    every_attn = gather_xor(attention[None], "tp")
    head_ids = jnp.arange(KVH, dtype=jnp.int32)
    pair_heads = kv_assign[0::2]
    inverse = jnp.sum(
        head_ids[None, :] * (pair_heads[None, :] == head_ids[:, None]).astype(jnp.int32), axis=1
    )
    slot_ids = jnp.arange(QG, dtype=jnp.int32)
    rank_of_slot = 2 * inverse[slot_ids // 2] + slot_ids % 2
    attn_grid = every_attn.reshape(group_count, ROLL, ROWS, GR, HD)
    row_slot = lax.dynamic_index_in_dim(attn_grid, grid_row, 3, keepdims=False)
    chosen = jnp.take(row_slot, rank_of_slot, axis=1)
    out_part = jnp.einsum("gabe,cae->gbc", chosen, o_blocks[0], preferred_element_type=jnp.float32)
    placed = jnp.zeros((group_count, ROWS, D), jnp.float32)
    placed = lax.dynamic_update_slice_in_dim(placed, out_part, grid_col * col_width, 2)
    out_term = (
        placed.reshape(group_count, ROWS, ROLL, DS).transpose(0, 2, 1, 3).reshape(ranks * ROWS, DS)
    )
    my_cols = scatter_sum_xor(out_term.reshape(ranks, ROWS, DS), "tp")[0]
    return my_cols.astype(jnp.bfloat16)[None]


def solution(mesh):
    return jax.shard_map(
        local,
        mesh=mesh,
        in_specs=(
            P(("groups", "tp"), None, None),
            P(),
            P("tp", None, None, None),
            P("tp", None, None, None),
            P(None, None, "tp"),
            P(),
            P(("groups", "tp"), None, None, None),
            P(("groups", "tp"), None, None, None),
            P(("groups", "tp"), None),
        ),
        out_specs=P(("groups", "tp"), None, None),
        check_vma=False,
    )
```

```python
import jax
import jax.numpy as jnp
from jax import lax
from jax.sharding import PartitionSpec as P

D = 8192
KVH = 8
HD = 128
ROLL = 16
ROWS = 8
GR = 4
QG = 16
DS = 512


def from_partner(value, axis, bit):
    mask = 2**bit
    pairs = [(source, source ^ mask) for source in range(lax.axis_size(axis))]
    return lax.ppermute(value, axis, pairs)


def xor_swap(value, axis, bit):
    return from_partner(value, axis, bit)


def gather_xor(value, axis):
    n = lax.axis_size(axis)
    me = lax.axis_index(axis)
    held = value
    for bit in range(n.bit_length() - 1):
        other = xor_swap(held, axis, bit)
        low = ((me >> bit) & 1) == 0
        held = jnp.where(low, jnp.concatenate([held, other], 0), jnp.concatenate([other, held], 0))
    return held


def scatter_rounds(held, order, axis, bits):
    me = lax.axis_index(axis)
    for bit in bits:
        pos = order.index(bit)
        order = order[:pos] + order[pos + 1 :]
        low = ((me >> bit) & 1) == 0
        first = lax.index_in_dim(held, 0, pos, keepdims=False)
        second = lax.index_in_dim(held, 1, pos, keepdims=False)
        keep = jnp.where(low, first, second)
        give = jnp.where(low, second, first)
        held = keep + xor_swap(give, axis, bit)
    return held, order


def scatter_sum_xor(pieces, axis):
    n = lax.axis_size(axis)
    bits = n.bit_length() - 1
    me = lax.axis_index(axis)
    held = pieces.reshape((2,) * bits + pieces.shape[1:])
    order = list(range(bits - 1, -1, -1))
    for bit in range(bits):
        pos = order.index(bit)
        order.pop(pos)
        low = ((me >> bit) & 1) == 0
        first = lax.index_in_dim(held, 0, pos, keepdims=False)
        second = lax.index_in_dim(held, 1, pos, keepdims=False)
        keep = jnp.where(low, first, second)
        give = jnp.where(low, second, first)
        held = keep + xor_swap(give, axis, bit)
    return held[None]


def norm_rows(rows_float, norm_gain):
    mean_square = jnp.mean(rows_float * rows_float, axis=-1, keepdims=True)
    return (rows_float * lax.rsqrt(mean_square + 1e-05) * norm_gain[None, :]).astype(jnp.bfloat16)


def local(
    hidden_in, norm_gain, q_blocks, o_blocks, kv_blocks, kv_assign, key_cache, value_cache, lengths
):
    ranks = lax.axis_size("tp")
    my_index = lax.axis_index("tp")
    my_rank = my_index % ROLL
    my_half = my_rank % 2
    grid_cols = ranks // GR
    group_count = ranks // ROLL
    col_width = q_blocks.shape[3]
    key_width = kv_blocks.shape[2]
    grid_row = my_index // grid_cols
    grid_col = my_index % grid_cols
    dest_ids = jnp.arange(ranks, dtype=jnp.int32)
    dest_rank = dest_ids % ROLL
    dest_head = kv_assign[dest_rank]
    dest_group = 2 * dest_head + dest_rank % 2
    dest_copy = dest_ids // ROLL
    every_rows = gather_xor(hidden_in, "tp")
    rows_float = (
        every_rows.reshape(group_count, ROLL, ROWS, DS)
        .transpose(0, 2, 1, 3)
        .reshape(group_count * ROWS, D)
        .astype(jnp.float32)
    )
    normed_every = norm_rows(rows_float, norm_gain)
    col_rows = lax.dynamic_slice_in_dim(normed_every, grid_col * col_width, col_width, 1)
    query_part = jnp.einsum(
        "rc,aec->rae", col_rows, q_blocks[0], preferred_element_type=jnp.float32
    )
    query_part = (
        query_part.reshape(group_count, ROWS, QG, HD)
        .transpose(0, 2, 1, 3)
        .reshape(group_count * QG, ROWS, HD)
    )
    query_pick = jnp.take(query_part, dest_copy * QG + dest_group, axis=0)
    key_rows = lax.dynamic_slice_in_dim(normed_every, my_index * key_width, key_width, 1)
    keyval_part = jnp.einsum("rc,kfc->rkf", key_rows, kv_blocks, preferred_element_type=jnp.float32)
    keyval_part = (
        keyval_part.reshape(group_count, ROWS, 2, KVH, HD)
        .transpose(0, 3, 1, 2, 4)
        .reshape(group_count * KVH, ROWS, 2 * HD)
    )
    keyval_term = jnp.take(keyval_part, dest_copy * KVH + dest_head, axis=0)
    bits = ranks.bit_length() - 1
    col_bits = grid_cols.bit_length() - 1
    compact = jnp.concatenate([query_pick, keyval_term], -1)
    held, order = scatter_rounds(
        compact.reshape((2,) * bits + (ROWS, 3 * HD)), list(range(bits - 1, -1, -1)), "tp", range(col_bits)
    )
    slot_here = jnp.arange(GR, dtype=jnp.int32) == grid_row
    query_slots = jnp.where(
        slot_here[:, None], held[..., None, :HD], jnp.zeros((), jnp.float32)
    ).reshape(held.shape[:-1] + (GR * HD,))
    held = jnp.concatenate([query_slots, held[..., HD:]], -1)
    projected, _ = scatter_rounds(held, order, "tp", range(col_bits, bits))
    queries = projected[:, : GR * HD].astype(jnp.bfloat16)
    keyval_new = projected[:, GR * HD :].astype(jnp.bfloat16)
    key_new = keyval_new[:, :HD]
    value_new = keyval_new[:, HD:]
    partner_queries = from_partner(queries, "tp", 0)
    both_queries = jnp.where(
        my_half == 0,
        jnp.concatenate([queries, partner_queries], 1),
        jnp.concatenate([partner_queries, queries], 1),
    )
    both_queries = both_queries.reshape(ROWS, 2 * GR, HD)
    scale = 1.0 / HD**0.5
    scores = (
        jnp.einsum("bhe,bte->bht", both_queries, key_cache[0], preferred_element_type=jnp.float32)
        * scale
    )
    positions = jnp.arange(scores.shape[2], dtype=jnp.int32)
    masked = positions[None, None, :] < lengths[0][:, None, None]
    new_score = (
        jnp.einsum("bhe,be->bh", both_queries, key_new, preferred_element_type=jnp.float32) * scale
    )
    new_score = jnp.where(my_half == 0, new_score, jnp.float32(-1e30))
    top = jnp.maximum(jnp.max(jnp.where(masked, scores, jnp.float32(-1e30)), axis=-1), new_score)
    weights = jnp.where(masked, jnp.exp(scores - top[..., None]), jnp.float32(0.0))
    new_weight = jnp.exp(new_score - top)
    total = jnp.sum(weights, axis=-1) + new_weight
    summed = jnp.einsum(
        "bht,bte->bhe",
        weights.astype(jnp.bfloat16),
        value_cache[0],
        preferred_element_type=jnp.float32,
    )
    new_rounded = lax.optimization_barrier(new_weight.astype(jnp.bfloat16)).astype(jnp.float32)
    summed = summed + new_rounded[..., None] * value_new.astype(jnp.float32)[:, None, :]
    top_split = top.reshape(ROWS, 2, GR)
    total_split = total.reshape(ROWS, 2, GR)
    summed_split = summed.reshape(ROWS, 2, GR, HD)
    first_half = my_half == 0
    own_top = jnp.where(first_half, top_split[:, 0], top_split[:, 1])
    own_total = jnp.where(first_half, total_split[:, 0], total_split[:, 1])
    own_summed = jnp.where(first_half, summed_split[:, 0], summed_split[:, 1])
    give_top = jnp.where(first_half, top_split[:, 1], top_split[:, 0])
    give_total = jnp.where(first_half, total_split[:, 1], total_split[:, 0])
    give_summed = jnp.where(first_half, summed_split[:, 1], summed_split[:, 0])
    give = jnp.concatenate([give_summed, give_top[..., None], give_total[..., None]], -1)
    got = from_partner(give, "tp", 0)
    got_summed, got_top, got_total = got[..., :HD], got[..., HD], got[..., HD + 1]
    joint = jnp.maximum(own_top, got_top)
    factor_own = jnp.exp(own_top - joint)
    factor_got = jnp.exp(got_top - joint)
    numer = own_summed * factor_own[..., None] + got_summed * factor_got[..., None]
    denom = own_total * factor_own + got_total * factor_got
    attention = (numer / denom[..., None]).astype(jnp.bfloat16).reshape(ROWS, GR * HD)
    every_attn = gather_xor(attention[None], "tp")
    head_ids = jnp.arange(KVH, dtype=jnp.int32)
    pair_heads = kv_assign[0::2]
    inverse = jnp.sum(
        head_ids[None, :] * (pair_heads[None, :] == head_ids[:, None]).astype(jnp.int32), axis=1
    )
    slot_ids = jnp.arange(QG, dtype=jnp.int32)
    rank_of_slot = 2 * inverse[slot_ids // 2] + slot_ids % 2
    attn_grid = every_attn.reshape(group_count, ROLL, ROWS, GR, HD)
    row_slot = lax.dynamic_index_in_dim(attn_grid, grid_row, 3, keepdims=False)
    chosen = jnp.take(row_slot, rank_of_slot, axis=1)
    out_part = jnp.einsum("gabe,cae->gbc", chosen, o_blocks[0], preferred_element_type=jnp.float32)
    if group_count == 1 and grid_cols == GR and col_width == GR * DS:
        col_bits = grid_cols.bit_length() - 1
        row_bits = GR.bit_length() - 1
        pieces = out_part[0].reshape(ROWS, GR, DS).transpose(1, 0, 2)
        held, _ = scatter_rounds(
            pieces.reshape((2,) * row_bits + (ROWS, DS)),
            list(range(col_bits + row_bits - 1, col_bits - 1, -1)),
            "tp",
            range(col_bits, col_bits + row_bits),
        )
        pairs = [(i * grid_cols + j, j * grid_cols + i) for i in range(GR) for j in range(grid_cols)]
        my_cols = lax.ppermute(held, "tp", pairs)
    else:
        placed = jnp.zeros((group_count, ROWS, D), jnp.float32)
        placed = lax.dynamic_update_slice_in_dim(placed, out_part, grid_col * col_width, 2)
        out_term = (
            placed.reshape(group_count, ROWS, ROLL, DS).transpose(0, 2, 1, 3).reshape(ranks * ROWS, DS)
        )
        my_cols = scatter_sum_xor(out_term.reshape(ranks, ROWS, DS), "tp")[0]
    return my_cols.astype(jnp.bfloat16)[None]


def solution(mesh):
    return jax.shard_map(
        local,
        mesh=mesh,
        in_specs=(
            P(("groups", "tp"), None, None),
            P(),
            P("tp", None, None, None),
            P("tp", None, None, None),
            P(None, None, "tp"),
            P(),
            P(("groups", "tp"), None, None, None),
            P(("groups", "tp"), None, None, None),
            P(("groups", "tp"), None),
        ),
        out_specs=P(("groups", "tp"), None, None),
        check_vma=False,
    )
```

```python
import jax
import jax.numpy as jnp
from jax import lax
from jax.sharding import PartitionSpec as P

D = 8192
KVH = 8
HD = 128
ROLL = 16
ROWS = 8
GR = 4
QG = 16
DS = 512


def from_partner(value, axis, bit):
    mask = 2**bit
    pairs = [(source, source ^ mask) for source in range(lax.axis_size(axis))]
    return lax.ppermute(value, axis, pairs)


def xor_swap(value, axis, bit):
    return from_partner(value, axis, bit)


def gather_xor(value, axis):
    n = lax.axis_size(axis)
    me = lax.axis_index(axis)
    held = value
    for bit in range(n.bit_length() - 1):
        other = xor_swap(held, axis, bit)
        low = ((me >> bit) & 1) == 0
        held = jnp.where(low, jnp.concatenate([held, other], 0), jnp.concatenate([other, held], 0))
    return held


def scatter_rounds(held, order, axis, bits):
    me = lax.axis_index(axis)
    for bit in bits:
        pos = order.index(bit)
        order = order[:pos] + order[pos + 1 :]
        low = ((me >> bit) & 1) == 0
        first = lax.index_in_dim(held, 0, pos, keepdims=False)
        second = lax.index_in_dim(held, 1, pos, keepdims=False)
        keep = jnp.where(low, first, second)
        give = jnp.where(low, second, first)
        held = keep + xor_swap(give, axis, bit)
    return held, order


def scatter_sum_xor(pieces, axis):
    n = lax.axis_size(axis)
    bits = n.bit_length() - 1
    me = lax.axis_index(axis)
    held = pieces.reshape((2,) * bits + pieces.shape[1:])
    order = list(range(bits - 1, -1, -1))
    for bit in range(bits):
        pos = order.index(bit)
        order.pop(pos)
        low = ((me >> bit) & 1) == 0
        first = lax.index_in_dim(held, 0, pos, keepdims=False)
        second = lax.index_in_dim(held, 1, pos, keepdims=False)
        keep = jnp.where(low, first, second)
        give = jnp.where(low, second, first)
        held = keep + xor_swap(give, axis, bit)
    return held[None]


def pick(table, idx):
    hit = idx[:, None] == jnp.arange(table.shape[0], dtype=idx.dtype)[None, :]
    hit = hit.reshape(hit.shape + (1,) * (table.ndim - 1))
    return jnp.sum(jnp.where(hit, table[None], jnp.zeros((), table.dtype)), axis=1)


def gather_rounds(held, axis, bits):
    me = lax.axis_index(axis)
    for bit in bits:
        other = xor_swap(held, axis, bit)
        low = ((me >> bit) & 1) == 0
        held = jnp.where(low, jnp.concatenate([held, other], 0), jnp.concatenate([other, held], 0))
    return held


def exchange_rounds(held, axis, bits):
    me = lax.axis_index(axis)
    count = len(bits)
    for done, bit in enumerate(bits):
        low = ((me >> bit) & 1) == 0
        first = lax.index_in_dim(held, 0, 0, keepdims=False)
        second = lax.index_in_dim(held, 1, 0, keepdims=False)
        keep = jnp.where(low, first, second)
        give = jnp.where(low, second, first)
        got = xor_swap(give, axis, bit)
        at = count - done - 1 + done
        held = jnp.where(low, jnp.stack([keep, got], at), jnp.stack([got, keep], at))
    return held


def norm_rows(rows_float, norm_gain):
    mean_square = jnp.mean(rows_float * rows_float, axis=-1, keepdims=True)
    return (rows_float * lax.rsqrt(mean_square + 1e-05) * norm_gain[None, :]).astype(jnp.bfloat16)


def local(
    hidden_in, norm_gain, q_blocks, o_blocks, kv_blocks, kv_assign, key_cache, value_cache, lengths
):
    ranks = lax.axis_size("tp")
    my_index = lax.axis_index("tp")
    my_rank = my_index % ROLL
    my_half = my_rank % 2
    grid_cols = ranks // GR
    group_count = ranks // ROLL
    col_width = q_blocks.shape[3]
    key_width = kv_blocks.shape[2]
    grid_row = my_index // grid_cols
    grid_col = my_index % grid_cols
    dest_ids = jnp.arange(ranks, dtype=jnp.int32)
    dest_rank = dest_ids % ROLL
    dest_head = kv_assign[dest_rank]
    dest_group = 2 * dest_head + dest_rank % 2
    dest_copy = dest_ids // ROLL
    every_rows = gather_xor(hidden_in, "tp")
    rows_float = (
        every_rows.reshape(group_count, ROLL, ROWS, DS)
        .transpose(0, 2, 1, 3)
        .reshape(group_count * ROWS, D)
        .astype(jnp.float32)
    )
    normed_every = norm_rows(rows_float, norm_gain)
    col_rows = lax.dynamic_slice_in_dim(normed_every, grid_col * col_width, col_width, 1)
    query_part = jnp.einsum(
        "rc,aec->rae", col_rows, q_blocks[0], preferred_element_type=jnp.float32
    )
    query_part = (
        query_part.reshape(group_count, ROWS, QG, HD)
        .transpose(0, 2, 1, 3)
        .reshape(group_count * QG, ROWS, HD)
    )
    query_pick = pick(query_part, dest_copy * QG + dest_group)
    key_rows = lax.dynamic_slice_in_dim(normed_every, my_index * key_width, key_width, 1)
    keyval_part = jnp.einsum("rc,kfc->rkf", key_rows, kv_blocks, preferred_element_type=jnp.float32)
    keyval_part = (
        keyval_part.reshape(group_count, ROWS, 2, KVH, HD)
        .transpose(0, 3, 1, 2, 4)
        .reshape(group_count * KVH, ROWS, 2 * HD)
    )
    keyval_term = pick(keyval_part, dest_copy * KVH + dest_head)
    bits = ranks.bit_length() - 1
    col_bits = grid_cols.bit_length() - 1
    compact = jnp.concatenate([query_pick, keyval_term], -1)
    held, order = scatter_rounds(
        compact.reshape((2,) * bits + (ROWS, 3 * HD)), list(range(bits - 1, -1, -1)), "tp", range(col_bits)
    )
    slot_here = jnp.arange(GR, dtype=jnp.int32) == grid_row
    query_slots = jnp.where(
        slot_here[:, None], held[..., None, :HD], jnp.zeros((), jnp.float32)
    ).reshape(held.shape[:-1] + (GR * HD,))
    held = jnp.concatenate([query_slots, held[..., HD:]], -1)
    projected, _ = scatter_rounds(held, order, "tp", range(col_bits, bits))
    queries = projected[:, : GR * HD].astype(jnp.bfloat16)
    keyval_new = projected[:, GR * HD :].astype(jnp.bfloat16)
    key_new = keyval_new[:, :HD]
    value_new = keyval_new[:, HD:]
    partner_queries = from_partner(queries, "tp", 0)
    both_queries = jnp.where(
        my_half == 0,
        jnp.concatenate([queries, partner_queries], 1),
        jnp.concatenate([partner_queries, queries], 1),
    )
    both_queries = both_queries.reshape(ROWS, 2 * GR, HD)
    scale = 1.0 / HD**0.5
    scores = (
        jnp.einsum("bhe,bte->bht", both_queries, key_cache[0], preferred_element_type=jnp.float32)
        * scale
    )
    positions = jnp.arange(scores.shape[2], dtype=jnp.int32)
    masked = positions[None, None, :] < lengths[0][:, None, None]
    new_score = (
        jnp.einsum("bhe,be->bh", both_queries, key_new, preferred_element_type=jnp.float32) * scale
    )
    new_score = jnp.where(my_half == 0, new_score, jnp.float32(-1e30))
    top = jnp.maximum(jnp.max(jnp.where(masked, scores, jnp.float32(-1e30)), axis=-1), new_score)
    weights = jnp.where(masked, jnp.exp(scores - top[..., None]), jnp.float32(0.0))
    new_weight = jnp.exp(new_score - top)
    total = jnp.sum(weights, axis=-1) + new_weight
    summed = jnp.einsum(
        "bht,bte->bhe",
        weights.astype(jnp.bfloat16),
        value_cache[0],
        preferred_element_type=jnp.float32,
    )
    new_rounded = lax.optimization_barrier(new_weight.astype(jnp.bfloat16)).astype(jnp.float32)
    summed = summed + new_rounded[..., None] * value_new.astype(jnp.float32)[:, None, :]
    top_split = top.reshape(ROWS, 2, GR)
    total_split = total.reshape(ROWS, 2, GR)
    summed_split = summed.reshape(ROWS, 2, GR, HD)
    first_half = my_half == 0
    own_top = jnp.where(first_half, top_split[:, 0], top_split[:, 1])
    own_total = jnp.where(first_half, total_split[:, 0], total_split[:, 1])
    own_summed = jnp.where(first_half, summed_split[:, 0], summed_split[:, 1])
    give_top = jnp.where(first_half, top_split[:, 1], top_split[:, 0])
    give_total = jnp.where(first_half, total_split[:, 1], total_split[:, 0])
    give_summed = jnp.where(first_half, summed_split[:, 1], summed_split[:, 0])
    give = jnp.concatenate([give_summed, give_top[..., None], give_total[..., None]], -1)
    got = from_partner(give, "tp", 0)
    got_summed, got_top, got_total = got[..., :HD], got[..., HD], got[..., HD + 1]
    joint = jnp.maximum(own_top, got_top)
    factor_own = jnp.exp(own_top - joint)
    factor_got = jnp.exp(got_top - joint)
    numer = own_summed * factor_own[..., None] + got_summed * factor_got[..., None]
    denom = own_total * factor_own + got_total * factor_got
    attention = (numer / denom[..., None]).astype(jnp.bfloat16)
    bits = ranks.bit_length() - 1
    col_bits = grid_cols.bit_length() - 1
    row_bits = GR.bit_length() - 1
    by_row = attention.transpose(1, 0, 2).reshape((2,) * row_bits + (ROWS, HD))
    by_row = exchange_rounds(by_row, "tp", list(range(bits - 1, col_bits - 1, -1)))
    by_row = by_row.reshape(GR, ROWS, HD)
    every_slot = gather_rounds(by_row[None], "tp", range(col_bits))
    every_slot = every_slot.transpose(1, 0, 2, 3).reshape(group_count, ROLL, ROWS, HD)
    head_ids = jnp.arange(KVH, dtype=jnp.int32)
    pair_heads = kv_assign[0::2]
    inverse = jnp.sum(
        head_ids[None, :] * (pair_heads[None, :] == head_ids[:, None]).astype(jnp.int32), axis=1
    )
    slot_ids = jnp.arange(QG, dtype=jnp.int32)
    rank_of_slot = 2 * inverse[slot_ids // 2] + slot_ids % 2
    chosen = jax.vmap(lambda per_group: pick(per_group, rank_of_slot))(every_slot)
    out_part = jnp.einsum("gabe,cae->gbc", chosen, o_blocks[0], preferred_element_type=jnp.float32)
    if group_count == 1 and grid_cols == GR and col_width == GR * DS:
        col_bits = grid_cols.bit_length() - 1
        row_bits = GR.bit_length() - 1
        pieces = out_part[0].reshape(ROWS, GR, DS).transpose(1, 0, 2)
        held, _ = scatter_rounds(
            pieces.reshape((2,) * row_bits + (ROWS, DS)),
            list(range(col_bits + row_bits - 1, col_bits - 1, -1)),
            "tp",
            range(col_bits, col_bits + row_bits),
        )
        pairs = [(i * grid_cols + j, j * grid_cols + i) for i in range(GR) for j in range(grid_cols)]
        my_cols = lax.ppermute(held.astype(jnp.bfloat16), "tp", pairs)
    else:
        placed = jnp.zeros((group_count, ROWS, D), jnp.float32)
        placed = lax.dynamic_update_slice_in_dim(placed, out_part, grid_col * col_width, 2)
        out_term = (
            placed.reshape(group_count, ROWS, ROLL, DS).transpose(0, 2, 1, 3).reshape(ranks * ROWS, DS)
        )
        my_cols = scatter_sum_xor(out_term.reshape(ranks, ROWS, DS), "tp")[0]
    return my_cols.astype(jnp.bfloat16)[None]


def solution(mesh):
    return jax.shard_map(
        local,
        mesh=mesh,
        in_specs=(
            P(("groups", "tp"), None, None),
            P(),
            P("tp", None, None, None),
            P("tp", None, None, None),
            P(None, None, "tp"),
            P(),
            P(("groups", "tp"), None, None, None),
            P(("groups", "tp"), None, None, None),
            P(("groups", "tp"), None),
        ),
        out_specs=P(("groups", "tp"), None, None),
        check_vma=False,
    )
```

```python
import jax
import jax.numpy as jnp
from jax import lax
from jax.sharding import PartitionSpec as P

D = 8192
KVH = 8
HD = 128
ROLL = 16
ROWS = 8
GR = 4
QG = 16
DS = 512


def from_partner(value, axis, bit):
    mask = 2**bit
    pairs = [(source, source ^ mask) for source in range(lax.axis_size(axis))]
    return lax.ppermute(value, axis, pairs)


def xor_swap(value, axis, bit):
    return from_partner(value, axis, bit)


def gather_xor(value, axis):
    n = lax.axis_size(axis)
    me = lax.axis_index(axis)
    held = value
    for bit in range(n.bit_length() - 1):
        other = xor_swap(held, axis, bit)
        low = ((me >> bit) & 1) == 0
        held = jnp.where(low, jnp.concatenate([held, other], 0), jnp.concatenate([other, held], 0))
    return held


def scatter_rounds(held, order, axis, bits):
    me = lax.axis_index(axis)
    for bit in bits:
        pos = order.index(bit)
        order = order[:pos] + order[pos + 1 :]
        low = ((me >> bit) & 1) == 0
        first = lax.index_in_dim(held, 0, pos, keepdims=False)
        second = lax.index_in_dim(held, 1, pos, keepdims=False)
        keep = jnp.where(low, first, second)
        give = jnp.where(low, second, first)
        held = keep + xor_swap(give, axis, bit)
    return held, order


def scatter_sum_xor(pieces, axis):
    n = lax.axis_size(axis)
    bits = n.bit_length() - 1
    me = lax.axis_index(axis)
    held = pieces.reshape((2,) * bits + pieces.shape[1:])
    order = list(range(bits - 1, -1, -1))
    for bit in range(bits):
        pos = order.index(bit)
        order.pop(pos)
        low = ((me >> bit) & 1) == 0
        first = lax.index_in_dim(held, 0, pos, keepdims=False)
        second = lax.index_in_dim(held, 1, pos, keepdims=False)
        keep = jnp.where(low, first, second)
        give = jnp.where(low, second, first)
        held = keep + xor_swap(give, axis, bit)
    return held[None]


def pick(table, idx):
    hit = idx[:, None] == jnp.arange(table.shape[0], dtype=idx.dtype)[None, :]
    hit = hit.reshape(hit.shape + (1,) * (table.ndim - 1))
    return jnp.sum(jnp.where(hit, table[None], jnp.zeros((), table.dtype)), axis=1)


def gather_rounds(held, axis, bits):
    me = lax.axis_index(axis)
    for bit in bits:
        other = xor_swap(held, axis, bit)
        low = ((me >> bit) & 1) == 0
        held = jnp.where(low, jnp.concatenate([held, other], 0), jnp.concatenate([other, held], 0))
    return held


def exchange_rounds(held, axis, bits):
    me = lax.axis_index(axis)
    count = len(bits)
    for done, bit in enumerate(bits):
        low = ((me >> bit) & 1) == 0
        first = lax.index_in_dim(held, 0, 0, keepdims=False)
        second = lax.index_in_dim(held, 1, 0, keepdims=False)
        keep = jnp.where(low, first, second)
        give = jnp.where(low, second, first)
        got = xor_swap(give, axis, bit)
        at = count - done - 1 + done
        held = jnp.where(low, jnp.stack([keep, got], at), jnp.stack([got, keep], at))
    return held


def norm_rows(rows_float, norm_gain):
    mean_square = jnp.mean(rows_float * rows_float, axis=-1, keepdims=True)
    return (rows_float * lax.rsqrt(mean_square + 1e-05) * norm_gain[None, :]).astype(jnp.bfloat16)


def local(
    hidden_in, norm_gain, q_blocks, o_blocks, kv_blocks, kv_assign, key_cache, value_cache, lengths
):
    ranks = lax.axis_size("tp")
    my_index = lax.axis_index("tp")
    my_rank = my_index % ROLL
    my_half = my_rank % 2
    grid_cols = ranks // GR
    group_count = ranks // ROLL
    col_width = q_blocks.shape[3]
    key_width = kv_blocks.shape[2]
    grid_row = my_index // grid_cols
    grid_col = my_index % grid_cols
    dest_ids = jnp.arange(ranks, dtype=jnp.int32)
    dest_rank = dest_ids % ROLL
    dest_head = kv_assign[dest_rank]
    dest_group = 2 * dest_head + dest_rank % 2
    dest_copy = dest_ids // ROLL
    every_rows = gather_xor(hidden_in, "tp")
    rows_float = (
        every_rows.reshape(group_count, ROLL, ROWS, DS)
        .transpose(0, 2, 1, 3)
        .reshape(group_count * ROWS, D)
        .astype(jnp.float32)
    )
    normed_every = norm_rows(rows_float, norm_gain)
    col_rows = lax.dynamic_slice_in_dim(normed_every, grid_col * col_width, col_width, 1)
    query_part = jnp.einsum(
        "rc,aec->rae", col_rows, q_blocks[0], preferred_element_type=jnp.float32
    )
    query_part = (
        query_part.reshape(group_count, ROWS, QG, HD)
        .transpose(0, 2, 1, 3)
        .reshape(group_count * QG, ROWS, HD)
    )
    query_pick = pick(query_part, dest_copy * QG + dest_group)
    key_rows = lax.dynamic_slice_in_dim(normed_every, my_index * key_width, key_width, 1)
    keyval_part = jnp.einsum("rc,kfc->rkf", key_rows, kv_blocks, preferred_element_type=jnp.float32)
    keyval_part = (
        keyval_part.reshape(group_count, ROWS, 2, KVH, HD)
        .transpose(0, 3, 1, 2, 4)
        .reshape(group_count * KVH, ROWS, 2 * HD)
    )
    keyval_term = pick(keyval_part, dest_copy * KVH + dest_head)
    bits = ranks.bit_length() - 1
    col_bits = grid_cols.bit_length() - 1
    compact = jnp.concatenate([query_pick, keyval_term], -1)
    held, order = scatter_rounds(
        compact.reshape((2,) * bits + (ROWS, 3 * HD)), list(range(bits - 1, -1, -1)), "tp", range(col_bits)
    )
    slot_here = jnp.arange(GR, dtype=jnp.int32) == grid_row
    query_slots = jnp.where(
        slot_here[:, None], held[..., None, :HD], jnp.zeros((), jnp.float32)
    ).reshape(held.shape[:-1] + (GR * HD,))
    held = jnp.concatenate([query_slots, held[..., HD:]], -1)
    projected, _ = scatter_rounds(held, order, "tp", range(col_bits, bits))
    queries = projected[:, : GR * HD].astype(jnp.bfloat16)
    keyval_new = projected[:, GR * HD :].astype(jnp.bfloat16)
    key_new = keyval_new[:, :HD]
    value_new = keyval_new[:, HD:]
    partner_queries = from_partner(queries, "tp", 0)
    both_queries = jnp.where(
        my_half == 0,
        jnp.concatenate([queries, partner_queries], 1),
        jnp.concatenate([partner_queries, queries], 1),
    )
    both_queries = both_queries.reshape(ROWS, 2 * GR, HD)
    scale = 1.0 / HD**0.5
    scores = (
        jnp.einsum("bhe,bte->bht", both_queries, key_cache[0], preferred_element_type=jnp.float32)
        * scale
    )
    positions = jnp.arange(scores.shape[2], dtype=jnp.int32)
    masked = positions[None, None, :] < lengths[0][:, None, None]
    new_score = (
        jnp.einsum("bhe,be->bh", both_queries, key_new, preferred_element_type=jnp.float32) * scale
    )
    new_score = jnp.where(my_half == 0, new_score, jnp.float32(-1e30))
    top = jnp.maximum(jnp.max(jnp.where(masked, scores, jnp.float32(-1e30)), axis=-1), new_score)
    weights = jnp.where(masked, jnp.exp(scores - top[..., None]), jnp.float32(0.0))
    new_weight = jnp.exp(new_score - top)
    total = jnp.sum(weights, axis=-1) + new_weight
    summed = jnp.einsum(
        "bht,bte->bhe",
        weights.astype(jnp.bfloat16),
        value_cache[0],
        preferred_element_type=jnp.float32,
    )
    new_rounded = lax.optimization_barrier(new_weight.astype(jnp.bfloat16)).astype(jnp.float32)
    summed = summed + new_rounded[..., None] * value_new.astype(jnp.float32)[:, None, :]
    top_split = top.reshape(ROWS, 2, GR)
    total_split = total.reshape(ROWS, 2, GR)
    summed_split = summed.reshape(ROWS, 2, GR, HD)
    first_half = my_half == 0
    own_top = jnp.where(first_half, top_split[:, 0], top_split[:, 1])
    own_total = jnp.where(first_half, total_split[:, 0], total_split[:, 1])
    own_summed = jnp.where(first_half, summed_split[:, 0], summed_split[:, 1])
    give_top = jnp.where(first_half, top_split[:, 1], top_split[:, 0])
    give_total = jnp.where(first_half, total_split[:, 1], total_split[:, 0])
    give_summed = jnp.where(first_half, summed_split[:, 1], summed_split[:, 0])
    give = jnp.concatenate([give_summed, give_top[..., None], give_total[..., None]], -1)
    got = from_partner(give, "tp", 0)
    got_summed, got_top, got_total = got[..., :HD], got[..., HD], got[..., HD + 1]
    joint = jnp.maximum(own_top, got_top)
    factor_own = jnp.exp(own_top - joint)
    factor_got = jnp.exp(got_top - joint)
    numer = own_summed * factor_own[..., None] + got_summed * factor_got[..., None]
    denom = own_total * factor_own + got_total * factor_got
    attention = (numer / denom[..., None]).astype(jnp.bfloat16)
    bits = ranks.bit_length() - 1
    col_bits = grid_cols.bit_length() - 1
    row_bits = GR.bit_length() - 1
    by_row = attention.transpose(1, 0, 2).reshape((2,) * row_bits + (ROWS, HD))
    by_row = exchange_rounds(by_row, "tp", list(range(bits - 1, col_bits - 1, -1)))
    by_row = by_row.reshape(GR, ROWS, HD)
    every_slot = gather_rounds(by_row[None], "tp", range(col_bits))
    every_slot = every_slot.transpose(1, 0, 2, 3).reshape(group_count, ROLL, ROWS, HD)
    head_ids = jnp.arange(KVH, dtype=jnp.int32)
    pair_heads = kv_assign[0::2]
    inverse = jnp.sum(
        head_ids[None, :] * (pair_heads[None, :] == head_ids[:, None]).astype(jnp.int32), axis=1
    )
    slot_ids = jnp.arange(QG, dtype=jnp.int32)
    rank_of_slot = 2 * inverse[slot_ids // 2] + slot_ids % 2
    chosen = jax.vmap(lambda per_group: pick(per_group, rank_of_slot))(every_slot)
    out_part = jnp.einsum("gabe,cae->gbc", chosen, o_blocks[0], preferred_element_type=jnp.float32)
    if group_count == 1 and grid_cols == GR and col_width == GR * DS:
        pieces = out_part[0].reshape(ROWS, GR, DS)
        my_cols = None
        for s in range(GR):
            piece = lax.dynamic_index_in_dim(pieces, grid_row ^ s, 1, keepdims=False)
            pairs = [(i * grid_cols + j, j * grid_cols + (i ^ s)) for i in range(GR) for j in range(grid_cols)]
            got = lax.ppermute(piece, "tp", pairs)
            my_cols = got if my_cols is None else my_cols + got
    else:
        placed = jnp.zeros((group_count, ROWS, D), jnp.float32)
        placed = lax.dynamic_update_slice_in_dim(placed, out_part, grid_col * col_width, 2)
        out_term = (
            placed.reshape(group_count, ROWS, ROLL, DS).transpose(0, 2, 1, 3).reshape(ranks * ROWS, DS)
        )
        my_cols = scatter_sum_xor(out_term.reshape(ranks, ROWS, DS), "tp")[0]
    return my_cols.astype(jnp.bfloat16)[None]


def solution(mesh):
    return jax.shard_map(
        local,
        mesh=mesh,
        in_specs=(
            P(("groups", "tp"), None, None),
            P(),
            P("tp", None, None, None),
            P("tp", None, None, None),
            P(None, None, "tp"),
            P(),
            P(("groups", "tp"), None, None, None),
            P(("groups", "tp"), None, None, None),
            P(("groups", "tp"), None),
        ),
        out_specs=P(("groups", "tp"), None, None),
        check_vma=False,
    )
```

```python
import jax
import jax.numpy as jnp
from jax import lax
from jax.sharding import PartitionSpec as P

D = 8192
KVH = 8
HD = 128
ROLL = 16
ROWS = 8
GR = 4
QG = 16
DS = 512


def from_partner(value, axis, bit):
    mask = 2**bit
    pairs = [(source, source ^ mask) for source in range(lax.axis_size(axis))]
    return lax.ppermute(value, axis, pairs)


def xor_swap(value, axis, bit):
    return from_partner(value, axis, bit)


def gather_xor(value, axis):
    n = lax.axis_size(axis)
    me = lax.axis_index(axis)
    held = value
    for bit in range(n.bit_length() - 1):
        other = xor_swap(held, axis, bit)
        low = ((me >> bit) & 1) == 0
        held = jnp.where(low, jnp.concatenate([held, other], 0), jnp.concatenate([other, held], 0))
    return held


def scatter_rounds(held, order, axis, bits):
    me = lax.axis_index(axis)
    for bit in bits:
        pos = order.index(bit)
        order = order[:pos] + order[pos + 1 :]
        low = ((me >> bit) & 1) == 0
        first = lax.index_in_dim(held, 0, pos, keepdims=False)
        second = lax.index_in_dim(held, 1, pos, keepdims=False)
        keep = jnp.where(low, first, second)
        give = jnp.where(low, second, first)
        held = keep + xor_swap(give, axis, bit)
    return held, order


def scatter_sum_xor(pieces, axis):
    n = lax.axis_size(axis)
    bits = n.bit_length() - 1
    me = lax.axis_index(axis)
    held = pieces.reshape((2,) * bits + pieces.shape[1:])
    order = list(range(bits - 1, -1, -1))
    for bit in range(bits):
        pos = order.index(bit)
        order.pop(pos)
        low = ((me >> bit) & 1) == 0
        first = lax.index_in_dim(held, 0, pos, keepdims=False)
        second = lax.index_in_dim(held, 1, pos, keepdims=False)
        keep = jnp.where(low, first, second)
        give = jnp.where(low, second, first)
        held = keep + xor_swap(give, axis, bit)
    return held[None]


def pick(table, idx):
    hit = idx[:, None] == jnp.arange(table.shape[0], dtype=idx.dtype)[None, :]
    hit = hit.reshape(hit.shape + (1,) * (table.ndim - 1))
    return jnp.sum(jnp.where(hit, table[None], jnp.zeros((), table.dtype)), axis=1)


def gather_rounds(held, axis, bits):
    me = lax.axis_index(axis)
    for bit in bits:
        other = xor_swap(held, axis, bit)
        low = ((me >> bit) & 1) == 0
        held = jnp.where(low, jnp.concatenate([held, other], 0), jnp.concatenate([other, held], 0))
    return held


def exchange_rounds(held, axis, bits):
    me = lax.axis_index(axis)
    count = len(bits)
    for done, bit in enumerate(bits):
        low = ((me >> bit) & 1) == 0
        first = lax.index_in_dim(held, 0, 0, keepdims=False)
        second = lax.index_in_dim(held, 1, 0, keepdims=False)
        keep = jnp.where(low, first, second)
        give = jnp.where(low, second, first)
        got = xor_swap(give, axis, bit)
        at = count - done - 1 + done
        held = jnp.where(low, jnp.stack([keep, got], at), jnp.stack([got, keep], at))
    return held


def swap_rows(value, axis, col_bits, s):
    shift = s << col_bits
    return lax.ppermute(value, axis, [(t, t ^ shift) for t in range(lax.axis_size(axis))])


def norm_rows(rows_float, norm_gain):
    mean_square = jnp.mean(rows_float * rows_float, axis=-1, keepdims=True)
    return (rows_float * lax.rsqrt(mean_square + 1e-05) * norm_gain[None, :]).astype(jnp.bfloat16)


def local(
    hidden_in, norm_gain, q_blocks, o_blocks, kv_blocks, kv_assign, key_cache, value_cache, lengths
):
    ranks = lax.axis_size("tp")
    my_index = lax.axis_index("tp")
    my_rank = my_index % ROLL
    my_half = my_rank % 2
    grid_cols = ranks // GR
    group_count = ranks // ROLL
    col_width = q_blocks.shape[3]
    key_width = kv_blocks.shape[2]
    grid_row = my_index // grid_cols
    grid_col = my_index % grid_cols
    dest_ids = jnp.arange(ranks, dtype=jnp.int32)
    dest_rank = dest_ids % ROLL
    dest_head = kv_assign[dest_rank]
    dest_group = 2 * dest_head + dest_rank % 2
    dest_copy = dest_ids // ROLL
    bits = ranks.bit_length() - 1
    col_bits = grid_cols.bit_length() - 1
    row_bits = GR.bit_length() - 1
    row_order = jnp.arange(GR, dtype=jnp.int32) ^ grid_row
    in_row = gather_rounds(hidden_in, "tp", range(col_bits))
    from_rows = [in_row] + [swap_rows(in_row, "tp", col_bits, s) for s in range(1, GR)]
    every_rows = pick(jnp.stack(from_rows), row_order).reshape(ranks, ROWS, DS)
    rows_float = (
        every_rows.reshape(group_count, ROLL, ROWS, DS)
        .transpose(0, 2, 1, 3)
        .reshape(group_count * ROWS, D)
        .astype(jnp.float32)
    )
    normed_every = norm_rows(rows_float, norm_gain)
    col_rows = lax.dynamic_slice_in_dim(normed_every, grid_col * col_width, col_width, 1)
    query_part = jnp.einsum(
        "rc,aec->rae", col_rows, q_blocks[0], preferred_element_type=jnp.float32
    )
    query_part = (
        query_part.reshape(group_count, ROWS, QG, HD)
        .transpose(0, 2, 1, 3)
        .reshape(group_count * QG, ROWS, HD)
    )
    query_pick = pick(query_part, dest_copy * QG + dest_group)
    key_rows = lax.dynamic_slice_in_dim(normed_every, my_index * key_width, key_width, 1)
    keyval_part = jnp.einsum("rc,kfc->rkf", key_rows, kv_blocks, preferred_element_type=jnp.float32)
    keyval_part = (
        keyval_part.reshape(group_count, ROWS, 2, KVH, HD)
        .transpose(0, 3, 1, 2, 4)
        .reshape(group_count * KVH, ROWS, 2 * HD)
    )
    keyval_term = pick(keyval_part, dest_copy * KVH + dest_head)
    compact = jnp.concatenate([query_pick, keyval_term], -1)
    held, _ = scatter_rounds(
        compact.reshape((2,) * bits + (ROWS, 3 * HD)), list(range(bits - 1, -1, -1)), "tp", range(col_bits)
    )
    held = held.reshape(GR, ROWS, 3 * HD)
    from_rows = [lax.dynamic_index_in_dim(held, grid_row, 0, keepdims=False)]
    for s in range(1, GR):
        piece = lax.dynamic_index_in_dim(held, grid_row ^ s, 0, keepdims=False)
        from_rows.append(swap_rows(piece, "tp", col_bits, s))
    query_slots = pick(jnp.stack([got[:, :HD] for got in from_rows]), row_order)
    query_slots = query_slots.transpose(1, 0, 2).reshape(ROWS, GR * HD)
    keyval_sum = from_rows[0][:, HD:]
    for got in from_rows[1:]:
        keyval_sum = keyval_sum + got[:, HD:]
    projected = jnp.concatenate([query_slots, keyval_sum], -1)
    queries = projected[:, : GR * HD].astype(jnp.bfloat16)
    keyval_new = projected[:, GR * HD :].astype(jnp.bfloat16)
    key_new = keyval_new[:, :HD]
    value_new = keyval_new[:, HD:]
    partner_queries = from_partner(queries, "tp", 0)
    both_queries = jnp.where(
        my_half == 0,
        jnp.concatenate([queries, partner_queries], 1),
        jnp.concatenate([partner_queries, queries], 1),
    )
    both_queries = both_queries.reshape(ROWS, 2 * GR, HD)
    scale = 1.0 / HD**0.5
    scores = (
        jnp.einsum("bhe,bte->bht", both_queries, key_cache[0], preferred_element_type=jnp.float32)
        * scale
    )
    positions = jnp.arange(scores.shape[2], dtype=jnp.int32)
    masked = positions[None, None, :] < lengths[0][:, None, None]
    new_score = (
        jnp.einsum("bhe,be->bh", both_queries, key_new, preferred_element_type=jnp.float32) * scale
    )
    new_score = jnp.where(my_half == 0, new_score, jnp.float32(-1e30))
    top = jnp.maximum(jnp.max(jnp.where(masked, scores, jnp.float32(-1e30)), axis=-1), new_score)
    weights = jnp.where(masked, jnp.exp(scores - top[..., None]), jnp.float32(0.0))
    new_weight = jnp.exp(new_score - top)
    total = jnp.sum(weights, axis=-1) + new_weight
    summed = jnp.einsum(
        "bht,bte->bhe",
        weights.astype(jnp.bfloat16),
        value_cache[0],
        preferred_element_type=jnp.float32,
    )
    new_rounded = lax.optimization_barrier(new_weight.astype(jnp.bfloat16)).astype(jnp.float32)
    summed = summed + new_rounded[..., None] * value_new.astype(jnp.float32)[:, None, :]
    top_split = top.reshape(ROWS, 2, GR)
    total_split = total.reshape(ROWS, 2, GR)
    summed_split = summed.reshape(ROWS, 2, GR, HD)
    first_half = my_half == 0
    own_top = jnp.where(first_half, top_split[:, 0], top_split[:, 1])
    own_total = jnp.where(first_half, total_split[:, 0], total_split[:, 1])
    own_summed = jnp.where(first_half, summed_split[:, 0], summed_split[:, 1])
    give_top = jnp.where(first_half, top_split[:, 1], top_split[:, 0])
    give_total = jnp.where(first_half, total_split[:, 1], total_split[:, 0])
    give_summed = jnp.where(first_half, summed_split[:, 1], summed_split[:, 0])
    give = jnp.concatenate([give_summed, give_top[..., None], give_total[..., None]], -1)
    got = from_partner(give, "tp", 0)
    got_summed, got_top, got_total = got[..., :HD], got[..., HD], got[..., HD + 1]
    joint = jnp.maximum(own_top, got_top)
    factor_own = jnp.exp(own_top - joint)
    factor_got = jnp.exp(got_top - joint)
    numer = own_summed * factor_own[..., None] + got_summed * factor_got[..., None]
    denom = own_total * factor_own + got_total * factor_got
    attention = (numer / denom[..., None]).astype(jnp.bfloat16)
    from_rows = [lax.dynamic_index_in_dim(attention, grid_row, 1, keepdims=False)]
    for s in range(1, GR):
        piece = lax.dynamic_index_in_dim(attention, grid_row ^ s, 1, keepdims=False)
        from_rows.append(swap_rows(piece, "tp", col_bits, s))
    by_row = pick(jnp.stack(from_rows), row_order)
    every_slot = gather_rounds(by_row[None], "tp", range(col_bits))
    every_slot = every_slot.transpose(1, 0, 2, 3).reshape(group_count, ROLL, ROWS, HD)
    head_ids = jnp.arange(KVH, dtype=jnp.int32)
    pair_heads = kv_assign[0::2]
    inverse = jnp.sum(
        head_ids[None, :] * (pair_heads[None, :] == head_ids[:, None]).astype(jnp.int32), axis=1
    )
    slot_ids = jnp.arange(QG, dtype=jnp.int32)
    rank_of_slot = 2 * inverse[slot_ids // 2] + slot_ids % 2
    chosen = jax.vmap(lambda per_group: pick(per_group, rank_of_slot))(every_slot)
    out_part = jnp.einsum("gabe,cae->gbc", chosen, o_blocks[0], preferred_element_type=jnp.float32)
    if group_count == 1 and grid_cols == GR and col_width == GR * DS:
        pieces = out_part[0].reshape(ROWS, GR, DS)
        my_cols = None
        for s in range(GR):
            piece = lax.dynamic_index_in_dim(pieces, grid_row ^ s, 1, keepdims=False)
            pairs = [(i * grid_cols + j, j * grid_cols + (i ^ s)) for i in range(GR) for j in range(grid_cols)]
            got = lax.ppermute(piece, "tp", pairs)
            my_cols = got if my_cols is None else my_cols + got
    else:
        placed = jnp.zeros((group_count, ROWS, D), jnp.float32)
        placed = lax.dynamic_update_slice_in_dim(placed, out_part, grid_col * col_width, 2)
        out_term = (
            placed.reshape(group_count, ROWS, ROLL, DS).transpose(0, 2, 1, 3).reshape(ranks * ROWS, DS)
        )
        my_cols = scatter_sum_xor(out_term.reshape(ranks, ROWS, DS), "tp")[0]
    return my_cols.astype(jnp.bfloat16)[None]


def solution(mesh):
    return jax.shard_map(
        local,
        mesh=mesh,
        in_specs=(
            P(("groups", "tp"), None, None),
            P(),
            P("tp", None, None, None),
            P("tp", None, None, None),
            P(None, None, "tp"),
            P(),
            P(("groups", "tp"), None, None, None),
            P(("groups", "tp"), None, None, None),
            P(("groups", "tp"), None),
        ),
        out_specs=P(("groups", "tp"), None, None),
        check_vma=False,
    )
```

```python
import jax
import jax.numpy as jnp
from jax import lax
from jax.sharding import PartitionSpec as P

D = 8192
KVH = 8
HD = 128
ROLL = 16
ROWS = 8
GR = 4
QG = 16
DS = 512


def from_partner(value, axis, bit):
    mask = 2**bit
    pairs = [(source, source ^ mask) for source in range(lax.axis_size(axis))]
    return lax.ppermute(value, axis, pairs)


def xor_swap(value, axis, bit):
    return from_partner(value, axis, bit)


def gather_xor(value, axis):
    n = lax.axis_size(axis)
    me = lax.axis_index(axis)
    held = value
    for bit in range(n.bit_length() - 1):
        other = xor_swap(held, axis, bit)
        low = ((me >> bit) & 1) == 0
        held = jnp.where(low, jnp.concatenate([held, other], 0), jnp.concatenate([other, held], 0))
    return held


def scatter_rounds(held, order, axis, bits):
    me = lax.axis_index(axis)
    for bit in bits:
        pos = order.index(bit)
        order = order[:pos] + order[pos + 1 :]
        low = ((me >> bit) & 1) == 0
        first = lax.index_in_dim(held, 0, pos, keepdims=False)
        second = lax.index_in_dim(held, 1, pos, keepdims=False)
        keep = jnp.where(low, first, second)
        give = jnp.where(low, second, first)
        held = keep + xor_swap(give, axis, bit)
    return held, order


def scatter_sum_xor(pieces, axis):
    n = lax.axis_size(axis)
    bits = n.bit_length() - 1
    me = lax.axis_index(axis)
    held = pieces.reshape((2,) * bits + pieces.shape[1:])
    order = list(range(bits - 1, -1, -1))
    for bit in range(bits):
        pos = order.index(bit)
        order.pop(pos)
        low = ((me >> bit) & 1) == 0
        first = lax.index_in_dim(held, 0, pos, keepdims=False)
        second = lax.index_in_dim(held, 1, pos, keepdims=False)
        keep = jnp.where(low, first, second)
        give = jnp.where(low, second, first)
        held = keep + xor_swap(give, axis, bit)
    return held[None]


def pick(table, idx):
    hit = idx[:, None] == jnp.arange(table.shape[0], dtype=idx.dtype)[None, :]
    hit = hit.reshape(hit.shape + (1,) * (table.ndim - 1))
    return jnp.sum(jnp.where(hit, table[None], jnp.zeros((), table.dtype)), axis=1)


def gather_rounds(held, axis, bits):
    me = lax.axis_index(axis)
    for bit in bits:
        other = xor_swap(held, axis, bit)
        low = ((me >> bit) & 1) == 0
        held = jnp.where(low, jnp.concatenate([held, other], 0), jnp.concatenate([other, held], 0))
    return held


def exchange_rounds(held, axis, bits):
    me = lax.axis_index(axis)
    count = len(bits)
    for done, bit in enumerate(bits):
        low = ((me >> bit) & 1) == 0
        first = lax.index_in_dim(held, 0, 0, keepdims=False)
        second = lax.index_in_dim(held, 1, 0, keepdims=False)
        keep = jnp.where(low, first, second)
        give = jnp.where(low, second, first)
        got = xor_swap(give, axis, bit)
        at = count - done - 1 + done
        held = jnp.where(low, jnp.stack([keep, got], at), jnp.stack([got, keep], at))
    return held


def swap_rows(value, axis, col_bits, s):
    shift = s << col_bits
    return lax.ppermute(value, axis, [(t, t ^ shift) for t in range(lax.axis_size(axis))])


def swap_cols(value, axis, s):
    return lax.ppermute(value, axis, [(t, t ^ s) for t in range(lax.axis_size(axis))])


def norm_rows(rows_float, norm_gain):
    mean_square = jnp.mean(rows_float * rows_float, axis=-1, keepdims=True)
    return (rows_float * lax.rsqrt(mean_square + 1e-05) * norm_gain[None, :]).astype(jnp.bfloat16)


def local(
    hidden_in, norm_gain, q_blocks, o_blocks, kv_blocks, kv_assign, key_cache, value_cache, lengths
):
    ranks = lax.axis_size("tp")
    my_index = lax.axis_index("tp")
    my_rank = my_index % ROLL
    my_half = my_rank % 2
    grid_cols = ranks // GR
    group_count = ranks // ROLL
    col_width = q_blocks.shape[3]
    key_width = kv_blocks.shape[2]
    grid_row = my_index // grid_cols
    grid_col = my_index % grid_cols
    dest_ids = jnp.arange(ranks, dtype=jnp.int32)
    dest_rank = dest_ids % ROLL
    dest_head = kv_assign[dest_rank]
    dest_group = 2 * dest_head + dest_rank % 2
    dest_copy = dest_ids // ROLL
    bits = ranks.bit_length() - 1
    col_bits = grid_cols.bit_length() - 1
    row_bits = GR.bit_length() - 1
    row_order = jnp.arange(GR, dtype=jnp.int32) ^ grid_row
    col_order = jnp.arange(grid_cols, dtype=jnp.int32) ^ grid_col
    direct_cols = grid_cols <= 4
    if direct_cols:
        from_cols = [hidden_in[0]] + [swap_cols(hidden_in[0], "tp", s) for s in range(1, grid_cols)]
        in_row = pick(jnp.stack(from_cols), col_order)
    else:
        in_row = gather_rounds(hidden_in, "tp", range(col_bits))
    from_rows = [in_row] + [swap_rows(in_row, "tp", col_bits, s) for s in range(1, GR)]
    every_rows = pick(jnp.stack(from_rows), row_order).reshape(ranks, ROWS, DS)
    rows_float = (
        every_rows.reshape(group_count, ROLL, ROWS, DS)
        .transpose(0, 2, 1, 3)
        .reshape(group_count * ROWS, D)
        .astype(jnp.float32)
    )
    normed_every = norm_rows(rows_float, norm_gain)
    col_rows = lax.dynamic_slice_in_dim(normed_every, grid_col * col_width, col_width, 1)
    query_part = jnp.einsum(
        "rc,aec->rae", col_rows, q_blocks[0], preferred_element_type=jnp.float32
    )
    query_part = (
        query_part.reshape(group_count, ROWS, QG, HD)
        .transpose(0, 2, 1, 3)
        .reshape(group_count * QG, ROWS, HD)
    )
    pair_first = dest_copy * QG + 2 * dest_head
    query_pick = jnp.concatenate([pick(query_part, pair_first), pick(query_part, pair_first + 1)], -1)
    key_rows = lax.dynamic_slice_in_dim(normed_every, my_index * key_width, key_width, 1)
    keyval_part = jnp.einsum("rc,kfc->rkf", key_rows, kv_blocks, preferred_element_type=jnp.float32)
    keyval_part = (
        keyval_part.reshape(group_count, ROWS, 2, KVH, HD)
        .transpose(0, 3, 1, 2, 4)
        .reshape(group_count * KVH, ROWS, 2 * HD)
    )
    keyval_term = pick(keyval_part, dest_copy * KVH + dest_head)
    width = 4 * HD
    compact = jnp.concatenate([query_pick, keyval_term], -1)
    if direct_cols:
        by_col = compact.reshape(GR, grid_cols, ROWS, width)
        held = lax.dynamic_index_in_dim(by_col, grid_col, 1, keepdims=False)
        for s in range(1, grid_cols):
            held = held + swap_cols(lax.dynamic_index_in_dim(by_col, grid_col ^ s, 1, keepdims=False), "tp", s)
    else:
        held, _ = scatter_rounds(
            compact.reshape((2,) * bits + (ROWS, width)), list(range(bits - 1, -1, -1)), "tp", range(col_bits)
        )
        held = held.reshape(GR, ROWS, width)
    from_rows = [lax.dynamic_index_in_dim(held, grid_row, 0, keepdims=False)]
    for s in range(1, GR):
        piece = lax.dynamic_index_in_dim(held, grid_row ^ s, 0, keepdims=False)
        from_rows.append(swap_rows(piece, "tp", col_bits, s))
    halves_q = [
        pick(jnp.stack([got[:, h * HD : (h + 1) * HD] for got in from_rows]), row_order) for h in range(2)
    ]
    both_queries = jnp.stack(halves_q).transpose(2, 0, 1, 3).reshape(ROWS, 2 * GR, HD).astype(jnp.bfloat16)
    keyval_sum = from_rows[0][:, 2 * HD :]
    for got in from_rows[1:]:
        keyval_sum = keyval_sum + got[:, 2 * HD :]
    keyval_new = keyval_sum.astype(jnp.bfloat16)
    key_new = keyval_new[:, :HD]
    value_new = keyval_new[:, HD:]
    scale = 1.0 / HD**0.5
    scores = (
        jnp.einsum("bhe,bte->bht", both_queries, key_cache[0], preferred_element_type=jnp.float32)
        * scale
    )
    positions = jnp.arange(scores.shape[2], dtype=jnp.int32)
    masked = positions[None, None, :] < lengths[0][:, None, None]
    new_score = (
        jnp.einsum("bhe,be->bh", both_queries, key_new, preferred_element_type=jnp.float32) * scale
    )
    new_score = jnp.where(my_half == 0, new_score, jnp.float32(-1e30))
    top = jnp.maximum(jnp.max(jnp.where(masked, scores, jnp.float32(-1e30)), axis=-1), new_score)
    weights = jnp.where(masked, jnp.exp(scores - top[..., None]), jnp.float32(0.0))
    new_weight = jnp.exp(new_score - top)
    total = jnp.sum(weights, axis=-1) + new_weight
    summed = jnp.einsum(
        "bht,bte->bhe",
        weights.astype(jnp.bfloat16),
        value_cache[0],
        preferred_element_type=jnp.float32,
    )
    new_rounded = lax.optimization_barrier(new_weight.astype(jnp.bfloat16)).astype(jnp.float32)
    summed = summed + new_rounded[..., None] * value_new.astype(jnp.float32)[:, None, :]
    top_split = top.reshape(ROWS, 2, GR)
    total_split = total.reshape(ROWS, 2, GR)
    summed_split = summed.reshape(ROWS, 2, GR, HD)
    first_half = my_half == 0
    own_top = jnp.where(first_half, top_split[:, 0], top_split[:, 1])
    own_total = jnp.where(first_half, total_split[:, 0], total_split[:, 1])
    own_summed = jnp.where(first_half, summed_split[:, 0], summed_split[:, 1])
    give_top = jnp.where(first_half, top_split[:, 1], top_split[:, 0])
    give_total = jnp.where(first_half, total_split[:, 1], total_split[:, 0])
    give_summed = jnp.where(first_half, summed_split[:, 1], summed_split[:, 0])
    give = jnp.concatenate([give_summed, give_top[..., None], give_total[..., None]], -1)
    got = from_partner(give, "tp", 0)
    got_summed, got_top, got_total = got[..., :HD], got[..., HD], got[..., HD + 1]
    joint = jnp.maximum(own_top, got_top)
    factor_own = jnp.exp(own_top - joint)
    factor_got = jnp.exp(got_top - joint)
    numer = own_summed * factor_own[..., None] + got_summed * factor_got[..., None]
    denom = own_total * factor_own + got_total * factor_got
    attention = (numer / denom[..., None]).astype(jnp.bfloat16)
    from_rows = [lax.dynamic_index_in_dim(attention, grid_row, 1, keepdims=False)]
    for s in range(1, GR):
        piece = lax.dynamic_index_in_dim(attention, grid_row ^ s, 1, keepdims=False)
        from_rows.append(swap_rows(piece, "tp", col_bits, s))
    by_row = pick(jnp.stack(from_rows), row_order)
    if direct_cols:
        from_cols = [by_row] + [swap_cols(by_row, "tp", s) for s in range(1, grid_cols)]
        every_slot = pick(jnp.stack(from_cols), col_order)
    else:
        every_slot = gather_rounds(by_row[None], "tp", range(col_bits))
    every_slot = every_slot.transpose(1, 0, 2, 3).reshape(group_count, ROLL, ROWS, HD)
    head_ids = jnp.arange(KVH, dtype=jnp.int32)
    pair_heads = kv_assign[0::2]
    inverse = jnp.sum(
        head_ids[None, :] * (pair_heads[None, :] == head_ids[:, None]).astype(jnp.int32), axis=1
    )
    slot_ids = jnp.arange(QG, dtype=jnp.int32)
    rank_of_slot = 2 * inverse[slot_ids // 2] + slot_ids % 2
    chosen = jax.vmap(lambda per_group: pick(per_group, rank_of_slot))(every_slot)
    out_part = jnp.einsum("gabe,cae->gbc", chosen, o_blocks[0], preferred_element_type=jnp.float32)
    if group_count == 1 and grid_cols == GR and col_width == GR * DS:
        pieces = out_part[0].reshape(ROWS, GR, DS)
        my_cols = None
        for s in range(GR):
            piece = lax.dynamic_index_in_dim(pieces, grid_row ^ s, 1, keepdims=False)
            pairs = [(i * grid_cols + j, j * grid_cols + (i ^ s)) for i in range(GR) for j in range(grid_cols)]
            got = lax.ppermute(piece, "tp", pairs)
            my_cols = got if my_cols is None else my_cols + got
    else:
        placed = jnp.zeros((group_count, ROWS, D), jnp.float32)
        placed = lax.dynamic_update_slice_in_dim(placed, out_part, grid_col * col_width, 2)
        out_term = (
            placed.reshape(group_count, ROWS, ROLL, DS).transpose(0, 2, 1, 3).reshape(ranks * ROWS, DS)
        )
        my_cols = scatter_sum_xor(out_term.reshape(ranks, ROWS, DS), "tp")[0]
    return my_cols.astype(jnp.bfloat16)[None]


def solution(mesh):
    return jax.shard_map(
        local,
        mesh=mesh,
        in_specs=(
            P(("groups", "tp"), None, None),
            P(),
            P("tp", None, None, None),
            P("tp", None, None, None),
            P(None, None, "tp"),
            P(),
            P(("groups", "tp"), None, None, None),
            P(("groups", "tp"), None, None, None),
            P(("groups", "tp"), None),
        ),
        out_specs=P(("groups", "tp"), None, None),
        check_vma=False,
    )
```

```python
import jax
import jax.numpy as jnp
from jax import lax
from jax.sharding import PartitionSpec as P

D = 8192
KVH = 8
HD = 128
ROLL = 16
ROWS = 8
GR = 4
QG = 16
DS = 512


def from_partner(value, axis, bit):
    mask = 2**bit
    pairs = [(source, source ^ mask) for source in range(lax.axis_size(axis))]
    return lax.ppermute(value, axis, pairs)


def xor_swap(value, axis, bit):
    return from_partner(value, axis, bit)


def gather_xor(value, axis):
    n = lax.axis_size(axis)
    me = lax.axis_index(axis)
    held = value
    for bit in range(n.bit_length() - 1):
        other = xor_swap(held, axis, bit)
        low = ((me >> bit) & 1) == 0
        held = jnp.where(low, jnp.concatenate([held, other], 0), jnp.concatenate([other, held], 0))
    return held


def scatter_rounds(held, order, axis, bits):
    me = lax.axis_index(axis)
    for bit in bits:
        pos = order.index(bit)
        order = order[:pos] + order[pos + 1 :]
        low = ((me >> bit) & 1) == 0
        first = lax.index_in_dim(held, 0, pos, keepdims=False)
        second = lax.index_in_dim(held, 1, pos, keepdims=False)
        keep = jnp.where(low, first, second)
        give = jnp.where(low, second, first)
        held = keep + xor_swap(give, axis, bit)
    return held, order


def scatter_sum_xor(pieces, axis):
    n = lax.axis_size(axis)
    bits = n.bit_length() - 1
    me = lax.axis_index(axis)
    held = pieces.reshape((2,) * bits + pieces.shape[1:])
    order = list(range(bits - 1, -1, -1))
    for bit in range(bits):
        pos = order.index(bit)
        order.pop(pos)
        low = ((me >> bit) & 1) == 0
        first = lax.index_in_dim(held, 0, pos, keepdims=False)
        second = lax.index_in_dim(held, 1, pos, keepdims=False)
        keep = jnp.where(low, first, second)
        give = jnp.where(low, second, first)
        held = keep + xor_swap(give, axis, bit)
    return held[None]


def pick(table, idx):
    hit = idx[:, None] == jnp.arange(table.shape[0], dtype=idx.dtype)[None, :]
    hit = hit.reshape(hit.shape + (1,) * (table.ndim - 1))
    return jnp.sum(jnp.where(hit, table[None], jnp.zeros((), table.dtype)), axis=1)


def gather_rounds(held, axis, bits):
    me = lax.axis_index(axis)
    for bit in bits:
        other = xor_swap(held, axis, bit)
        low = ((me >> bit) & 1) == 0
        held = jnp.where(low, jnp.concatenate([held, other], 0), jnp.concatenate([other, held], 0))
    return held


def exchange_rounds(held, axis, bits):
    me = lax.axis_index(axis)
    count = len(bits)
    for done, bit in enumerate(bits):
        low = ((me >> bit) & 1) == 0
        first = lax.index_in_dim(held, 0, 0, keepdims=False)
        second = lax.index_in_dim(held, 1, 0, keepdims=False)
        keep = jnp.where(low, first, second)
        give = jnp.where(low, second, first)
        got = xor_swap(give, axis, bit)
        at = count - done - 1 + done
        held = jnp.where(low, jnp.stack([keep, got], at), jnp.stack([got, keep], at))
    return held


def swap_rows(value, axis, col_bits, s):
    shift = s << col_bits
    return lax.ppermute(value, axis, [(t, t ^ shift) for t in range(lax.axis_size(axis))])


def swap_cols(value, axis, s):
    return lax.ppermute(value, axis, [(t, t ^ s) for t in range(lax.axis_size(axis))])


def norm_rows(rows_float, norm_gain):
    mean_square = jnp.mean(rows_float * rows_float, axis=-1, keepdims=True)
    return (rows_float * lax.rsqrt(mean_square + 1e-05) * norm_gain[None, :]).astype(jnp.bfloat16)


def local(
    hidden_in, norm_gain, q_blocks, o_blocks, kv_blocks, kv_assign, key_cache, value_cache, lengths
):
    ranks = lax.axis_size("tp")
    my_index = lax.axis_index("tp")
    my_rank = my_index % ROLL
    my_half = my_rank % 2
    grid_cols = ranks // GR
    group_count = ranks // ROLL
    col_width = q_blocks.shape[3]
    key_width = kv_blocks.shape[2]
    grid_row = my_index // grid_cols
    grid_col = my_index % grid_cols
    dest_ids = jnp.arange(ranks, dtype=jnp.int32)
    dest_rank = dest_ids % ROLL
    dest_head = kv_assign[dest_rank]
    dest_group = 2 * dest_head + dest_rank % 2
    dest_copy = dest_ids // ROLL
    bits = ranks.bit_length() - 1
    col_bits = grid_cols.bit_length() - 1
    row_bits = GR.bit_length() - 1
    row_order = jnp.arange(GR, dtype=jnp.int32) ^ grid_row
    col_order = jnp.arange(grid_cols, dtype=jnp.int32) ^ grid_col
    direct_cols = grid_cols <= 4
    if direct_cols:
        from_cols = [hidden_in[0]] + [swap_cols(hidden_in[0], "tp", s) for s in range(1, grid_cols)]
        in_row = pick(jnp.stack(from_cols), col_order)
    else:
        in_row = gather_rounds(hidden_in, "tp", range(col_bits))
    from_rows = [in_row] + [swap_rows(in_row, "tp", col_bits, s) for s in range(1, GR)]
    every_rows = pick(jnp.stack(from_rows), row_order).reshape(ranks, ROWS, DS)
    rows_float = (
        every_rows.reshape(group_count, ROLL, ROWS, DS)
        .transpose(0, 2, 1, 3)
        .reshape(group_count * ROWS, D)
        .astype(jnp.float32)
    )
    normed_every = norm_rows(rows_float, norm_gain)
    col_rows = lax.dynamic_slice_in_dim(normed_every, grid_col * col_width, col_width, 1)
    query_part = jnp.einsum(
        "rc,aec->rae", col_rows, q_blocks[0], preferred_element_type=jnp.float32
    )
    query_part = (
        query_part.reshape(group_count, ROWS, QG, HD)
        .transpose(0, 2, 1, 3)
        .reshape(group_count * QG, ROWS, HD)
    )
    pair_first = dest_copy * QG + 2 * dest_head
    query_pick = jnp.concatenate([pick(query_part, pair_first), pick(query_part, pair_first + 1)], -1)
    key_rows = lax.dynamic_slice_in_dim(normed_every, my_index * key_width, key_width, 1)
    keyval_part = jnp.einsum("rc,kfc->rkf", key_rows, kv_blocks, preferred_element_type=jnp.float32)
    keyval_part = (
        keyval_part.reshape(group_count, ROWS, 2, KVH, HD)
        .transpose(0, 3, 1, 2, 4)
        .reshape(group_count * KVH, ROWS, 2 * HD)
    )
    keyval_term = pick(keyval_part, dest_copy * KVH + dest_head)
    width = 4 * HD
    compact = jnp.concatenate([query_pick, keyval_term], -1)
    if direct_cols:
        by_col = compact.reshape(GR, grid_cols, ROWS, width)
        held = lax.dynamic_index_in_dim(by_col, grid_col, 1, keepdims=False)
        for s in range(1, grid_cols):
            held = held + swap_cols(lax.dynamic_index_in_dim(by_col, grid_col ^ s, 1, keepdims=False), "tp", s)
    else:
        held, _ = scatter_rounds(
            compact.reshape((2,) * bits + (ROWS, width)), list(range(bits - 1, -1, -1)), "tp", range(col_bits)
        )
        held = held.reshape(GR, ROWS, width)
    from_rows = [lax.dynamic_index_in_dim(held, grid_row, 0, keepdims=False)]
    for s in range(1, GR):
        piece = lax.dynamic_index_in_dim(held, grid_row ^ s, 0, keepdims=False)
        from_rows.append(swap_rows(piece, "tp", col_bits, s))
    halves_q = [
        pick(jnp.stack([got[:, h * HD : (h + 1) * HD] for got in from_rows]), row_order) for h in range(2)
    ]
    both_queries = jnp.stack(halves_q).transpose(2, 0, 1, 3).reshape(ROWS, 2 * GR, HD).astype(jnp.bfloat16)
    keyval_sum = from_rows[0][:, 2 * HD :]
    for got in from_rows[1:]:
        keyval_sum = keyval_sum + got[:, 2 * HD :]
    keyval_new = keyval_sum.astype(jnp.bfloat16)
    key_new = keyval_new[:, :HD]
    value_new = keyval_new[:, HD:]
    scale = 1.0 / HD**0.5
    scores = (
        jnp.einsum("bhe,bte->bht", both_queries, key_cache[0], preferred_element_type=jnp.float32)
        * scale
    )
    positions = jnp.arange(scores.shape[2], dtype=jnp.int32)
    masked = positions[None, None, :] < lengths[0][:, None, None]
    new_score = (
        jnp.einsum("bhe,be->bh", both_queries, key_new, preferred_element_type=jnp.float32) * scale
    )
    new_score = jnp.where(my_half == 0, new_score, jnp.float32(-1e30))
    top = jnp.maximum(jnp.max(jnp.where(masked, scores, jnp.float32(-1e30)), axis=-1), new_score)
    weights = jnp.where(masked, jnp.exp(scores - top[..., None]), jnp.float32(0.0))
    new_weight = jnp.exp(new_score - top)
    total = jnp.sum(weights, axis=-1) + new_weight
    summed = jnp.einsum(
        "bht,bte->bhe",
        weights.astype(jnp.bfloat16),
        value_cache[0],
        preferred_element_type=jnp.float32,
    )
    new_rounded = lax.optimization_barrier(new_weight.astype(jnp.bfloat16)).astype(jnp.float32)
    summed = summed + new_rounded[..., None] * value_new.astype(jnp.float32)[:, None, :]
    parts = jnp.concatenate([summed, top[..., None], total[..., None]], -1)
    parts = parts.reshape(ROWS, 2, GR, HD + 2).transpose(2, 0, 1, 3)
    from_rows = [lax.dynamic_index_in_dim(parts, grid_row, 0, keepdims=False)]
    for s in range(1, GR):
        piece = lax.dynamic_index_in_dim(parts, grid_row ^ s, 0, keepdims=False)
        from_rows.append(swap_rows(piece, "tp", col_bits, s))
    mine = pick(jnp.stack(from_rows), row_order)
    theirs = swap_cols(mine, "tp", 1)
    even_col = grid_col % 2 == 0
    first = jnp.where(even_col, mine, theirs)
    second = jnp.where(even_col, theirs, mine)
    joint = jnp.maximum(first[..., HD], second[..., HD])
    factor_first = jnp.exp(first[..., HD] - joint)
    factor_second = jnp.exp(second[..., HD] - joint)
    numer = first[..., :HD] * factor_first[..., None] + second[..., :HD] * factor_second[..., None]
    denom = first[..., HD + 1] * factor_first + second[..., HD + 1] * factor_second
    pair_attn = (numer / denom[..., None]).astype(jnp.bfloat16)
    if grid_cols == 4:
        every_pair = jnp.stack([pair_attn, swap_cols(pair_attn, "tp", 2)])
        every_pair = jnp.where(grid_col // 2 == 0, every_pair, every_pair[::-1])
    else:
        every_pair = gather_rounds(pair_attn[None], "tp", range(1, col_bits))
    every_slot = every_pair.transpose(1, 0, 3, 2, 4).reshape(group_count, ROLL, ROWS, HD)
    head_ids = jnp.arange(KVH, dtype=jnp.int32)
    pair_heads = kv_assign[0::2]
    inverse = jnp.sum(
        head_ids[None, :] * (pair_heads[None, :] == head_ids[:, None]).astype(jnp.int32), axis=1
    )
    slot_ids = jnp.arange(QG, dtype=jnp.int32)
    rank_of_slot = 2 * inverse[slot_ids // 2] + slot_ids % 2
    chosen = jax.vmap(lambda per_group: pick(per_group, rank_of_slot))(every_slot)
    out_part = jnp.einsum("gabe,cae->gbc", chosen, o_blocks[0], preferred_element_type=jnp.float32)
    if group_count == 1 and grid_cols == GR and col_width == GR * DS:
        pieces = out_part[0].reshape(ROWS, GR, DS)
        my_cols = None
        for s in range(GR):
            piece = lax.dynamic_index_in_dim(pieces, grid_row ^ s, 1, keepdims=False)
            pairs = [(i * grid_cols + j, j * grid_cols + (i ^ s)) for i in range(GR) for j in range(grid_cols)]
            got = lax.ppermute(piece, "tp", pairs)
            my_cols = got if my_cols is None else my_cols + got
    else:
        placed = jnp.zeros((group_count, ROWS, D), jnp.float32)
        placed = lax.dynamic_update_slice_in_dim(placed, out_part, grid_col * col_width, 2)
        out_term = (
            placed.reshape(group_count, ROWS, ROLL, DS).transpose(0, 2, 1, 3).reshape(ranks * ROWS, DS)
        )
        my_cols = scatter_sum_xor(out_term.reshape(ranks, ROWS, DS), "tp")[0]
    return my_cols.astype(jnp.bfloat16)[None]


def solution(mesh):
    return jax.shard_map(
        local,
        mesh=mesh,
        in_specs=(
            P(("groups", "tp"), None, None),
            P(),
            P("tp", None, None, None),
            P("tp", None, None, None),
            P(None, None, "tp"),
            P(),
            P(("groups", "tp"), None, None, None),
            P(("groups", "tp"), None, None, None),
            P(("groups", "tp"), None),
        ),
        out_specs=P(("groups", "tp"), None, None),
        check_vma=False,
    )
```

```python
import jax
import jax.numpy as jnp
from jax import lax
from jax.sharding import PartitionSpec as P

D = 8192
KVH = 8
HD = 128
ROLL = 16
ROWS = 8
GR = 4
QG = 16
DS = 512


def from_partner(value, axis, bit):
    mask = 2**bit
    pairs = [(source, source ^ mask) for source in range(lax.axis_size(axis))]
    return lax.ppermute(value, axis, pairs)


def xor_swap(value, axis, bit):
    return from_partner(value, axis, bit)


def gather_xor(value, axis):
    n = lax.axis_size(axis)
    me = lax.axis_index(axis)
    held = value
    for bit in range(n.bit_length() - 1):
        other = xor_swap(held, axis, bit)
        low = ((me >> bit) & 1) == 0
        held = jnp.where(low, jnp.concatenate([held, other], 0), jnp.concatenate([other, held], 0))
    return held


def scatter_rounds(held, order, axis, bits):
    me = lax.axis_index(axis)
    for bit in bits:
        pos = order.index(bit)
        order = order[:pos] + order[pos + 1 :]
        low = ((me >> bit) & 1) == 0
        first = lax.index_in_dim(held, 0, pos, keepdims=False)
        second = lax.index_in_dim(held, 1, pos, keepdims=False)
        keep = jnp.where(low, first, second)
        give = jnp.where(low, second, first)
        held = keep + xor_swap(give, axis, bit)
    return held, order


def scatter_sum_xor(pieces, axis):
    n = lax.axis_size(axis)
    bits = n.bit_length() - 1
    me = lax.axis_index(axis)
    held = pieces.reshape((2,) * bits + pieces.shape[1:])
    order = list(range(bits - 1, -1, -1))
    for bit in range(bits):
        pos = order.index(bit)
        order.pop(pos)
        low = ((me >> bit) & 1) == 0
        first = lax.index_in_dim(held, 0, pos, keepdims=False)
        second = lax.index_in_dim(held, 1, pos, keepdims=False)
        keep = jnp.where(low, first, second)
        give = jnp.where(low, second, first)
        held = keep + xor_swap(give, axis, bit)
    return held[None]


def pick(table, idx):
    hit = idx[:, None] == jnp.arange(table.shape[0], dtype=idx.dtype)[None, :]
    hit = hit.reshape(hit.shape + (1,) * (table.ndim - 1))
    return jnp.sum(jnp.where(hit, table[None], jnp.zeros((), table.dtype)), axis=1)


def gather_rounds(held, axis, bits):
    me = lax.axis_index(axis)
    for bit in bits:
        other = xor_swap(held, axis, bit)
        low = ((me >> bit) & 1) == 0
        held = jnp.where(low, jnp.concatenate([held, other], 0), jnp.concatenate([other, held], 0))
    return held


def exchange_rounds(held, axis, bits):
    me = lax.axis_index(axis)
    count = len(bits)
    for done, bit in enumerate(bits):
        low = ((me >> bit) & 1) == 0
        first = lax.index_in_dim(held, 0, 0, keepdims=False)
        second = lax.index_in_dim(held, 1, 0, keepdims=False)
        keep = jnp.where(low, first, second)
        give = jnp.where(low, second, first)
        got = xor_swap(give, axis, bit)
        at = count - done - 1 + done
        held = jnp.where(low, jnp.stack([keep, got], at), jnp.stack([got, keep], at))
    return held


def swap_rows(value, axis, col_bits, s):
    shift = s << col_bits
    return lax.ppermute(value, axis, [(t, t ^ shift) for t in range(lax.axis_size(axis))])


def swap_cols(value, axis, s):
    return lax.ppermute(value, axis, [(t, t ^ s) for t in range(lax.axis_size(axis))])


def norm_rows(rows_float, norm_gain):
    mean_square = jnp.mean(rows_float * rows_float, axis=-1, keepdims=True)
    return (rows_float * lax.rsqrt(mean_square + 1e-05) * norm_gain[None, :]).astype(jnp.bfloat16)


def local(
    hidden_in, norm_gain, q_blocks, o_blocks, kv_blocks, kv_assign, key_cache, value_cache, lengths
):
    ranks = lax.axis_size("tp")
    my_index = lax.axis_index("tp")
    my_rank = my_index % ROLL
    my_half = my_rank % 2
    grid_cols = ranks // GR
    group_count = ranks // ROLL
    col_width = q_blocks.shape[3]
    key_width = kv_blocks.shape[2]
    grid_row = my_index // grid_cols
    grid_col = my_index % grid_cols
    dest_ids = jnp.arange(ranks, dtype=jnp.int32)
    dest_rank = dest_ids % ROLL
    dest_head = pick(kv_assign, dest_rank)
    dest_group = 2 * dest_head + dest_rank % 2
    dest_copy = dest_ids // ROLL
    bits = ranks.bit_length() - 1
    col_bits = grid_cols.bit_length() - 1
    row_bits = GR.bit_length() - 1
    row_order = jnp.arange(GR, dtype=jnp.int32) ^ grid_row
    col_order = jnp.arange(grid_cols, dtype=jnp.int32) ^ grid_col
    direct_cols = grid_cols <= 4
    fast_norm = direct_cols and group_count == 1 and GR == grid_cols and col_width == grid_cols * DS
    fast_norm = fast_norm and key_width == DS
    if direct_cols:
        from_cols = [hidden_in[0]] + [swap_cols(hidden_in[0], "tp", s) for s in range(1, grid_cols)]
        in_row = jnp.stack(from_cols)
        if not fast_norm:
            in_row = pick(in_row, col_order)
    else:
        in_row = gather_rounds(hidden_in, "tp", range(col_bits))
    from_rows = [in_row] + [swap_rows(in_row, "tp", col_bits, s) for s in range(1, GR)]
    if fast_norm:
        arrived = jnp.stack(from_rows).astype(jnp.float32)
        mean_square = jnp.sum(arrived * arrived, axis=(0, 1, 3))[:, None] / D
        scale_rows = lax.rsqrt(mean_square + 1e-05)
        col_x = pick(lax.dynamic_index_in_dim(arrived, grid_row ^ grid_col, 0, keepdims=False), col_order)
        col_x = col_x.transpose(1, 0, 2).reshape(ROWS, col_width)
        col_gain = lax.dynamic_slice_in_dim(norm_gain, grid_col * col_width, col_width)
        col_rows = (col_x * scale_rows * col_gain[None, :]).astype(jnp.bfloat16)
        own_gain = lax.dynamic_slice_in_dim(norm_gain, my_index * key_width, key_width)
        key_rows = (hidden_in[0].astype(jnp.float32) * scale_rows * own_gain[None, :]).astype(jnp.bfloat16)
    else:
        every_rows = pick(jnp.stack(from_rows), row_order).reshape(ranks, ROWS, DS)
        rows_float = (
            every_rows.reshape(group_count, ROLL, ROWS, DS)
            .transpose(0, 2, 1, 3)
            .reshape(group_count * ROWS, D)
            .astype(jnp.float32)
        )
        normed_every = norm_rows(rows_float, norm_gain)
        col_rows = lax.dynamic_slice_in_dim(normed_every, grid_col * col_width, col_width, 1)
        key_rows = lax.dynamic_slice_in_dim(normed_every, my_index * key_width, key_width, 1)
    query_part = jnp.einsum(
        "rc,aec->rae", col_rows, q_blocks[0], preferred_element_type=jnp.float32
    )
    query_part = (
        query_part.reshape(group_count, ROWS, QG, HD)
        .transpose(0, 2, 1, 3)
        .reshape(group_count * QG, ROWS, HD)
    )
    query_pairs = pick(query_part.reshape(group_count * KVH, 2, ROWS, HD), dest_copy * KVH + dest_head)
    query_pick = query_pairs.transpose(0, 2, 1, 3).reshape(ranks, ROWS, 2 * HD)
    keyval_part = jnp.einsum("rc,kfc->rkf", key_rows, kv_blocks, preferred_element_type=jnp.float32)
    keyval_part = (
        keyval_part.reshape(group_count, ROWS, 2, KVH, HD)
        .transpose(0, 3, 1, 2, 4)
        .reshape(group_count * KVH, ROWS, 2 * HD)
    )
    keyval_term = pick(keyval_part, dest_copy * KVH + dest_head)
    width = 4 * HD
    compact = jnp.concatenate([query_pick, keyval_term], -1)
    if direct_cols:
        by_col = compact.reshape(GR, grid_cols, ROWS, width)
        held = lax.dynamic_index_in_dim(by_col, grid_col, 1, keepdims=False)
        for s in range(1, grid_cols):
            held = held + swap_cols(lax.dynamic_index_in_dim(by_col, grid_col ^ s, 1, keepdims=False), "tp", s)
    else:
        held, _ = scatter_rounds(
            compact.reshape((2,) * bits + (ROWS, width)), list(range(bits - 1, -1, -1)), "tp", range(col_bits)
        )
        held = held.reshape(GR, ROWS, width)
    from_rows = [lax.dynamic_index_in_dim(held, grid_row, 0, keepdims=False)]
    for s in range(1, GR):
        piece = lax.dynamic_index_in_dim(held, grid_row ^ s, 0, keepdims=False)
        from_rows.append(swap_rows(piece, "tp", col_bits, s))
    halves_q = [
        pick(jnp.stack([got[:, h * HD : (h + 1) * HD] for got in from_rows]), row_order) for h in range(2)
    ]
    both_queries = jnp.stack(halves_q).transpose(2, 0, 1, 3).reshape(ROWS, 2 * GR, HD).astype(jnp.bfloat16)
    keyval_sum = from_rows[0][:, 2 * HD :]
    for got in from_rows[1:]:
        keyval_sum = keyval_sum + got[:, 2 * HD :]
    keyval_new = keyval_sum.astype(jnp.bfloat16)
    key_new = keyval_new[:, :HD]
    value_new = keyval_new[:, HD:]
    scale = 1.0 / HD**0.5
    scores = (
        jnp.einsum("bhe,bte->bht", both_queries, key_cache[0], preferred_element_type=jnp.float32)
        * scale
    )
    positions = jnp.arange(scores.shape[2], dtype=jnp.int32)
    masked = positions[None, None, :] < lengths[0][:, None, None]
    new_score = (
        jnp.einsum("bhe,be->bh", both_queries, key_new, preferred_element_type=jnp.float32) * scale
    )
    new_score = jnp.where(my_half == 0, new_score, jnp.float32(-1e30))
    top = jnp.maximum(jnp.max(jnp.where(masked, scores, jnp.float32(-1e30)), axis=-1), new_score)
    weights = jnp.where(masked, jnp.exp(scores - top[..., None]), jnp.float32(0.0))
    new_weight = jnp.exp(new_score - top)
    total = jnp.sum(weights, axis=-1) + new_weight
    summed = jnp.einsum(
        "bht,bte->bhe",
        weights.astype(jnp.bfloat16),
        value_cache[0],
        preferred_element_type=jnp.float32,
    )
    new_rounded = lax.optimization_barrier(new_weight.astype(jnp.bfloat16)).astype(jnp.float32)
    summed = summed + new_rounded[..., None] * value_new.astype(jnp.float32)[:, None, :]
    top_split = top.reshape(ROWS, 2, GR)
    total_split = total.reshape(ROWS, 2, GR)
    summed_split = summed.reshape(ROWS, 2, GR, HD)
    first_half = my_half == 0
    own_top = jnp.where(first_half, top_split[:, 0], top_split[:, 1])
    own_total = jnp.where(first_half, total_split[:, 0], total_split[:, 1])
    own_summed = jnp.where(first_half, summed_split[:, 0], summed_split[:, 1])
    give_top = jnp.where(first_half, top_split[:, 1], top_split[:, 0])
    give_total = jnp.where(first_half, total_split[:, 1], total_split[:, 0])
    give_summed = jnp.where(first_half, summed_split[:, 1], summed_split[:, 0])
    give = jnp.concatenate([give_summed, give_top[..., None], give_total[..., None]], -1)
    got = from_partner(give, "tp", 0)
    got_summed, got_top, got_total = got[..., :HD], got[..., HD], got[..., HD + 1]
    joint = jnp.maximum(own_top, got_top)
    factor_own = jnp.exp(own_top - joint)
    factor_got = jnp.exp(got_top - joint)
    numer = own_summed * factor_own[..., None] + got_summed * factor_got[..., None]
    denom = own_total * factor_own + got_total * factor_got
    attention = (numer / denom[..., None]).astype(jnp.bfloat16)
    from_rows = [lax.dynamic_index_in_dim(attention, grid_row, 1, keepdims=False)]
    for s in range(1, GR):
        piece = lax.dynamic_index_in_dim(attention, grid_row ^ s, 1, keepdims=False)
        from_rows.append(swap_rows(piece, "tp", col_bits, s))
    by_row = pick(jnp.stack(from_rows), row_order)
    if direct_cols:
        from_cols = [by_row] + [swap_cols(by_row, "tp", s) for s in range(1, grid_cols)]
        every_slot = pick(jnp.stack(from_cols), col_order)
    else:
        every_slot = gather_rounds(by_row[None], "tp", range(col_bits))
    every_slot = every_slot.transpose(1, 0, 2, 3).reshape(group_count, ROLL, ROWS, HD)
    head_ids = jnp.arange(KVH, dtype=jnp.int32)
    pair_heads = kv_assign.reshape(KVH, 2)[:, 0]
    inverse = jnp.sum(
        head_ids[None, :] * (pair_heads[None, :] == head_ids[:, None]).astype(jnp.int32), axis=1
    )
    slot_ids = jnp.arange(QG, dtype=jnp.int32)
    rank_of_slot = 2 * jnp.broadcast_to(inverse[:, None], (KVH, 2)).reshape(QG) + slot_ids % 2
    chosen = jax.vmap(lambda per_group: pick(per_group, rank_of_slot))(every_slot)
    out_part = jnp.einsum("gabe,cae->gbc", chosen, o_blocks[0], preferred_element_type=jnp.float32)
    if group_count == 1 and grid_cols == GR and col_width == GR * DS:
        pieces = out_part[0].reshape(ROWS, GR, DS)
        my_cols = None
        for s in range(GR):
            piece = lax.dynamic_index_in_dim(pieces, grid_row ^ s, 1, keepdims=False)
            pairs = [(i * grid_cols + j, j * grid_cols + (i ^ s)) for i in range(GR) for j in range(grid_cols)]
            got = lax.ppermute(piece, "tp", pairs)
            my_cols = got if my_cols is None else my_cols + got
    else:
        placed = jnp.zeros((group_count, ROWS, D), jnp.float32)
        placed = lax.dynamic_update_slice_in_dim(placed, out_part, grid_col * col_width, 2)
        out_term = (
            placed.reshape(group_count, ROWS, ROLL, DS).transpose(0, 2, 1, 3).reshape(ranks * ROWS, DS)
        )
        my_cols = scatter_sum_xor(out_term.reshape(ranks, ROWS, DS), "tp")[0]
    return my_cols.astype(jnp.bfloat16)[None]


def solution(mesh):
    return jax.shard_map(
        local,
        mesh=mesh,
        in_specs=(
            P(("groups", "tp"), None, None),
            P(),
            P("tp", None, None, None),
            P("tp", None, None, None),
            P(None, None, "tp"),
            P(),
            P(("groups", "tp"), None, None, None),
            P(("groups", "tp"), None, None, None),
            P(("groups", "tp"), None),
        ),
        out_specs=P(("groups", "tp"), None, None),
        check_vma=False,
    )
```

```python
import jax
import jax.numpy as jnp
from jax import lax
from jax.sharding import PartitionSpec as P

D = 8192
KVH = 8
HD = 128
ROLL = 16
ROWS = 8
GR = 4
QG = 16
DS = 512


def from_partner(value, axis, bit):
    mask = 2**bit
    pairs = [(source, source ^ mask) for source in range(lax.axis_size(axis))]
    return lax.ppermute(value, axis, pairs)


def xor_swap(value, axis, bit):
    return from_partner(value, axis, bit)


def gather_xor(value, axis):
    n = lax.axis_size(axis)
    me = lax.axis_index(axis)
    held = value
    for bit in range(n.bit_length() - 1):
        other = xor_swap(held, axis, bit)
        low = ((me >> bit) & 1) == 0
        held = jnp.where(low, jnp.concatenate([held, other], 0), jnp.concatenate([other, held], 0))
    return held


def scatter_rounds(held, order, axis, bits):
    me = lax.axis_index(axis)
    for bit in bits:
        pos = order.index(bit)
        order = order[:pos] + order[pos + 1 :]
        low = ((me >> bit) & 1) == 0
        first = lax.index_in_dim(held, 0, pos, keepdims=False)
        second = lax.index_in_dim(held, 1, pos, keepdims=False)
        keep = jnp.where(low, first, second)
        give = jnp.where(low, second, first)
        held = keep + xor_swap(give, axis, bit)
    return held, order


def scatter_sum_xor(pieces, axis):
    n = lax.axis_size(axis)
    bits = n.bit_length() - 1
    me = lax.axis_index(axis)
    held = pieces.reshape((2,) * bits + pieces.shape[1:])
    order = list(range(bits - 1, -1, -1))
    for bit in range(bits):
        pos = order.index(bit)
        order.pop(pos)
        low = ((me >> bit) & 1) == 0
        first = lax.index_in_dim(held, 0, pos, keepdims=False)
        second = lax.index_in_dim(held, 1, pos, keepdims=False)
        keep = jnp.where(low, first, second)
        give = jnp.where(low, second, first)
        held = keep + xor_swap(give, axis, bit)
    return held[None]


def pick(table, idx):
    hit = idx[:, None] == jnp.arange(table.shape[0], dtype=idx.dtype)[None, :]
    hit = hit.reshape(hit.shape + (1,) * (table.ndim - 1))
    return jnp.sum(jnp.where(hit, table[None], jnp.zeros((), table.dtype)), axis=1)


def gather_rounds(held, axis, bits):
    me = lax.axis_index(axis)
    for bit in bits:
        other = xor_swap(held, axis, bit)
        low = ((me >> bit) & 1) == 0
        held = jnp.where(low, jnp.concatenate([held, other], 0), jnp.concatenate([other, held], 0))
    return held


def exchange_rounds(held, axis, bits):
    me = lax.axis_index(axis)
    count = len(bits)
    for done, bit in enumerate(bits):
        low = ((me >> bit) & 1) == 0
        first = lax.index_in_dim(held, 0, 0, keepdims=False)
        second = lax.index_in_dim(held, 1, 0, keepdims=False)
        keep = jnp.where(low, first, second)
        give = jnp.where(low, second, first)
        got = xor_swap(give, axis, bit)
        at = count - done - 1 + done
        held = jnp.where(low, jnp.stack([keep, got], at), jnp.stack([got, keep], at))
    return held


def swap_rows(value, axis, col_bits, s):
    shift = s << col_bits
    return lax.ppermute(value, axis, [(t, t ^ shift) for t in range(lax.axis_size(axis))])


def swap_cols(value, axis, s):
    return lax.ppermute(value, axis, [(t, t ^ s) for t in range(lax.axis_size(axis))])


def norm_rows(rows_float, norm_gain):
    mean_square = jnp.mean(rows_float * rows_float, axis=-1, keepdims=True)
    return (rows_float * lax.rsqrt(mean_square + 1e-05) * norm_gain[None, :]).astype(jnp.bfloat16)


def local(
    hidden_in, norm_gain, q_blocks, o_blocks, kv_blocks, kv_assign, key_cache, value_cache, lengths
):
    ranks = lax.axis_size("tp")
    my_index = lax.axis_index("tp")
    my_rank = my_index % ROLL
    my_half = my_rank % 2
    grid_cols = ranks // GR
    group_count = ranks // ROLL
    col_width = q_blocks.shape[3]
    key_width = kv_blocks.shape[2]
    grid_row = my_index // grid_cols
    grid_col = my_index % grid_cols
    dest_ids = jnp.arange(ranks, dtype=jnp.int32)
    dest_rank = dest_ids % ROLL
    dest_head = pick(kv_assign, dest_rank)
    dest_group = 2 * dest_head + dest_rank % 2
    dest_copy = dest_ids // ROLL
    bits = ranks.bit_length() - 1
    col_bits = grid_cols.bit_length() - 1
    row_bits = GR.bit_length() - 1
    row_order = jnp.arange(GR, dtype=jnp.int32) ^ grid_row
    col_order = jnp.arange(grid_cols, dtype=jnp.int32) ^ grid_col
    direct_cols = False
    fast_norm = group_count == 1 and GR == grid_cols and col_width == grid_cols * DS
    fast_norm = fast_norm and key_width == DS
    if direct_cols:
        from_cols = [hidden_in[0]] + [swap_cols(hidden_in[0], "tp", s) for s in range(1, grid_cols)]
        in_row = jnp.stack(from_cols)
        if not fast_norm:
            in_row = pick(in_row, col_order)
    else:
        in_row = gather_rounds(hidden_in, "tp", range(col_bits))
    from_rows = [in_row] + [swap_rows(in_row, "tp", col_bits, s) for s in range(1, GR)]
    if fast_norm:
        arrived = jnp.stack(from_rows).astype(jnp.float32)
        mean_square = jnp.sum(arrived * arrived, axis=(0, 1, 3))[:, None] / D
        scale_rows = lax.rsqrt(mean_square + 1e-05)
        col_x = lax.dynamic_index_in_dim(arrived, grid_row ^ grid_col, 0, keepdims=False)
        if direct_cols:
            col_x = pick(col_x, col_order)
        col_x = col_x.transpose(1, 0, 2).reshape(ROWS, col_width)
        col_gain = lax.dynamic_slice_in_dim(norm_gain, grid_col * col_width, col_width)
        col_rows = (col_x * scale_rows * col_gain[None, :]).astype(jnp.bfloat16)
        own_gain = lax.dynamic_slice_in_dim(norm_gain, my_index * key_width, key_width)
        key_rows = (hidden_in[0].astype(jnp.float32) * scale_rows * own_gain[None, :]).astype(jnp.bfloat16)
    else:
        every_rows = pick(jnp.stack(from_rows), row_order).reshape(ranks, ROWS, DS)
        rows_float = (
            every_rows.reshape(group_count, ROLL, ROWS, DS)
            .transpose(0, 2, 1, 3)
            .reshape(group_count * ROWS, D)
            .astype(jnp.float32)
        )
        normed_every = norm_rows(rows_float, norm_gain)
        col_rows = lax.dynamic_slice_in_dim(normed_every, grid_col * col_width, col_width, 1)
        key_rows = lax.dynamic_slice_in_dim(normed_every, my_index * key_width, key_width, 1)
    query_part = jnp.einsum(
        "rc,aec->rae", col_rows, q_blocks[0], preferred_element_type=jnp.float32
    )
    query_part = (
        query_part.reshape(group_count, ROWS, QG, HD)
        .transpose(0, 2, 1, 3)
        .reshape(group_count * QG, ROWS, HD)
    )
    query_pairs = pick(query_part.reshape(group_count * KVH, 2, ROWS, HD), dest_copy * KVH + dest_head)
    query_pick = query_pairs.transpose(0, 2, 1, 3).reshape(ranks, ROWS, 2 * HD)
    keyval_part = jnp.einsum("rc,kfc->rkf", key_rows, kv_blocks, preferred_element_type=jnp.float32)
    keyval_part = (
        keyval_part.reshape(group_count, ROWS, 2, KVH, HD)
        .transpose(0, 3, 1, 2, 4)
        .reshape(group_count * KVH, ROWS, 2 * HD)
    )
    keyval_term = pick(keyval_part, dest_copy * KVH + dest_head)
    width = 4 * HD
    compact = jnp.concatenate([query_pick, keyval_term], -1)
    if direct_cols:
        by_col = compact.reshape(GR, grid_cols, ROWS, width)
        held = lax.dynamic_index_in_dim(by_col, grid_col, 1, keepdims=False)
        for s in range(1, grid_cols):
            held = held + swap_cols(lax.dynamic_index_in_dim(by_col, grid_col ^ s, 1, keepdims=False), "tp", s)
    else:
        held, _ = scatter_rounds(
            compact.reshape((2,) * bits + (ROWS, width)), list(range(bits - 1, -1, -1)), "tp", range(col_bits)
        )
        held = held.reshape(GR, ROWS, width)
    from_rows = [lax.dynamic_index_in_dim(held, grid_row, 0, keepdims=False)]
    for s in range(1, GR):
        piece = lax.dynamic_index_in_dim(held, grid_row ^ s, 0, keepdims=False)
        from_rows.append(swap_rows(piece, "tp", col_bits, s))
    halves_q = [
        pick(jnp.stack([got[:, h * HD : (h + 1) * HD] for got in from_rows]), row_order) for h in range(2)
    ]
    both_queries = jnp.stack(halves_q).transpose(2, 0, 1, 3).reshape(ROWS, 2 * GR, HD).astype(jnp.bfloat16)
    keyval_sum = from_rows[0][:, 2 * HD :]
    for got in from_rows[1:]:
        keyval_sum = keyval_sum + got[:, 2 * HD :]
    keyval_new = keyval_sum.astype(jnp.bfloat16)
    key_new = keyval_new[:, :HD]
    value_new = keyval_new[:, HD:]
    scale = 1.0 / HD**0.5
    scores = (
        jnp.einsum("bhe,bte->bht", both_queries, key_cache[0], preferred_element_type=jnp.float32)
        * scale
    )
    positions = jnp.arange(scores.shape[2], dtype=jnp.int32)
    masked = positions[None, None, :] < lengths[0][:, None, None]
    new_score = (
        jnp.einsum("bhe,be->bh", both_queries, key_new, preferred_element_type=jnp.float32) * scale
    )
    new_score = jnp.where(my_half == 0, new_score, jnp.float32(-1e30))
    top = jnp.maximum(jnp.max(jnp.where(masked, scores, jnp.float32(-1e30)), axis=-1), new_score)
    weights = jnp.where(masked, jnp.exp(scores - top[..., None]), jnp.float32(0.0))
    new_weight = jnp.exp(new_score - top)
    total = jnp.sum(weights, axis=-1) + new_weight
    summed = jnp.einsum(
        "bht,bte->bhe",
        weights.astype(jnp.bfloat16),
        value_cache[0],
        preferred_element_type=jnp.float32,
    )
    new_rounded = lax.optimization_barrier(new_weight.astype(jnp.bfloat16)).astype(jnp.float32)
    summed = summed + new_rounded[..., None] * value_new.astype(jnp.float32)[:, None, :]
    top_split = top.reshape(ROWS, 2, GR)
    total_split = total.reshape(ROWS, 2, GR)
    summed_split = summed.reshape(ROWS, 2, GR, HD)
    first_half = my_half == 0
    own_top = jnp.where(first_half, top_split[:, 0], top_split[:, 1])
    own_total = jnp.where(first_half, total_split[:, 0], total_split[:, 1])
    own_summed = jnp.where(first_half, summed_split[:, 0], summed_split[:, 1])
    give_top = jnp.where(first_half, top_split[:, 1], top_split[:, 0])
    give_total = jnp.where(first_half, total_split[:, 1], total_split[:, 0])
    give_summed = jnp.where(first_half, summed_split[:, 1], summed_split[:, 0])
    give = jnp.concatenate([give_summed, give_top[..., None], give_total[..., None]], -1)
    got = from_partner(give, "tp", 0)
    got_summed, got_top, got_total = got[..., :HD], got[..., HD], got[..., HD + 1]
    joint = jnp.maximum(own_top, got_top)
    factor_own = jnp.exp(own_top - joint)
    factor_got = jnp.exp(got_top - joint)
    numer = own_summed * factor_own[..., None] + got_summed * factor_got[..., None]
    denom = own_total * factor_own + got_total * factor_got
    attention = (numer / denom[..., None]).astype(jnp.bfloat16)
    from_rows = [lax.dynamic_index_in_dim(attention, grid_row, 1, keepdims=False)]
    for s in range(1, GR):
        piece = lax.dynamic_index_in_dim(attention, grid_row ^ s, 1, keepdims=False)
        from_rows.append(swap_rows(piece, "tp", col_bits, s))
    by_row = pick(jnp.stack(from_rows), row_order)
    if direct_cols:
        from_cols = [by_row] + [swap_cols(by_row, "tp", s) for s in range(1, grid_cols)]
        every_slot = pick(jnp.stack(from_cols), col_order)
    else:
        every_slot = gather_rounds(by_row[None], "tp", range(col_bits))
    every_slot = every_slot.transpose(1, 0, 2, 3).reshape(group_count, ROLL, ROWS, HD)
    head_ids = jnp.arange(KVH, dtype=jnp.int32)
    pair_heads = kv_assign.reshape(KVH, 2)[:, 0]
    inverse = jnp.sum(
        head_ids[None, :] * (pair_heads[None, :] == head_ids[:, None]).astype(jnp.int32), axis=1
    )
    slot_ids = jnp.arange(QG, dtype=jnp.int32)
    rank_of_slot = 2 * jnp.broadcast_to(inverse[:, None], (KVH, 2)).reshape(QG) + slot_ids % 2
    chosen = jax.vmap(lambda per_group: pick(per_group, rank_of_slot))(every_slot)
    out_part = jnp.einsum("gabe,cae->gbc", chosen, o_blocks[0], preferred_element_type=jnp.float32)
    if group_count == 1 and grid_cols == GR and col_width == GR * DS:
        pieces = out_part[0].reshape(ROWS, GR, DS)
        my_cols = None
        for s in range(GR):
            piece = lax.dynamic_index_in_dim(pieces, grid_row ^ s, 1, keepdims=False)
            pairs = [(i * grid_cols + j, j * grid_cols + (i ^ s)) for i in range(GR) for j in range(grid_cols)]
            got = lax.ppermute(piece, "tp", pairs)
            my_cols = got if my_cols is None else my_cols + got
    else:
        placed = jnp.zeros((group_count, ROWS, D), jnp.float32)
        placed = lax.dynamic_update_slice_in_dim(placed, out_part, grid_col * col_width, 2)
        out_term = (
            placed.reshape(group_count, ROWS, ROLL, DS).transpose(0, 2, 1, 3).reshape(ranks * ROWS, DS)
        )
        my_cols = scatter_sum_xor(out_term.reshape(ranks, ROWS, DS), "tp")[0]
    return my_cols.astype(jnp.bfloat16)[None]


def solution(mesh):
    return jax.shard_map(
        local,
        mesh=mesh,
        in_specs=(
            P(("groups", "tp"), None, None),
            P(),
            P("tp", None, None, None),
            P("tp", None, None, None),
            P(None, None, "tp"),
            P(),
            P(("groups", "tp"), None, None, None),
            P(("groups", "tp"), None, None, None),
            P(("groups", "tp"), None),
        ),
        out_specs=P(("groups", "tp"), None, None),
        check_vma=False,
    )
```

```python
import jax
import jax.numpy as jnp
from jax import lax
from jax.sharding import PartitionSpec as P

D = 8192
KVH = 8
HD = 128
ROLL = 16
ROWS = 8
GR = 4
QG = 16
DS = 512


def from_partner(value, axis, bit):
    mask = 2**bit
    pairs = [(source, source ^ mask) for source in range(lax.axis_size(axis))]
    return lax.ppermute(value, axis, pairs)


def xor_swap(value, axis, bit):
    return from_partner(value, axis, bit)


def gather_xor(value, axis):
    n = lax.axis_size(axis)
    me = lax.axis_index(axis)
    held = value
    for bit in range(n.bit_length() - 1):
        other = xor_swap(held, axis, bit)
        low = ((me >> bit) & 1) == 0
        held = jnp.where(low, jnp.concatenate([held, other], 0), jnp.concatenate([other, held], 0))
    return held


def scatter_rounds(held, order, axis, bits):
    me = lax.axis_index(axis)
    for bit in bits:
        pos = order.index(bit)
        order = order[:pos] + order[pos + 1 :]
        low = ((me >> bit) & 1) == 0
        first = lax.index_in_dim(held, 0, pos, keepdims=False)
        second = lax.index_in_dim(held, 1, pos, keepdims=False)
        keep = jnp.where(low, first, second)
        give = jnp.where(low, second, first)
        held = keep + xor_swap(give, axis, bit)
    return held, order


def scatter_sum_xor(pieces, axis):
    n = lax.axis_size(axis)
    bits = n.bit_length() - 1
    me = lax.axis_index(axis)
    held = pieces.reshape((2,) * bits + pieces.shape[1:])
    order = list(range(bits - 1, -1, -1))
    for bit in range(bits):
        pos = order.index(bit)
        order.pop(pos)
        low = ((me >> bit) & 1) == 0
        first = lax.index_in_dim(held, 0, pos, keepdims=False)
        second = lax.index_in_dim(held, 1, pos, keepdims=False)
        keep = jnp.where(low, first, second)
        give = jnp.where(low, second, first)
        held = keep + xor_swap(give, axis, bit)
    return held[None]


def pick(table, idx):
    hit = idx[:, None] == jnp.arange(table.shape[0], dtype=idx.dtype)[None, :]
    hit = hit.reshape(hit.shape + (1,) * (table.ndim - 1))
    return jnp.sum(jnp.where(hit, table[None], jnp.zeros((), table.dtype)), axis=1)


def gather_rounds(held, axis, bits):
    me = lax.axis_index(axis)
    for bit in bits:
        other = xor_swap(held, axis, bit)
        low = ((me >> bit) & 1) == 0
        held = jnp.where(low, jnp.concatenate([held, other], 0), jnp.concatenate([other, held], 0))
    return held


def exchange_rounds(held, axis, bits):
    me = lax.axis_index(axis)
    count = len(bits)
    for done, bit in enumerate(bits):
        low = ((me >> bit) & 1) == 0
        first = lax.index_in_dim(held, 0, 0, keepdims=False)
        second = lax.index_in_dim(held, 1, 0, keepdims=False)
        keep = jnp.where(low, first, second)
        give = jnp.where(low, second, first)
        got = xor_swap(give, axis, bit)
        at = count - done - 1 + done
        held = jnp.where(low, jnp.stack([keep, got], at), jnp.stack([got, keep], at))
    return held


def swap_rows(value, axis, col_bits, s):
    shift = s << col_bits
    return lax.ppermute(value, axis, [(t, t ^ shift) for t in range(lax.axis_size(axis))])


def swap_cols(value, axis, s):
    return lax.ppermute(value, axis, [(t, t ^ s) for t in range(lax.axis_size(axis))])


def norm_rows(rows_float, norm_gain):
    mean_square = jnp.mean(rows_float * rows_float, axis=-1, keepdims=True)
    return (rows_float * lax.rsqrt(mean_square + 1e-05) * norm_gain[None, :]).astype(jnp.bfloat16)


def local(
    hidden_in, norm_gain, q_blocks, o_blocks, kv_blocks, kv_assign, key_cache, value_cache, lengths
):
    ranks = lax.axis_size("tp")
    my_index = lax.axis_index("tp")
    my_rank = my_index % ROLL
    my_half = my_rank % 2
    grid_cols = ranks // GR
    group_count = ranks // ROLL
    col_width = q_blocks.shape[3]
    key_width = kv_blocks.shape[2]
    grid_row = my_index // grid_cols
    grid_col = my_index % grid_cols
    dest_ids = jnp.arange(ranks, dtype=jnp.int32)
    dest_rank = dest_ids % ROLL
    dest_head = pick(kv_assign, dest_rank)
    dest_group = 2 * dest_head + dest_rank % 2
    dest_copy = dest_ids // ROLL
    bits = ranks.bit_length() - 1
    col_bits = grid_cols.bit_length() - 1
    row_bits = GR.bit_length() - 1
    row_order = jnp.arange(GR, dtype=jnp.int32) ^ grid_row
    col_order = jnp.arange(grid_cols, dtype=jnp.int32) ^ grid_col
    direct_cols = grid_cols <= 4
    fast_norm = direct_cols and group_count == 1 and GR == grid_cols and col_width == grid_cols * DS
    fast_norm = fast_norm and key_width == DS
    if direct_cols:
        from_cols = [hidden_in[0]] + [swap_cols(hidden_in[0], "tp", s) for s in range(1, grid_cols)]
        in_row = jnp.stack(from_cols)
        if not fast_norm:
            in_row = pick(in_row, col_order)
    else:
        in_row = gather_rounds(hidden_in, "tp", range(col_bits))
    from_rows = [in_row] + [swap_rows(in_row, "tp", col_bits, s) for s in range(1, GR)]
    if fast_norm:
        arrived = jnp.stack(from_rows).astype(jnp.float32)
        mean_square = jnp.sum(arrived * arrived, axis=(0, 1, 3))[:, None] / D
        scale_rows = lax.rsqrt(mean_square + 1e-05)
        col_x = pick(lax.dynamic_index_in_dim(arrived, grid_row ^ grid_col, 0, keepdims=False), col_order)
        col_x = col_x.transpose(1, 0, 2).reshape(ROWS, col_width)
        col_gain = lax.dynamic_slice_in_dim(norm_gain, grid_col * col_width, col_width)
        col_rows = (col_x * scale_rows * col_gain[None, :]).astype(jnp.bfloat16)
        own_gain = lax.dynamic_slice_in_dim(norm_gain, my_index * key_width, key_width)
        key_rows = (hidden_in[0].astype(jnp.float32) * scale_rows * own_gain[None, :]).astype(jnp.bfloat16)
    else:
        every_rows = pick(jnp.stack(from_rows), row_order).reshape(ranks, ROWS, DS)
        rows_float = (
            every_rows.reshape(group_count, ROLL, ROWS, DS)
            .transpose(0, 2, 1, 3)
            .reshape(group_count * ROWS, D)
            .astype(jnp.float32)
        )
        normed_every = norm_rows(rows_float, norm_gain)
        col_rows = lax.dynamic_slice_in_dim(normed_every, grid_col * col_width, col_width, 1)
        key_rows = lax.dynamic_slice_in_dim(normed_every, my_index * key_width, key_width, 1)
    query_part = jnp.einsum(
        "rc,aec->rae", col_rows, q_blocks[0], preferred_element_type=jnp.float32
    )
    query_part = (
        query_part.reshape(group_count, ROWS, QG, HD)
        .transpose(0, 2, 1, 3)
        .reshape(group_count * QG, ROWS, HD)
    )
    query_pairs = pick(query_part.reshape(group_count * KVH, 2, ROWS, HD), dest_copy * KVH + dest_head)
    query_pick = query_pairs.transpose(0, 2, 1, 3).reshape(ranks, ROWS, 2 * HD)
    keyval_part = jnp.einsum("rc,kfc->rkf", key_rows, kv_blocks, preferred_element_type=jnp.float32)
    keyval_part = (
        keyval_part.reshape(group_count, ROWS, 2, KVH, HD)
        .transpose(0, 3, 1, 2, 4)
        .reshape(group_count * KVH, ROWS, 2 * HD)
    )
    keyval_term = pick(keyval_part, dest_copy * KVH + dest_head)
    width = 4 * HD
    compact = jnp.concatenate([query_pick, keyval_term], -1)
    if direct_cols:
        by_col = compact.reshape(GR, grid_cols, ROWS, width)
        held = lax.dynamic_index_in_dim(by_col, grid_col, 1, keepdims=False)
        for s in range(1, grid_cols):
            held = held + swap_cols(lax.dynamic_index_in_dim(by_col, grid_col ^ s, 1, keepdims=False), "tp", s)
    else:
        held, _ = scatter_rounds(
            compact.reshape((2,) * bits + (ROWS, width)), list(range(bits - 1, -1, -1)), "tp", range(col_bits)
        )
        held = held.reshape(GR, ROWS, width)
    from_rows = [lax.dynamic_index_in_dim(held, grid_row, 0, keepdims=False)]
    for s in range(1, GR):
        piece = lax.dynamic_index_in_dim(held, grid_row ^ s, 0, keepdims=False)
        from_rows.append(swap_rows(piece, "tp", col_bits, s))
    halves_q = [
        pick(jnp.stack([got[:, h * HD : (h + 1) * HD] for got in from_rows]), row_order) for h in range(2)
    ]
    both_queries = jnp.stack(halves_q).transpose(2, 0, 1, 3).reshape(ROWS, 2 * GR, HD).astype(jnp.bfloat16)
    keyval_sum = from_rows[0][:, 2 * HD :]
    for got in from_rows[1:]:
        keyval_sum = keyval_sum + got[:, 2 * HD :]
    keyval_new = keyval_sum.astype(jnp.bfloat16)
    key_new = keyval_new[:, :HD]
    value_new = keyval_new[:, HD:]
    scale = 1.0 / HD**0.5
    scores = (
        jnp.einsum("bhe,bte->bht", both_queries, key_cache[0], preferred_element_type=jnp.float32)
        * scale
    )
    positions = jnp.arange(scores.shape[2], dtype=jnp.int32)
    masked = positions[None, None, :] < lengths[0][:, None, None]
    new_score = (
        jnp.einsum("bhe,be->bh", both_queries, key_new, preferred_element_type=jnp.float32) * scale
    )
    new_score = jnp.where(my_half == 0, new_score, jnp.float32(-1e30))
    top = jnp.maximum(jnp.max(jnp.where(masked, scores, jnp.float32(-1e30)), axis=-1), new_score)
    weights = jnp.where(masked, jnp.exp(scores - top[..., None]), jnp.float32(0.0))
    new_weight = jnp.exp(new_score - top)
    total = jnp.sum(weights, axis=-1) + new_weight
    summed = jnp.einsum(
        "bht,bte->bhe",
        weights.astype(jnp.bfloat16),
        value_cache[0],
        preferred_element_type=jnp.float32,
    )
    new_rounded = lax.optimization_barrier(new_weight.astype(jnp.bfloat16)).astype(jnp.float32)
    summed = summed + new_rounded[..., None] * value_new.astype(jnp.float32)[:, None, :]
    if direct_cols:
        parts = jnp.concatenate([summed, top[..., None], total[..., None]], -1)
        parts = parts.reshape(ROWS, 2, GR, HD + 2).transpose(2, 0, 1, 3)
        from_rows = [lax.dynamic_index_in_dim(parts, grid_row, 0, keepdims=False)]
        for s in range(1, GR):
            piece = lax.dynamic_index_in_dim(parts, grid_row ^ s, 0, keepdims=False)
            from_rows.append(swap_rows(piece, "tp", col_bits, s))
        by_row = pick(jnp.stack(from_rows), row_order)
        from_cols = [by_row] + [swap_cols(by_row, "tp", s) for s in range(1, grid_cols)]
        every_part = pick(jnp.stack(from_cols), col_order).reshape(grid_cols // 2, 2, GR, ROWS, 2, HD + 2)
        first = every_part[:, 0]
        second = every_part[:, 1]
        joint = jnp.maximum(first[..., HD], second[..., HD])
        factor_first = jnp.exp(first[..., HD] - joint)
        factor_second = jnp.exp(second[..., HD] - joint)
        numer = first[..., :HD] * factor_first[..., None] + second[..., :HD] * factor_second[..., None]
        denom = first[..., HD + 1] * factor_first + second[..., HD + 1] * factor_second
        pair_attn = (numer / denom[..., None]).astype(jnp.bfloat16)
        every_slot = pair_attn.transpose(1, 0, 3, 2, 4).reshape(group_count, ROLL, ROWS, HD)
    else:
        top_split = top.reshape(ROWS, 2, GR)
        total_split = total.reshape(ROWS, 2, GR)
        summed_split = summed.reshape(ROWS, 2, GR, HD)
        first_half = my_half == 0
        own_top = jnp.where(first_half, top_split[:, 0], top_split[:, 1])
        own_total = jnp.where(first_half, total_split[:, 0], total_split[:, 1])
        own_summed = jnp.where(first_half, summed_split[:, 0], summed_split[:, 1])
        give_top = jnp.where(first_half, top_split[:, 1], top_split[:, 0])
        give_total = jnp.where(first_half, total_split[:, 1], total_split[:, 0])
        give_summed = jnp.where(first_half, summed_split[:, 1], summed_split[:, 0])
        give = jnp.concatenate([give_summed, give_top[..., None], give_total[..., None]], -1)
        got = from_partner(give, "tp", 0)
        got_summed, got_top, got_total = got[..., :HD], got[..., HD], got[..., HD + 1]
        joint = jnp.maximum(own_top, got_top)
        factor_own = jnp.exp(own_top - joint)
        factor_got = jnp.exp(got_top - joint)
        numer = own_summed * factor_own[..., None] + got_summed * factor_got[..., None]
        denom = own_total * factor_own + got_total * factor_got
        attention = (numer / denom[..., None]).astype(jnp.bfloat16)
        from_rows = [lax.dynamic_index_in_dim(attention, grid_row, 1, keepdims=False)]
        for s in range(1, GR):
            piece = lax.dynamic_index_in_dim(attention, grid_row ^ s, 1, keepdims=False)
            from_rows.append(swap_rows(piece, "tp", col_bits, s))
        by_row = pick(jnp.stack(from_rows), row_order)
        if direct_cols:
            from_cols = [by_row] + [swap_cols(by_row, "tp", s) for s in range(1, grid_cols)]
            every_slot = pick(jnp.stack(from_cols), col_order)
        else:
            every_slot = gather_rounds(by_row[None], "tp", range(col_bits))
        every_slot = every_slot.transpose(1, 0, 2, 3).reshape(group_count, ROLL, ROWS, HD)
    head_ids = jnp.arange(KVH, dtype=jnp.int32)
    pair_heads = kv_assign.reshape(KVH, 2)[:, 0]
    inverse = jnp.sum(
        head_ids[None, :] * (pair_heads[None, :] == head_ids[:, None]).astype(jnp.int32), axis=1
    )
    slot_ids = jnp.arange(QG, dtype=jnp.int32)
    rank_of_slot = 2 * jnp.broadcast_to(inverse[:, None], (KVH, 2)).reshape(QG) + slot_ids % 2
    chosen = jax.vmap(lambda per_group: pick(per_group, rank_of_slot))(every_slot)
    out_part = jnp.einsum("gabe,cae->gbc", chosen, o_blocks[0], preferred_element_type=jnp.float32)
    if group_count == 1 and grid_cols == GR and col_width == GR * DS:
        pieces = out_part[0].reshape(ROWS, GR, DS)
        my_cols = None
        for s in range(GR):
            piece = lax.dynamic_index_in_dim(pieces, grid_row ^ s, 1, keepdims=False)
            pairs = [(i * grid_cols + j, j * grid_cols + (i ^ s)) for i in range(GR) for j in range(grid_cols)]
            got = lax.ppermute(piece, "tp", pairs)
            my_cols = got if my_cols is None else my_cols + got
    else:
        placed = jnp.zeros((group_count, ROWS, D), jnp.float32)
        placed = lax.dynamic_update_slice_in_dim(placed, out_part, grid_col * col_width, 2)
        out_term = (
            placed.reshape(group_count, ROWS, ROLL, DS).transpose(0, 2, 1, 3).reshape(ranks * ROWS, DS)
        )
        my_cols = scatter_sum_xor(out_term.reshape(ranks, ROWS, DS), "tp")[0]
    return my_cols.astype(jnp.bfloat16)[None]


def solution(mesh):
    return jax.shard_map(
        local,
        mesh=mesh,
        in_specs=(
            P(("groups", "tp"), None, None),
            P(),
            P("tp", None, None, None),
            P("tp", None, None, None),
            P(None, None, "tp"),
            P(),
            P(("groups", "tp"), None, None, None),
            P(("groups", "tp"), None, None, None),
            P(("groups", "tp"), None),
        ),
        out_specs=P(("groups", "tp"), None, None),
        check_vma=False,
    )
```

```python
import jax
import jax.numpy as jnp
from jax import lax
from jax.sharding import PartitionSpec as P

D = 8192
KVH = 8
HD = 128
ROLL = 16
ROWS = 8
GR = 4
QG = 16
DS = 512


def from_partner(value, axis, bit):
    mask = 2**bit
    pairs = [(source, source ^ mask) for source in range(lax.axis_size(axis))]
    return lax.ppermute(value, axis, pairs)


def xor_swap(value, axis, bit):
    return from_partner(value, axis, bit)


def gather_xor(value, axis):
    n = lax.axis_size(axis)
    me = lax.axis_index(axis)
    held = value
    for bit in range(n.bit_length() - 1):
        other = xor_swap(held, axis, bit)
        low = ((me >> bit) & 1) == 0
        held = jnp.where(low, jnp.concatenate([held, other], 0), jnp.concatenate([other, held], 0))
    return held


def scatter_rounds(held, order, axis, bits):
    me = lax.axis_index(axis)
    for bit in bits:
        pos = order.index(bit)
        order = order[:pos] + order[pos + 1 :]
        low = ((me >> bit) & 1) == 0
        first = lax.index_in_dim(held, 0, pos, keepdims=False)
        second = lax.index_in_dim(held, 1, pos, keepdims=False)
        keep = jnp.where(low, first, second)
        give = jnp.where(low, second, first)
        held = keep + xor_swap(give, axis, bit)
    return held, order


def scatter_sum_xor(pieces, axis):
    n = lax.axis_size(axis)
    bits = n.bit_length() - 1
    me = lax.axis_index(axis)
    held = pieces.reshape((2,) * bits + pieces.shape[1:])
    order = list(range(bits - 1, -1, -1))
    for bit in range(bits):
        pos = order.index(bit)
        order.pop(pos)
        low = ((me >> bit) & 1) == 0
        first = lax.index_in_dim(held, 0, pos, keepdims=False)
        second = lax.index_in_dim(held, 1, pos, keepdims=False)
        keep = jnp.where(low, first, second)
        give = jnp.where(low, second, first)
        held = keep + xor_swap(give, axis, bit)
    return held[None]


def pick(table, idx):
    hit = idx[:, None] == jnp.arange(table.shape[0], dtype=idx.dtype)[None, :]
    hit = hit.reshape(hit.shape + (1,) * (table.ndim - 1))
    return jnp.sum(jnp.where(hit, table[None], jnp.zeros((), table.dtype)), axis=1)


def gather_rounds(held, axis, bits):
    me = lax.axis_index(axis)
    for bit in bits:
        other = xor_swap(held, axis, bit)
        low = ((me >> bit) & 1) == 0
        held = jnp.where(low, jnp.concatenate([held, other], 0), jnp.concatenate([other, held], 0))
    return held


def exchange_rounds(held, axis, bits):
    me = lax.axis_index(axis)
    count = len(bits)
    for done, bit in enumerate(bits):
        low = ((me >> bit) & 1) == 0
        first = lax.index_in_dim(held, 0, 0, keepdims=False)
        second = lax.index_in_dim(held, 1, 0, keepdims=False)
        keep = jnp.where(low, first, second)
        give = jnp.where(low, second, first)
        got = xor_swap(give, axis, bit)
        at = count - done - 1 + done
        held = jnp.where(low, jnp.stack([keep, got], at), jnp.stack([got, keep], at))
    return held


def swap_rows(value, axis, col_bits, s):
    shift = s << col_bits
    return lax.ppermute(value, axis, [(t, t ^ shift) for t in range(lax.axis_size(axis))])


def swap_cols(value, axis, s):
    return lax.ppermute(value, axis, [(t, t ^ s) for t in range(lax.axis_size(axis))])


def norm_rows(rows_float, norm_gain):
    mean_square = jnp.mean(rows_float * rows_float, axis=-1, keepdims=True)
    return (rows_float * lax.rsqrt(mean_square + 1e-05) * norm_gain[None, :]).astype(jnp.bfloat16)


def local(
    hidden_in, norm_gain, q_blocks, o_blocks, kv_blocks, kv_assign, key_cache, value_cache, lengths
):
    ranks = lax.axis_size("tp")
    my_index = lax.axis_index("tp")
    my_rank = my_index % ROLL
    my_half = my_rank % 2
    grid_cols = ranks // GR
    group_count = ranks // ROLL
    col_width = q_blocks.shape[3]
    key_width = kv_blocks.shape[2]
    grid_row = my_index // grid_cols
    grid_col = my_index % grid_cols
    dest_ids = jnp.arange(ranks, dtype=jnp.int32)
    dest_rank = dest_ids % ROLL
    dest_head = kv_assign[dest_rank]
    dest_group = 2 * dest_head + dest_rank % 2
    dest_copy = dest_ids // ROLL
    bits = ranks.bit_length() - 1
    col_bits = grid_cols.bit_length() - 1
    row_bits = GR.bit_length() - 1
    row_order = jnp.arange(GR, dtype=jnp.int32) ^ grid_row
    col_order = jnp.arange(grid_cols, dtype=jnp.int32) ^ grid_col
    direct_cols = grid_cols <= 4
    direct_sums = False
    if direct_cols:
        from_cols = [hidden_in[0]] + [swap_cols(hidden_in[0], "tp", s) for s in range(1, grid_cols)]
        in_row = pick(jnp.stack(from_cols), col_order)
    else:
        in_row = gather_rounds(hidden_in, "tp", range(col_bits))
    from_rows = [in_row] + [swap_rows(in_row, "tp", col_bits, s) for s in range(1, GR)]
    every_rows = pick(jnp.stack(from_rows), row_order).reshape(ranks, ROWS, DS)
    rows_float = (
        every_rows.reshape(group_count, ROLL, ROWS, DS)
        .transpose(0, 2, 1, 3)
        .reshape(group_count * ROWS, D)
        .astype(jnp.float32)
    )
    normed_every = norm_rows(rows_float, norm_gain)
    col_rows = lax.dynamic_slice_in_dim(normed_every, grid_col * col_width, col_width, 1)
    query_part = jnp.einsum(
        "rc,aec->rae", col_rows, q_blocks[0], preferred_element_type=jnp.float32
    )
    query_part = (
        query_part.reshape(group_count, ROWS, QG, HD)
        .transpose(0, 2, 1, 3)
        .reshape(group_count * QG, ROWS, HD)
    )
    pair_first = dest_copy * QG + 2 * dest_head
    query_pick = jnp.concatenate([pick(query_part, pair_first), pick(query_part, pair_first + 1)], -1)
    key_rows = lax.dynamic_slice_in_dim(normed_every, my_index * key_width, key_width, 1)
    keyval_part = jnp.einsum("rc,kfc->rkf", key_rows, kv_blocks, preferred_element_type=jnp.float32)
    keyval_part = (
        keyval_part.reshape(group_count, ROWS, 2, KVH, HD)
        .transpose(0, 3, 1, 2, 4)
        .reshape(group_count * KVH, ROWS, 2 * HD)
    )
    keyval_term = pick(keyval_part, dest_copy * KVH + dest_head)
    width = 4 * HD
    compact = jnp.concatenate([query_pick, keyval_term], -1)
    if direct_sums:
        by_col = compact.reshape(GR, grid_cols, ROWS, width)
        held = lax.dynamic_index_in_dim(by_col, grid_col, 1, keepdims=False)
        for s in range(1, grid_cols):
            held = held + swap_cols(lax.dynamic_index_in_dim(by_col, grid_col ^ s, 1, keepdims=False), "tp", s)
    else:
        held, _ = scatter_rounds(
            compact.reshape((2,) * bits + (ROWS, width)), list(range(bits - 1, -1, -1)), "tp", range(col_bits)
        )
        held = held.reshape(GR, ROWS, width)
    from_rows = [lax.dynamic_index_in_dim(held, grid_row, 0, keepdims=False)]
    for s in range(1, GR):
        piece = lax.dynamic_index_in_dim(held, grid_row ^ s, 0, keepdims=False)
        from_rows.append(swap_rows(piece, "tp", col_bits, s))
    halves_q = [
        pick(jnp.stack([got[:, h * HD : (h + 1) * HD] for got in from_rows]), row_order) for h in range(2)
    ]
    both_queries = jnp.stack(halves_q).transpose(2, 0, 1, 3).reshape(ROWS, 2 * GR, HD).astype(jnp.bfloat16)
    keyval_sum = from_rows[0][:, 2 * HD :]
    for got in from_rows[1:]:
        keyval_sum = keyval_sum + got[:, 2 * HD :]
    keyval_new = keyval_sum.astype(jnp.bfloat16)
    key_new = keyval_new[:, :HD]
    value_new = keyval_new[:, HD:]
    scale = 1.0 / HD**0.5
    scores = (
        jnp.einsum("bhe,bte->bht", both_queries, key_cache[0], preferred_element_type=jnp.float32)
        * scale
    )
    positions = jnp.arange(scores.shape[2], dtype=jnp.int32)
    masked = positions[None, None, :] < lengths[0][:, None, None]
    new_score = (
        jnp.einsum("bhe,be->bh", both_queries, key_new, preferred_element_type=jnp.float32) * scale
    )
    new_score = jnp.where(my_half == 0, new_score, jnp.float32(-1e30))
    top = jnp.maximum(jnp.max(jnp.where(masked, scores, jnp.float32(-1e30)), axis=-1), new_score)
    weights = jnp.where(masked, jnp.exp(scores - top[..., None]), jnp.float32(0.0))
    new_weight = jnp.exp(new_score - top)
    total = jnp.sum(weights, axis=-1) + new_weight
    summed = jnp.einsum(
        "bht,bte->bhe",
        weights.astype(jnp.bfloat16),
        value_cache[0],
        preferred_element_type=jnp.float32,
    )
    new_rounded = lax.optimization_barrier(new_weight.astype(jnp.bfloat16)).astype(jnp.float32)
    summed = summed + new_rounded[..., None] * value_new.astype(jnp.float32)[:, None, :]
    top_split = top.reshape(ROWS, 2, GR)
    total_split = total.reshape(ROWS, 2, GR)
    summed_split = summed.reshape(ROWS, 2, GR, HD)
    first_half = my_half == 0
    own_top = jnp.where(first_half, top_split[:, 0], top_split[:, 1])
    own_total = jnp.where(first_half, total_split[:, 0], total_split[:, 1])
    own_summed = jnp.where(first_half, summed_split[:, 0], summed_split[:, 1])
    give_top = jnp.where(first_half, top_split[:, 1], top_split[:, 0])
    give_total = jnp.where(first_half, total_split[:, 1], total_split[:, 0])
    give_summed = jnp.where(first_half, summed_split[:, 1], summed_split[:, 0])
    give = jnp.concatenate([give_summed, give_top[..., None], give_total[..., None]], -1)
    got = from_partner(give, "tp", 0)
    got_summed, got_top, got_total = got[..., :HD], got[..., HD], got[..., HD + 1]
    joint = jnp.maximum(own_top, got_top)
    factor_own = jnp.exp(own_top - joint)
    factor_got = jnp.exp(got_top - joint)
    numer = own_summed * factor_own[..., None] + got_summed * factor_got[..., None]
    denom = own_total * factor_own + got_total * factor_got
    attention = (numer / denom[..., None]).astype(jnp.bfloat16)
    from_rows = [lax.dynamic_index_in_dim(attention, grid_row, 1, keepdims=False)]
    for s in range(1, GR):
        piece = lax.dynamic_index_in_dim(attention, grid_row ^ s, 1, keepdims=False)
        from_rows.append(swap_rows(piece, "tp", col_bits, s))
    by_row = pick(jnp.stack(from_rows), row_order)
    if direct_cols:
        from_cols = [by_row] + [swap_cols(by_row, "tp", s) for s in range(1, grid_cols)]
        every_slot = pick(jnp.stack(from_cols), col_order)
    else:
        every_slot = gather_rounds(by_row[None], "tp", range(col_bits))
    every_slot = every_slot.transpose(1, 0, 2, 3).reshape(group_count, ROLL, ROWS, HD)
    head_ids = jnp.arange(KVH, dtype=jnp.int32)
    pair_heads = kv_assign[0::2]
    inverse = jnp.sum(
        head_ids[None, :] * (pair_heads[None, :] == head_ids[:, None]).astype(jnp.int32), axis=1
    )
    slot_ids = jnp.arange(QG, dtype=jnp.int32)
    rank_of_slot = 2 * inverse[slot_ids // 2] + slot_ids % 2
    chosen = jax.vmap(lambda per_group: pick(per_group, rank_of_slot))(every_slot)
    out_part = jnp.einsum("gabe,cae->gbc", chosen, o_blocks[0], preferred_element_type=jnp.float32)
    if group_count == 1 and grid_cols == GR and col_width == GR * DS:
        pieces = out_part[0].reshape(ROWS, GR, DS)
        my_cols = None
        for s in range(GR):
            piece = lax.dynamic_index_in_dim(pieces, grid_row ^ s, 1, keepdims=False)
            pairs = [(i * grid_cols + j, j * grid_cols + (i ^ s)) for i in range(GR) for j in range(grid_cols)]
            got = lax.ppermute(piece, "tp", pairs)
            my_cols = got if my_cols is None else my_cols + got
    else:
        placed = jnp.zeros((group_count, ROWS, D), jnp.float32)
        placed = lax.dynamic_update_slice_in_dim(placed, out_part, grid_col * col_width, 2)
        out_term = (
            placed.reshape(group_count, ROWS, ROLL, DS).transpose(0, 2, 1, 3).reshape(ranks * ROWS, DS)
        )
        my_cols = scatter_sum_xor(out_term.reshape(ranks, ROWS, DS), "tp")[0]
    return my_cols.astype(jnp.bfloat16)[None]


def solution(mesh):
    return jax.shard_map(
        local,
        mesh=mesh,
        in_specs=(
            P(("groups", "tp"), None, None),
            P(),
            P("tp", None, None, None),
            P("tp", None, None, None),
            P(None, None, "tp"),
            P(),
            P(("groups", "tp"), None, None, None),
            P(("groups", "tp"), None, None, None),
            P(("groups", "tp"), None),
        ),
        out_specs=P(("groups", "tp"), None, None),
        check_vma=False,
    )
```

```python
import jax
import jax.numpy as jnp
from jax import lax
from jax.sharding import PartitionSpec as P

D = 8192
KVH = 8
HD = 128
ROLL = 16
ROWS = 8
GR = 4
QG = 16
DS = 512


def from_partner(value, axis, bit):
    mask = 2**bit
    pairs = [(source, source ^ mask) for source in range(lax.axis_size(axis))]
    return lax.ppermute(value, axis, pairs)


def xor_swap(value, axis, bit):
    return from_partner(value, axis, bit)


def gather_xor(value, axis):
    n = lax.axis_size(axis)
    me = lax.axis_index(axis)
    held = value
    for bit in range(n.bit_length() - 1):
        other = xor_swap(held, axis, bit)
        low = ((me >> bit) & 1) == 0
        held = jnp.where(low, jnp.concatenate([held, other], 0), jnp.concatenate([other, held], 0))
    return held


def scatter_rounds(held, order, axis, bits):
    me = lax.axis_index(axis)
    for bit in bits:
        pos = order.index(bit)
        order = order[:pos] + order[pos + 1 :]
        low = ((me >> bit) & 1) == 0
        first = lax.index_in_dim(held, 0, pos, keepdims=False)
        second = lax.index_in_dim(held, 1, pos, keepdims=False)
        keep = jnp.where(low, first, second)
        give = jnp.where(low, second, first)
        held = keep + xor_swap(give, axis, bit)
    return held, order


def scatter_sum_xor(pieces, axis):
    n = lax.axis_size(axis)
    bits = n.bit_length() - 1
    me = lax.axis_index(axis)
    held = pieces.reshape((2,) * bits + pieces.shape[1:])
    order = list(range(bits - 1, -1, -1))
    for bit in range(bits):
        pos = order.index(bit)
        order.pop(pos)
        low = ((me >> bit) & 1) == 0
        first = lax.index_in_dim(held, 0, pos, keepdims=False)
        second = lax.index_in_dim(held, 1, pos, keepdims=False)
        keep = jnp.where(low, first, second)
        give = jnp.where(low, second, first)
        held = keep + xor_swap(give, axis, bit)
    return held[None]


def pick(table, idx):
    hit = idx[:, None] == jnp.arange(table.shape[0], dtype=idx.dtype)[None, :]
    hit = hit.reshape(hit.shape + (1,) * (table.ndim - 1))
    return jnp.sum(jnp.where(hit, table[None], jnp.zeros((), table.dtype)), axis=1)


def gather_rounds(held, axis, bits):
    me = lax.axis_index(axis)
    for bit in bits:
        other = xor_swap(held, axis, bit)
        low = ((me >> bit) & 1) == 0
        held = jnp.where(low, jnp.concatenate([held, other], 0), jnp.concatenate([other, held], 0))
    return held


def exchange_rounds(held, axis, bits):
    me = lax.axis_index(axis)
    count = len(bits)
    for done, bit in enumerate(bits):
        low = ((me >> bit) & 1) == 0
        first = lax.index_in_dim(held, 0, 0, keepdims=False)
        second = lax.index_in_dim(held, 1, 0, keepdims=False)
        keep = jnp.where(low, first, second)
        give = jnp.where(low, second, first)
        got = xor_swap(give, axis, bit)
        at = count - done - 1 + done
        held = jnp.where(low, jnp.stack([keep, got], at), jnp.stack([got, keep], at))
    return held


def swap_rows(value, axis, col_bits, s):
    shift = s << col_bits
    return lax.ppermute(value, axis, [(t, t ^ shift) for t in range(lax.axis_size(axis))])


def swap_cols(value, axis, s):
    return lax.ppermute(value, axis, [(t, t ^ s) for t in range(lax.axis_size(axis))])


def norm_rows(rows_float, norm_gain):
    mean_square = jnp.mean(rows_float * rows_float, axis=-1, keepdims=True)
    return (rows_float * lax.rsqrt(mean_square + 1e-05) * norm_gain[None, :]).astype(jnp.bfloat16)


def local(
    hidden_in, norm_gain, q_blocks, o_blocks, kv_blocks, kv_assign, key_cache, value_cache, lengths
):
    ranks = lax.axis_size("tp")
    my_index = lax.axis_index("tp")
    my_rank = my_index % ROLL
    my_half = my_rank % 2
    grid_cols = ranks // GR
    group_count = ranks // ROLL
    col_width = q_blocks.shape[3]
    key_width = kv_blocks.shape[2]
    grid_row = my_index // grid_cols
    grid_col = my_index % grid_cols
    dest_ids = jnp.arange(ranks, dtype=jnp.int32)
    dest_rank = dest_ids % ROLL
    dest_head = kv_assign[dest_rank]
    dest_group = 2 * dest_head + dest_rank % 2
    dest_copy = dest_ids // ROLL
    bits = ranks.bit_length() - 1
    col_bits = grid_cols.bit_length() - 1
    row_bits = GR.bit_length() - 1
    row_order = jnp.arange(GR, dtype=jnp.int32) ^ grid_row
    col_order = jnp.arange(grid_cols, dtype=jnp.int32) ^ grid_col
    direct_cols = grid_cols <= 4
    if direct_cols:
        from_cols = [hidden_in[0]] + [swap_cols(hidden_in[0], "tp", s) for s in range(1, grid_cols)]
        in_row = pick(jnp.stack(from_cols), col_order)
    else:
        in_row = gather_rounds(hidden_in, "tp", range(col_bits))
    from_rows = [in_row] + [swap_rows(in_row, "tp", col_bits, s) for s in range(1, GR)]
    every_rows = pick(jnp.stack(from_rows), row_order).reshape(ranks, ROWS, DS)
    rows_float = (
        every_rows.reshape(group_count, ROLL, ROWS, DS)
        .transpose(0, 2, 1, 3)
        .reshape(group_count * ROWS, D)
        .astype(jnp.float32)
    )
    normed_every = norm_rows(rows_float, norm_gain)
    col_rows = lax.dynamic_slice_in_dim(normed_every, grid_col * col_width, col_width, 1)
    query_part = jnp.einsum(
        "rc,aec->rae", col_rows, q_blocks[0], preferred_element_type=jnp.float32
    )
    query_part = (
        query_part.reshape(group_count, ROWS, QG, HD)
        .transpose(0, 2, 1, 3)
        .reshape(group_count * QG, ROWS, HD)
    )
    pair_first = dest_copy * QG + 2 * dest_head
    query_pick = jnp.concatenate([pick(query_part, pair_first), pick(query_part, pair_first + 1)], -1)
    key_rows = lax.dynamic_slice_in_dim(normed_every, my_index * key_width, key_width, 1)
    keyval_part = jnp.einsum("rc,kfc->rkf", key_rows, kv_blocks, preferred_element_type=jnp.float32)
    keyval_part = (
        keyval_part.reshape(group_count, ROWS, 2, KVH, HD)
        .transpose(0, 3, 1, 2, 4)
        .reshape(group_count * KVH, ROWS, 2 * HD)
    )
    keyval_term = pick(keyval_part, dest_copy * KVH + dest_head)
    width = 4 * HD
    compact = jnp.concatenate([query_pick, keyval_term], -1)
    if direct_cols:
        by_col = compact.reshape(GR, grid_cols, ROWS, width)
        held = lax.dynamic_index_in_dim(by_col, grid_col, 1, keepdims=False)
        for s in range(1, grid_cols):
            held = held + swap_cols(lax.dynamic_index_in_dim(by_col, grid_col ^ s, 1, keepdims=False), "tp", s)
    else:
        held, _ = scatter_rounds(
            compact.reshape((2,) * bits + (ROWS, width)), list(range(bits - 1, -1, -1)), "tp", range(col_bits)
        )
        held = held.reshape(GR, ROWS, width)
    from_rows = [lax.dynamic_index_in_dim(held, grid_row, 0, keepdims=False)]
    for s in range(1, GR):
        piece = lax.dynamic_index_in_dim(held, grid_row ^ s, 0, keepdims=False)
        from_rows.append(swap_rows(piece, "tp", col_bits, s))
    halves_q = [
        pick(jnp.stack([got[:, h * HD : (h + 1) * HD] for got in from_rows]), row_order) for h in range(2)
    ]
    both_queries = jnp.stack(halves_q).transpose(2, 0, 1, 3).reshape(ROWS, 2 * GR, HD).astype(jnp.bfloat16)
    keyval_sum = from_rows[0][:, 2 * HD :]
    for got in from_rows[1:]:
        keyval_sum = keyval_sum + got[:, 2 * HD :]
    keyval_new = keyval_sum.astype(jnp.bfloat16)
    key_new = keyval_new[:, :HD]
    value_new = keyval_new[:, HD:]
    def attend(lo, hi):
        queries_c, keys_c, values_c = both_queries[lo:hi], key_cache[0, lo:hi], value_cache[0, lo:hi]
        lengths_c, key_new_c, value_new_c = lengths[0, lo:hi], key_new[lo:hi], value_new[lo:hi]
        scale = 1.0 / HD**0.5
        scores = (
            jnp.einsum("bhe,bte->bht", queries_c, keys_c, preferred_element_type=jnp.float32)
            * scale
        )
        positions = jnp.arange(scores.shape[2], dtype=jnp.int32)
        masked = positions[None, None, :] < lengths_c[:, None, None]
        new_score = (
            jnp.einsum("bhe,be->bh", queries_c, key_new_c, preferred_element_type=jnp.float32) * scale
        )
        new_score = jnp.where(my_half == 0, new_score, jnp.float32(-1e30))
        top = jnp.maximum(jnp.max(jnp.where(masked, scores, jnp.float32(-1e30)), axis=-1), new_score)
        weights = jnp.where(masked, jnp.exp(scores - top[..., None]), jnp.float32(0.0))
        new_weight = jnp.exp(new_score - top)
        total = jnp.sum(weights, axis=-1) + new_weight
        summed = jnp.einsum(
            "bht,bte->bhe",
            weights.astype(jnp.bfloat16),
            values_c,
            preferred_element_type=jnp.float32,
        )
        new_rounded = lax.optimization_barrier(new_weight.astype(jnp.bfloat16)).astype(jnp.float32)
        summed = summed + new_rounded[..., None] * value_new_c.astype(jnp.float32)[:, None, :]
        top_split = top.reshape(-1, 2, GR)
        total_split = total.reshape(-1, 2, GR)
        summed_split = summed.reshape(-1, 2, GR, HD)
        first_half = my_half == 0
        own_top = jnp.where(first_half, top_split[:, 0], top_split[:, 1])
        own_total = jnp.where(first_half, total_split[:, 0], total_split[:, 1])
        own_summed = jnp.where(first_half, summed_split[:, 0], summed_split[:, 1])
        give_top = jnp.where(first_half, top_split[:, 1], top_split[:, 0])
        give_total = jnp.where(first_half, total_split[:, 1], total_split[:, 0])
        give_summed = jnp.where(first_half, summed_split[:, 1], summed_split[:, 0])
        give = jnp.concatenate([give_summed, give_top[..., None], give_total[..., None]], -1)
        got = from_partner(give, "tp", 0)
        got_summed, got_top, got_total = got[..., :HD], got[..., HD], got[..., HD + 1]
        joint = jnp.maximum(own_top, got_top)
        factor_own = jnp.exp(own_top - joint)
        factor_got = jnp.exp(got_top - joint)
        numer = own_summed * factor_own[..., None] + got_summed * factor_got[..., None]
        denom = own_total * factor_own + got_total * factor_got
        return (numer / denom[..., None]).astype(jnp.bfloat16)

    attention = jnp.concatenate([attend(0, ROWS // 2), attend(ROWS // 2, ROWS)], 0)
    from_rows = [lax.dynamic_index_in_dim(attention, grid_row, 1, keepdims=False)]
    for s in range(1, GR):
        piece = lax.dynamic_index_in_dim(attention, grid_row ^ s, 1, keepdims=False)
        from_rows.append(swap_rows(piece, "tp", col_bits, s))
    by_row = pick(jnp.stack(from_rows), row_order)
    if direct_cols:
        from_cols = [by_row] + [swap_cols(by_row, "tp", s) for s in range(1, grid_cols)]
        every_slot = pick(jnp.stack(from_cols), col_order)
    else:
        every_slot = gather_rounds(by_row[None], "tp", range(col_bits))
    every_slot = every_slot.transpose(1, 0, 2, 3).reshape(group_count, ROLL, ROWS, HD)
    head_ids = jnp.arange(KVH, dtype=jnp.int32)
    pair_heads = kv_assign[0::2]
    inverse = jnp.sum(
        head_ids[None, :] * (pair_heads[None, :] == head_ids[:, None]).astype(jnp.int32), axis=1
    )
    slot_ids = jnp.arange(QG, dtype=jnp.int32)
    rank_of_slot = 2 * inverse[slot_ids // 2] + slot_ids % 2
    chosen = jax.vmap(lambda per_group: pick(per_group, rank_of_slot))(every_slot)
    out_part = jnp.einsum("gabe,cae->gbc", chosen, o_blocks[0], preferred_element_type=jnp.float32)
    if group_count == 1 and grid_cols == GR and col_width == GR * DS:
        pieces = out_part[0].reshape(ROWS, GR, DS)
        my_cols = None
        for s in range(GR):
            piece = lax.dynamic_index_in_dim(pieces, grid_row ^ s, 1, keepdims=False)
            pairs = [(i * grid_cols + j, j * grid_cols + (i ^ s)) for i in range(GR) for j in range(grid_cols)]
            got = lax.ppermute(piece, "tp", pairs)
            my_cols = got if my_cols is None else my_cols + got
    else:
        placed = jnp.zeros((group_count, ROWS, D), jnp.float32)
        placed = lax.dynamic_update_slice_in_dim(placed, out_part, grid_col * col_width, 2)
        out_term = (
            placed.reshape(group_count, ROWS, ROLL, DS).transpose(0, 2, 1, 3).reshape(ranks * ROWS, DS)
        )
        my_cols = scatter_sum_xor(out_term.reshape(ranks, ROWS, DS), "tp")[0]
    return my_cols.astype(jnp.bfloat16)[None]


def solution(mesh):
    return jax.shard_map(
        local,
        mesh=mesh,
        in_specs=(
            P(("groups", "tp"), None, None),
            P(),
            P("tp", None, None, None),
            P("tp", None, None, None),
            P(None, None, "tp"),
            P(),
            P(("groups", "tp"), None, None, None),
            P(("groups", "tp"), None, None, None),
            P(("groups", "tp"), None),
        ),
        out_specs=P(("groups", "tp"), None, None),
        check_vma=False,
    )
```

```python
import jax
import jax.numpy as jnp
from jax import lax
from jax.sharding import PartitionSpec as P

D = 8192
KVH = 8
HD = 128
ROLL = 16
ROWS = 8
GR = 4
QG = 16
DS = 512


def from_partner(value, axis, bit):
    mask = 2**bit
    pairs = [(source, source ^ mask) for source in range(lax.axis_size(axis))]
    return lax.ppermute(value, axis, pairs)


def xor_swap(value, axis, bit):
    return from_partner(value, axis, bit)


def gather_xor(value, axis):
    n = lax.axis_size(axis)
    me = lax.axis_index(axis)
    held = value
    for bit in range(n.bit_length() - 1):
        other = xor_swap(held, axis, bit)
        low = ((me >> bit) & 1) == 0
        held = jnp.where(low, jnp.concatenate([held, other], 0), jnp.concatenate([other, held], 0))
    return held


def scatter_rounds(held, order, axis, bits):
    me = lax.axis_index(axis)
    for bit in bits:
        pos = order.index(bit)
        order = order[:pos] + order[pos + 1 :]
        low = ((me >> bit) & 1) == 0
        first = lax.index_in_dim(held, 0, pos, keepdims=False)
        second = lax.index_in_dim(held, 1, pos, keepdims=False)
        keep = jnp.where(low, first, second)
        give = jnp.where(low, second, first)
        held = keep + xor_swap(give, axis, bit)
    return held, order


def scatter_sum_xor(pieces, axis):
    n = lax.axis_size(axis)
    bits = n.bit_length() - 1
    me = lax.axis_index(axis)
    held = pieces.reshape((2,) * bits + pieces.shape[1:])
    order = list(range(bits - 1, -1, -1))
    for bit in range(bits):
        pos = order.index(bit)
        order.pop(pos)
        low = ((me >> bit) & 1) == 0
        first = lax.index_in_dim(held, 0, pos, keepdims=False)
        second = lax.index_in_dim(held, 1, pos, keepdims=False)
        keep = jnp.where(low, first, second)
        give = jnp.where(low, second, first)
        held = keep + xor_swap(give, axis, bit)
    return held[None]


def pick(table, idx):
    hit = idx[:, None] == jnp.arange(table.shape[0], dtype=idx.dtype)[None, :]
    hit = hit.reshape(hit.shape + (1,) * (table.ndim - 1))
    return jnp.sum(jnp.where(hit, table[None], jnp.zeros((), table.dtype)), axis=1)


def gather_rounds(held, axis, bits):
    me = lax.axis_index(axis)
    for bit in bits:
        other = xor_swap(held, axis, bit)
        low = ((me >> bit) & 1) == 0
        held = jnp.where(low, jnp.concatenate([held, other], 0), jnp.concatenate([other, held], 0))
    return held


def exchange_rounds(held, axis, bits):
    me = lax.axis_index(axis)
    count = len(bits)
    for done, bit in enumerate(bits):
        low = ((me >> bit) & 1) == 0
        first = lax.index_in_dim(held, 0, 0, keepdims=False)
        second = lax.index_in_dim(held, 1, 0, keepdims=False)
        keep = jnp.where(low, first, second)
        give = jnp.where(low, second, first)
        got = xor_swap(give, axis, bit)
        at = count - done - 1 + done
        held = jnp.where(low, jnp.stack([keep, got], at), jnp.stack([got, keep], at))
    return held


def swap_rows(value, axis, col_bits, s):
    shift = s << col_bits
    return lax.ppermute(value, axis, [(t, t ^ shift) for t in range(lax.axis_size(axis))])


def swap_cols(value, axis, s):
    return lax.ppermute(value, axis, [(t, t ^ s) for t in range(lax.axis_size(axis))])


def norm_rows(rows_float, norm_gain):
    mean_square = jnp.mean(rows_float * rows_float, axis=-1, keepdims=True)
    return (rows_float * lax.rsqrt(mean_square + 1e-05) * norm_gain[None, :]).astype(jnp.bfloat16)


def local(
    hidden_in, norm_gain, q_blocks, o_blocks, kv_blocks, kv_assign, key_cache, value_cache, lengths
):
    ranks = lax.axis_size("tp")
    my_index = lax.axis_index("tp")
    my_rank = my_index % ROLL
    my_half = my_rank % 2
    grid_cols = ranks // GR
    group_count = ranks // ROLL
    col_width = q_blocks.shape[3]
    key_width = kv_blocks.shape[2]
    grid_row = my_index // grid_cols
    grid_col = my_index % grid_cols
    dest_ids = jnp.arange(ranks, dtype=jnp.int32)
    dest_rank = dest_ids % ROLL
    dest_head = kv_assign[dest_rank]
    dest_group = 2 * dest_head + dest_rank % 2
    dest_copy = dest_ids // ROLL
    bits = ranks.bit_length() - 1
    col_bits = grid_cols.bit_length() - 1
    row_bits = GR.bit_length() - 1
    row_order = jnp.arange(GR, dtype=jnp.int32) ^ grid_row
    col_order = jnp.arange(grid_cols, dtype=jnp.int32) ^ grid_col
    direct_cols = grid_cols <= 4
    if direct_cols:
        from_rows = [hidden_in[0]] + [swap_rows(hidden_in[0], "tp", col_bits, s) for s in range(1, GR)]
        by_rows = pick(jnp.stack(from_rows), row_order)
        from_cols = [by_rows] + [swap_cols(by_rows, "tp", s) for s in range(1, grid_cols)]
        every_rows = pick(jnp.stack(from_cols), col_order).transpose(1, 0, 2, 3).reshape(ranks, ROWS, DS)
    else:
        in_row = gather_rounds(hidden_in, "tp", range(col_bits))
        from_rows = [in_row] + [swap_rows(in_row, "tp", col_bits, s) for s in range(1, GR)]
        every_rows = pick(jnp.stack(from_rows), row_order).reshape(ranks, ROWS, DS)
    rows_float = (
        every_rows.reshape(group_count, ROLL, ROWS, DS)
        .transpose(0, 2, 1, 3)
        .reshape(group_count * ROWS, D)
        .astype(jnp.float32)
    )
    normed_every = norm_rows(rows_float, norm_gain)
    col_rows = lax.dynamic_slice_in_dim(normed_every, grid_col * col_width, col_width, 1)
    query_part = jnp.einsum(
        "rc,aec->rae", col_rows, q_blocks[0], preferred_element_type=jnp.float32
    )
    query_part = (
        query_part.reshape(group_count, ROWS, QG, HD)
        .transpose(0, 2, 1, 3)
        .reshape(group_count * QG, ROWS, HD)
    )
    pair_first = dest_copy * QG + 2 * dest_head
    query_pick = jnp.concatenate([pick(query_part, pair_first), pick(query_part, pair_first + 1)], -1)
    key_rows = lax.dynamic_slice_in_dim(normed_every, my_index * key_width, key_width, 1)
    keyval_part = jnp.einsum("rc,kfc->rkf", key_rows, kv_blocks, preferred_element_type=jnp.float32)
    keyval_part = (
        keyval_part.reshape(group_count, ROWS, 2, KVH, HD)
        .transpose(0, 3, 1, 2, 4)
        .reshape(group_count * KVH, ROWS, 2 * HD)
    )
    keyval_term = pick(keyval_part, dest_copy * KVH + dest_head)
    width = 4 * HD
    compact = jnp.concatenate([query_pick, keyval_term], -1)
    if direct_cols:
        by_col = compact.reshape(GR, grid_cols, ROWS, width)
        held = lax.dynamic_index_in_dim(by_col, grid_col, 1, keepdims=False)
        for s in range(1, grid_cols):
            held = held + swap_cols(lax.dynamic_index_in_dim(by_col, grid_col ^ s, 1, keepdims=False), "tp", s)
    else:
        held, _ = scatter_rounds(
            compact.reshape((2,) * bits + (ROWS, width)), list(range(bits - 1, -1, -1)), "tp", range(col_bits)
        )
        held = held.reshape(GR, ROWS, width)
    from_rows = [lax.dynamic_index_in_dim(held, grid_row, 0, keepdims=False)]
    for s in range(1, GR):
        piece = lax.dynamic_index_in_dim(held, grid_row ^ s, 0, keepdims=False)
        from_rows.append(swap_rows(piece, "tp", col_bits, s))
    halves_q = [
        pick(jnp.stack([got[:, h * HD : (h + 1) * HD] for got in from_rows]), row_order) for h in range(2)
    ]
    both_queries = jnp.stack(halves_q).transpose(2, 0, 1, 3).reshape(ROWS, 2 * GR, HD).astype(jnp.bfloat16)
    keyval_sum = from_rows[0][:, 2 * HD :]
    for got in from_rows[1:]:
        keyval_sum = keyval_sum + got[:, 2 * HD :]
    keyval_new = keyval_sum.astype(jnp.bfloat16)
    key_new = keyval_new[:, :HD]
    value_new = keyval_new[:, HD:]
    scale = 1.0 / HD**0.5
    scores = (
        jnp.einsum("bhe,bte->bht", both_queries, key_cache[0], preferred_element_type=jnp.float32)
        * scale
    )
    positions = jnp.arange(scores.shape[2], dtype=jnp.int32)
    masked = positions[None, None, :] < lengths[0][:, None, None]
    new_score = (
        jnp.einsum("bhe,be->bh", both_queries, key_new, preferred_element_type=jnp.float32) * scale
    )
    new_score = jnp.where(my_half == 0, new_score, jnp.float32(-1e30))
    top = jnp.maximum(jnp.max(jnp.where(masked, scores, jnp.float32(-1e30)), axis=-1), new_score)
    weights = jnp.where(masked, jnp.exp(scores - top[..., None]), jnp.float32(0.0))
    new_weight = jnp.exp(new_score - top)
    total = jnp.sum(weights, axis=-1) + new_weight
    summed = jnp.einsum(
        "bht,bte->bhe",
        weights.astype(jnp.bfloat16),
        value_cache[0],
        preferred_element_type=jnp.float32,
    )
    new_rounded = lax.optimization_barrier(new_weight.astype(jnp.bfloat16)).astype(jnp.float32)
    summed = summed + new_rounded[..., None] * value_new.astype(jnp.float32)[:, None, :]
    top_split = top.reshape(ROWS, 2, GR)
    total_split = total.reshape(ROWS, 2, GR)
    summed_split = summed.reshape(ROWS, 2, GR, HD)
    first_half = my_half == 0
    own_top = jnp.where(first_half, top_split[:, 0], top_split[:, 1])
    own_total = jnp.where(first_half, total_split[:, 0], total_split[:, 1])
    own_summed = jnp.where(first_half, summed_split[:, 0], summed_split[:, 1])
    give_top = jnp.where(first_half, top_split[:, 1], top_split[:, 0])
    give_total = jnp.where(first_half, total_split[:, 1], total_split[:, 0])
    give_summed = jnp.where(first_half, summed_split[:, 1], summed_split[:, 0])
    give = jnp.concatenate([give_summed, give_top[..., None], give_total[..., None]], -1)
    got = from_partner(give, "tp", 0)
    got_summed, got_top, got_total = got[..., :HD], got[..., HD], got[..., HD + 1]
    joint = jnp.maximum(own_top, got_top)
    factor_own = jnp.exp(own_top - joint)
    factor_got = jnp.exp(got_top - joint)
    numer = own_summed * factor_own[..., None] + got_summed * factor_got[..., None]
    denom = own_total * factor_own + got_total * factor_got
    attention = (numer / denom[..., None]).astype(jnp.bfloat16)
    from_rows = [lax.dynamic_index_in_dim(attention, grid_row, 1, keepdims=False)]
    for s in range(1, GR):
        piece = lax.dynamic_index_in_dim(attention, grid_row ^ s, 1, keepdims=False)
        from_rows.append(swap_rows(piece, "tp", col_bits, s))
    by_row = pick(jnp.stack(from_rows), row_order)
    if direct_cols:
        from_cols = [by_row] + [swap_cols(by_row, "tp", s) for s in range(1, grid_cols)]
        every_slot = pick(jnp.stack(from_cols), col_order)
    else:
        every_slot = gather_rounds(by_row[None], "tp", range(col_bits))
    every_slot = every_slot.transpose(1, 0, 2, 3).reshape(group_count, ROLL, ROWS, HD)
    head_ids = jnp.arange(KVH, dtype=jnp.int32)
    pair_heads = kv_assign[0::2]
    inverse = jnp.sum(
        head_ids[None, :] * (pair_heads[None, :] == head_ids[:, None]).astype(jnp.int32), axis=1
    )
    slot_ids = jnp.arange(QG, dtype=jnp.int32)
    rank_of_slot = 2 * inverse[slot_ids // 2] + slot_ids % 2
    chosen = jax.vmap(lambda per_group: pick(per_group, rank_of_slot))(every_slot)
    out_part = jnp.einsum("gabe,cae->gbc", chosen, o_blocks[0], preferred_element_type=jnp.float32)
    if group_count == 1 and grid_cols == GR and col_width == GR * DS:
        pieces = out_part[0].reshape(ROWS, GR, DS)
        my_cols = None
        for s in range(GR):
            piece = lax.dynamic_index_in_dim(pieces, grid_row ^ s, 1, keepdims=False)
            pairs = [(i * grid_cols + j, j * grid_cols + (i ^ s)) for i in range(GR) for j in range(grid_cols)]
            got = lax.ppermute(piece, "tp", pairs)
            my_cols = got if my_cols is None else my_cols + got
    else:
        placed = jnp.zeros((group_count, ROWS, D), jnp.float32)
        placed = lax.dynamic_update_slice_in_dim(placed, out_part, grid_col * col_width, 2)
        out_term = (
            placed.reshape(group_count, ROWS, ROLL, DS).transpose(0, 2, 1, 3).reshape(ranks * ROWS, DS)
        )
        my_cols = scatter_sum_xor(out_term.reshape(ranks, ROWS, DS), "tp")[0]
    return my_cols.astype(jnp.bfloat16)[None]


def solution(mesh):
    return jax.shard_map(
        local,
        mesh=mesh,
        in_specs=(
            P(("groups", "tp"), None, None),
            P(),
            P("tp", None, None, None),
            P("tp", None, None, None),
            P(None, None, "tp"),
            P(),
            P(("groups", "tp"), None, None, None),
            P(("groups", "tp"), None, None, None),
            P(("groups", "tp"), None),
        ),
        out_specs=P(("groups", "tp"), None, None),
        check_vma=False,
    )
```

```python
import jax
import jax.numpy as jnp
from jax import lax
from jax.sharding import PartitionSpec as P

D = 8192
KVH = 8
HD = 128
ROLL = 16
ROWS = 8
GR = 4
QG = 16
DS = 512


def from_partner(value, axis, bit):
    mask = 2**bit
    pairs = [(source, source ^ mask) for source in range(lax.axis_size(axis))]
    return lax.ppermute(value, axis, pairs)


def xor_swap(value, axis, bit):
    return from_partner(value, axis, bit)


def gather_xor(value, axis):
    n = lax.axis_size(axis)
    me = lax.axis_index(axis)
    held = value
    for bit in range(n.bit_length() - 1):
        other = xor_swap(held, axis, bit)
        low = ((me >> bit) & 1) == 0
        held = jnp.where(low, jnp.concatenate([held, other], 0), jnp.concatenate([other, held], 0))
    return held


def scatter_rounds(held, order, axis, bits):
    me = lax.axis_index(axis)
    for bit in bits:
        pos = order.index(bit)
        order = order[:pos] + order[pos + 1 :]
        low = ((me >> bit) & 1) == 0
        first = lax.index_in_dim(held, 0, pos, keepdims=False)
        second = lax.index_in_dim(held, 1, pos, keepdims=False)
        keep = jnp.where(low, first, second)
        give = jnp.where(low, second, first)
        held = keep + xor_swap(give, axis, bit)
    return held, order


def scatter_sum_xor(pieces, axis):
    n = lax.axis_size(axis)
    bits = n.bit_length() - 1
    me = lax.axis_index(axis)
    held = pieces.reshape((2,) * bits + pieces.shape[1:])
    order = list(range(bits - 1, -1, -1))
    for bit in range(bits):
        pos = order.index(bit)
        order.pop(pos)
        low = ((me >> bit) & 1) == 0
        first = lax.index_in_dim(held, 0, pos, keepdims=False)
        second = lax.index_in_dim(held, 1, pos, keepdims=False)
        keep = jnp.where(low, first, second)
        give = jnp.where(low, second, first)
        held = keep + xor_swap(give, axis, bit)
    return held[None]


def pick(table, idx):
    hit = idx[:, None] == jnp.arange(table.shape[0], dtype=idx.dtype)[None, :]
    hit = hit.reshape(hit.shape + (1,) * (table.ndim - 1))
    return jnp.sum(jnp.where(hit, table[None], jnp.zeros((), table.dtype)), axis=1)


def gather_rounds(held, axis, bits):
    me = lax.axis_index(axis)
    for bit in bits:
        other = xor_swap(held, axis, bit)
        low = ((me >> bit) & 1) == 0
        held = jnp.where(low, jnp.concatenate([held, other], 0), jnp.concatenate([other, held], 0))
    return held


def exchange_rounds(held, axis, bits):
    me = lax.axis_index(axis)
    count = len(bits)
    for done, bit in enumerate(bits):
        low = ((me >> bit) & 1) == 0
        first = lax.index_in_dim(held, 0, 0, keepdims=False)
        second = lax.index_in_dim(held, 1, 0, keepdims=False)
        keep = jnp.where(low, first, second)
        give = jnp.where(low, second, first)
        got = xor_swap(give, axis, bit)
        at = count - done - 1 + done
        held = jnp.where(low, jnp.stack([keep, got], at), jnp.stack([got, keep], at))
    return held


def swap_rows(value, axis, col_bits, s):
    shift = s << col_bits
    return lax.ppermute(value, axis, [(t, t ^ shift) for t in range(lax.axis_size(axis))])


def swap_cols(value, axis, s):
    return lax.ppermute(value, axis, [(t, t ^ s) for t in range(lax.axis_size(axis))])


def norm_rows(rows_float, norm_gain):
    mean_square = jnp.mean(rows_float * rows_float, axis=-1, keepdims=True)
    return (rows_float * lax.rsqrt(mean_square + 1e-05) * norm_gain[None, :]).astype(jnp.bfloat16)


def local(
    hidden_in, norm_gain, q_blocks, o_blocks, kv_blocks, kv_assign, key_cache, value_cache, lengths
):
    ranks = lax.axis_size("tp")
    my_index = lax.axis_index("tp")
    my_rank = my_index % ROLL
    my_half = my_rank % 2
    grid_cols = ranks // GR
    group_count = ranks // ROLL
    col_width = q_blocks.shape[3]
    key_width = kv_blocks.shape[2]
    grid_row = my_index // grid_cols
    grid_col = my_index % grid_cols
    dest_ids = jnp.arange(ranks, dtype=jnp.int32)
    dest_rank = dest_ids % ROLL
    dest_head = kv_assign[dest_rank]
    dest_group = 2 * dest_head + dest_rank % 2
    dest_copy = dest_ids // ROLL
    bits = ranks.bit_length() - 1
    col_bits = grid_cols.bit_length() - 1
    row_bits = GR.bit_length() - 1
    row_order = jnp.arange(GR, dtype=jnp.int32) ^ grid_row
    col_order = jnp.arange(grid_cols, dtype=jnp.int32) ^ grid_col
    direct_cols = grid_cols <= 4
    if direct_cols:
        from_cols = [hidden_in[0]] + [swap_cols(hidden_in[0], "tp", s) for s in range(1, grid_cols)]
        in_row = pick(jnp.stack(from_cols), col_order)
    else:
        in_row = gather_rounds(hidden_in, "tp", range(col_bits))
    from_rows = [in_row] + [swap_rows(in_row, "tp", col_bits, s) for s in range(1, GR)]
    every_rows = pick(jnp.stack(from_rows), row_order).reshape(ranks, ROWS, DS)
    rows_float = (
        every_rows.reshape(group_count, ROLL, ROWS, DS)
        .transpose(0, 2, 1, 3)
        .reshape(group_count * ROWS, D)
        .astype(jnp.float32)
    )
    normed_every = norm_rows(rows_float, norm_gain)
    col_rows = lax.dynamic_slice_in_dim(normed_every, grid_col * col_width, col_width, 1)
    query_part = jnp.einsum(
        "rc,aec->rae", col_rows, q_blocks[0], preferred_element_type=jnp.float32
    )
    query_part = (
        query_part.reshape(group_count, ROWS, QG, HD)
        .transpose(0, 2, 1, 3)
        .reshape(group_count * QG, ROWS, HD)
    )
    pair_first = dest_copy * QG + 2 * dest_head
    query_pick = jnp.concatenate([pick(query_part, pair_first), pick(query_part, pair_first + 1)], -1)
    key_rows = lax.dynamic_slice_in_dim(normed_every, my_index * key_width, key_width, 1)
    keyval_part = jnp.einsum("rc,kfc->rkf", key_rows, kv_blocks, preferred_element_type=jnp.float32)
    keyval_part = (
        keyval_part.reshape(group_count, ROWS, 2, KVH, HD)
        .transpose(0, 3, 1, 2, 4)
        .reshape(group_count * KVH, ROWS, 2 * HD)
    )
    keyval_term = pick(keyval_part, dest_copy * KVH + dest_head)
    width = 4 * HD
    compact = jnp.concatenate([query_pick, keyval_term], -1)
    if direct_cols:
        by_col = compact.reshape(GR, grid_cols, ROWS, width)
        held = lax.dynamic_index_in_dim(by_col, grid_col, 1, keepdims=False)
        for s in range(1, grid_cols):
            held = held + swap_cols(lax.dynamic_index_in_dim(by_col, grid_col ^ s, 1, keepdims=False), "tp", s)
    else:
        held, _ = scatter_rounds(
            compact.reshape((2,) * bits + (ROWS, width)), list(range(bits - 1, -1, -1)), "tp", range(col_bits)
        )
        held = held.reshape(GR, ROWS, width)
    from_rows = [lax.dynamic_index_in_dim(held, grid_row, 0, keepdims=False)]
    for s in range(1, GR):
        piece = lax.dynamic_index_in_dim(held, grid_row ^ s, 0, keepdims=False)
        from_rows.append(swap_rows(piece, "tp", col_bits, s))
    halves_q = [
        pick(jnp.stack([got[:, h * HD : (h + 1) * HD] for got in from_rows]), row_order) for h in range(2)
    ]
    both_queries = jnp.stack(halves_q).transpose(2, 0, 1, 3).reshape(ROWS, 2 * GR, HD).astype(jnp.bfloat16)
    keyval_sum = from_rows[0][:, 2 * HD :]
    for got in from_rows[1:]:
        keyval_sum = keyval_sum + got[:, 2 * HD :]
    keyval_new = keyval_sum.astype(jnp.bfloat16)
    key_new = keyval_new[:, :HD]
    value_new = keyval_new[:, HD:]
    scale = 1.0 / HD**0.5
    scores = (
        jnp.einsum("bhe,bte->bht", both_queries, key_cache[0], preferred_element_type=jnp.float32)
        * scale
    )
    positions = jnp.arange(scores.shape[2], dtype=jnp.int32)
    masked = positions[None, None, :] < lengths[0][:, None, None]
    new_score = (
        jnp.einsum("bhe,be->bh", both_queries, key_new, preferred_element_type=jnp.float32) * scale
    )
    new_score = jnp.where(my_half == 0, new_score, jnp.float32(-1e30))
    top = jnp.maximum(jnp.max(jnp.where(masked, scores, jnp.float32(-1e30)), axis=-1), new_score)
    weights = jnp.where(masked, jnp.exp(scores - top[..., None]), jnp.float32(0.0))
    new_weight = jnp.exp(new_score - top)
    total = jnp.sum(weights, axis=-1) + new_weight
    summed = jnp.einsum(
        "bht,bte->bhe",
        weights.astype(jnp.bfloat16),
        value_cache[0],
        preferred_element_type=jnp.float32,
    )
    new_rounded = lax.optimization_barrier(new_weight.astype(jnp.bfloat16)).astype(jnp.float32)
    summed = summed + new_rounded[..., None] * value_new.astype(jnp.float32)[:, None, :]
    top_split = top.reshape(ROWS, 2, GR)
    total_split = total.reshape(ROWS, 2, GR)
    summed_split = summed.reshape(ROWS, 2, GR, HD)
    first_half = my_half == 0
    own_top = jnp.where(first_half, top_split[:, 0], top_split[:, 1])
    own_total = jnp.where(first_half, total_split[:, 0], total_split[:, 1])
    own_summed = jnp.where(first_half, summed_split[:, 0], summed_split[:, 1])
    give_top = jnp.where(first_half, top_split[:, 1], top_split[:, 0])
    give_total = jnp.where(first_half, total_split[:, 1], total_split[:, 0])
    give_summed = jnp.where(first_half, summed_split[:, 1], summed_split[:, 0])
    give = jnp.concatenate([give_summed, give_top[..., None], give_total[..., None]], -1)
    got = from_partner(give, "tp", 0)
    got_summed, got_top, got_total = got[..., :HD], got[..., HD], got[..., HD + 1]
    joint = jnp.maximum(own_top, got_top)
    factor_own = jnp.exp(own_top - joint)
    factor_got = jnp.exp(got_top - joint)
    numer = own_summed * factor_own[..., None] + got_summed * factor_got[..., None]
    denom = own_total * factor_own + got_total * factor_got
    attention = (numer / denom[..., None]).astype(jnp.bfloat16)
    if direct_cols:
        from_cols = [attention] + [swap_cols(attention, "tp", s) for s in range(1, grid_cols)]
        in_row_attn = pick(jnp.stack(from_cols), col_order)
        from_rows = [lax.dynamic_index_in_dim(in_row_attn, grid_row, 2, keepdims=False)]
        for s in range(1, GR):
            piece = lax.dynamic_index_in_dim(in_row_attn, grid_row ^ s, 2, keepdims=False)
            from_rows.append(swap_rows(piece, "tp", col_bits, s))
        every_slot = pick(jnp.stack(from_rows), row_order).reshape(group_count, ROLL, ROWS, HD)
    else:
        from_rows = [lax.dynamic_index_in_dim(attention, grid_row, 1, keepdims=False)]
        for s in range(1, GR):
            piece = lax.dynamic_index_in_dim(attention, grid_row ^ s, 1, keepdims=False)
            from_rows.append(swap_rows(piece, "tp", col_bits, s))
        by_row = pick(jnp.stack(from_rows), row_order)
        every_slot = gather_rounds(by_row[None], "tp", range(col_bits))
        every_slot = every_slot.transpose(1, 0, 2, 3).reshape(group_count, ROLL, ROWS, HD)
    head_ids = jnp.arange(KVH, dtype=jnp.int32)
    pair_heads = kv_assign[0::2]
    inverse = jnp.sum(
        head_ids[None, :] * (pair_heads[None, :] == head_ids[:, None]).astype(jnp.int32), axis=1
    )
    slot_ids = jnp.arange(QG, dtype=jnp.int32)
    rank_of_slot = 2 * inverse[slot_ids // 2] + slot_ids % 2
    chosen = jax.vmap(lambda per_group: pick(per_group, rank_of_slot))(every_slot)
    out_part = jnp.einsum("gabe,cae->gbc", chosen, o_blocks[0], preferred_element_type=jnp.float32)
    if group_count == 1 and grid_cols == GR and col_width == GR * DS:
        pieces = out_part[0].reshape(ROWS, GR, DS)
        my_cols = None
        for s in range(GR):
            piece = lax.dynamic_index_in_dim(pieces, grid_row ^ s, 1, keepdims=False)
            pairs = [(i * grid_cols + j, j * grid_cols + (i ^ s)) for i in range(GR) for j in range(grid_cols)]
            got = lax.ppermute(piece, "tp", pairs)
            my_cols = got if my_cols is None else my_cols + got
    else:
        placed = jnp.zeros((group_count, ROWS, D), jnp.float32)
        placed = lax.dynamic_update_slice_in_dim(placed, out_part, grid_col * col_width, 2)
        out_term = (
            placed.reshape(group_count, ROWS, ROLL, DS).transpose(0, 2, 1, 3).reshape(ranks * ROWS, DS)
        )
        my_cols = scatter_sum_xor(out_term.reshape(ranks, ROWS, DS), "tp")[0]
    return my_cols.astype(jnp.bfloat16)[None]


def solution(mesh):
    return jax.shard_map(
        local,
        mesh=mesh,
        in_specs=(
            P(("groups", "tp"), None, None),
            P(),
            P("tp", None, None, None),
            P("tp", None, None, None),
            P(None, None, "tp"),
            P(),
            P(("groups", "tp"), None, None, None),
            P(("groups", "tp"), None, None, None),
            P(("groups", "tp"), None),
        ),
        out_specs=P(("groups", "tp"), None, None),
        check_vma=False,
    )
```

```python
import jax
import jax.numpy as jnp
from jax import lax
from jax.sharding import PartitionSpec as P

D = 8192
KVH = 8
HD = 128
ROLL = 16
ROWS = 8
GR = 4
QG = 16
DS = 512


def from_partner(value, axis, bit):
    mask = 2**bit
    pairs = [(source, source ^ mask) for source in range(lax.axis_size(axis))]
    return lax.ppermute(value, axis, pairs)


def xor_swap(value, axis, bit):
    return from_partner(value, axis, bit)


def gather_xor(value, axis):
    n = lax.axis_size(axis)
    me = lax.axis_index(axis)
    held = value
    for bit in range(n.bit_length() - 1):
        other = xor_swap(held, axis, bit)
        low = ((me >> bit) & 1) == 0
        held = jnp.where(low, jnp.concatenate([held, other], 0), jnp.concatenate([other, held], 0))
    return held


def scatter_rounds(held, order, axis, bits):
    me = lax.axis_index(axis)
    for bit in bits:
        pos = order.index(bit)
        order = order[:pos] + order[pos + 1 :]
        low = ((me >> bit) & 1) == 0
        first = lax.index_in_dim(held, 0, pos, keepdims=False)
        second = lax.index_in_dim(held, 1, pos, keepdims=False)
        keep = jnp.where(low, first, second)
        give = jnp.where(low, second, first)
        held = keep + xor_swap(give, axis, bit)
    return held, order


def scatter_sum_xor(pieces, axis):
    n = lax.axis_size(axis)
    bits = n.bit_length() - 1
    me = lax.axis_index(axis)
    held = pieces.reshape((2,) * bits + pieces.shape[1:])
    order = list(range(bits - 1, -1, -1))
    for bit in range(bits):
        pos = order.index(bit)
        order.pop(pos)
        low = ((me >> bit) & 1) == 0
        first = lax.index_in_dim(held, 0, pos, keepdims=False)
        second = lax.index_in_dim(held, 1, pos, keepdims=False)
        keep = jnp.where(low, first, second)
        give = jnp.where(low, second, first)
        held = keep + xor_swap(give, axis, bit)
    return held[None]


def pick(table, idx):
    hit = idx[:, None] == jnp.arange(table.shape[0], dtype=idx.dtype)[None, :]
    hit = hit.reshape(hit.shape + (1,) * (table.ndim - 1))
    return jnp.sum(jnp.where(hit, table[None], jnp.zeros((), table.dtype)), axis=1)


def gather_rounds(held, axis, bits):
    me = lax.axis_index(axis)
    for bit in bits:
        other = xor_swap(held, axis, bit)
        low = ((me >> bit) & 1) == 0
        held = jnp.where(low, jnp.concatenate([held, other], 0), jnp.concatenate([other, held], 0))
    return held


def exchange_rounds(held, axis, bits):
    me = lax.axis_index(axis)
    count = len(bits)
    for done, bit in enumerate(bits):
        low = ((me >> bit) & 1) == 0
        first = lax.index_in_dim(held, 0, 0, keepdims=False)
        second = lax.index_in_dim(held, 1, 0, keepdims=False)
        keep = jnp.where(low, first, second)
        give = jnp.where(low, second, first)
        got = xor_swap(give, axis, bit)
        at = count - done - 1 + done
        held = jnp.where(low, jnp.stack([keep, got], at), jnp.stack([got, keep], at))
    return held


def swap_rows(value, axis, col_bits, s):
    shift = s << col_bits
    return lax.ppermute(value, axis, [(t, t ^ shift) for t in range(lax.axis_size(axis))])


def swap_cols(value, axis, s):
    return lax.ppermute(value, axis, [(t, t ^ s) for t in range(lax.axis_size(axis))])


def norm_rows(rows_float, norm_gain):
    mean_square = jnp.mean(rows_float * rows_float, axis=-1, keepdims=True)
    return (rows_float * lax.rsqrt(mean_square + 1e-05) * norm_gain[None, :]).astype(jnp.bfloat16)


def local(
    hidden_in, norm_gain, q_blocks, o_blocks, kv_blocks, kv_assign, key_cache, value_cache, lengths
):
    ranks = lax.axis_size("tp")
    my_index = lax.axis_index("tp")
    my_rank = my_index % ROLL
    my_half = my_rank % 2
    grid_cols = ranks // GR
    group_count = ranks // ROLL
    col_width = q_blocks.shape[3]
    key_width = kv_blocks.shape[2]
    grid_row = my_index // grid_cols
    grid_col = my_index % grid_cols
    dest_ids = jnp.arange(ranks, dtype=jnp.int32)
    dest_rank = dest_ids % ROLL
    dest_head = kv_assign[dest_rank]
    dest_group = 2 * dest_head + dest_rank % 2
    dest_copy = dest_ids // ROLL
    bits = ranks.bit_length() - 1
    col_bits = grid_cols.bit_length() - 1
    row_bits = GR.bit_length() - 1
    row_order = jnp.arange(GR, dtype=jnp.int32) ^ grid_row
    col_order = jnp.arange(grid_cols, dtype=jnp.int32) ^ grid_col
    direct_cols = grid_cols <= 4
    if direct_cols:
        from_cols = [hidden_in[0]] + [swap_cols(hidden_in[0], "tp", s) for s in range(1, grid_cols)]
        in_row = pick(jnp.stack(from_cols), col_order)
    else:
        in_row = gather_rounds(hidden_in, "tp", range(col_bits))
    from_rows = [in_row] + [swap_rows(in_row, "tp", col_bits, s) for s in range(1, GR)]
    every_rows = pick(jnp.stack(from_rows), row_order).reshape(ranks, ROWS, DS)
    rows_float = (
        every_rows.reshape(group_count, ROLL, ROWS, DS)
        .transpose(0, 2, 1, 3)
        .reshape(group_count * ROWS, D)
        .astype(jnp.float32)
    )
    normed_every = norm_rows(rows_float, norm_gain)
    col_rows = lax.dynamic_slice_in_dim(normed_every, grid_col * col_width, col_width, 1)
    query_part = jnp.einsum(
        "rc,aec->rae", col_rows, q_blocks[0], preferred_element_type=jnp.float32
    )
    query_part = (
        query_part.reshape(group_count, ROWS, QG, HD)
        .transpose(0, 2, 1, 3)
        .reshape(group_count * QG, ROWS, HD)
    )
    pair_first = dest_copy * QG + 2 * dest_head
    query_pick = jnp.concatenate([pick(query_part, pair_first), pick(query_part, pair_first + 1)], -1)
    key_rows = lax.dynamic_slice_in_dim(normed_every, my_index * key_width, key_width, 1)
    keyval_part = jnp.einsum("rc,kfc->rkf", key_rows, kv_blocks, preferred_element_type=jnp.float32)
    keyval_part = (
        keyval_part.reshape(group_count, ROWS, 2, KVH, HD)
        .transpose(0, 3, 1, 2, 4)
        .reshape(group_count * KVH, ROWS, 2 * HD)
    )
    keyval_term = pick(keyval_part, dest_copy * KVH + dest_head)
    width = 4 * HD
    compact = jnp.concatenate([query_pick, keyval_term], -1)
    if direct_cols:
        by_col = compact.reshape(GR, grid_cols, ROWS, width)
        held = lax.dynamic_index_in_dim(by_col, grid_col, 1, keepdims=False)
        for s in range(1, grid_cols):
            held = held + swap_cols(lax.dynamic_index_in_dim(by_col, grid_col ^ s, 1, keepdims=False), "tp", s)
    else:
        held, _ = scatter_rounds(
            compact.reshape((2,) * bits + (ROWS, width)), list(range(bits - 1, -1, -1)), "tp", range(col_bits)
        )
        held = held.reshape(GR, ROWS, width)
    from_rows = [lax.dynamic_index_in_dim(held, grid_row, 0, keepdims=False)]
    for s in range(1, GR):
        piece = lax.dynamic_index_in_dim(held, grid_row ^ s, 0, keepdims=False)
        from_rows.append(swap_rows(piece, "tp", col_bits, s))
    halves_q = [
        pick(jnp.stack([got[:, h * HD : (h + 1) * HD] for got in from_rows]), row_order) for h in range(2)
    ]
    both_queries = jnp.stack(halves_q).transpose(2, 0, 1, 3).reshape(ROWS, 2 * GR, HD).astype(jnp.bfloat16)
    keyval_sum = from_rows[0][:, 2 * HD :]
    for got in from_rows[1:]:
        keyval_sum = keyval_sum + got[:, 2 * HD :]
    keyval_new = keyval_sum.astype(jnp.bfloat16)
    key_new = keyval_new[:, :HD]
    value_new = keyval_new[:, HD:]
    scale = 1.0 / HD**0.5
    scores = (
        jnp.einsum("bhe,bte->bht", both_queries, key_cache[0], preferred_element_type=jnp.float32)
        * scale
    )
    positions = jnp.arange(scores.shape[2], dtype=jnp.int32)
    masked = positions[None, None, :] < lengths[0][:, None, None]
    new_score = (
        jnp.einsum("bhe,be->bh", both_queries, key_new, preferred_element_type=jnp.float32) * scale
    )
    new_score = jnp.where(my_half == 0, new_score, jnp.float32(-1e30))
    top = jnp.maximum(jnp.max(jnp.where(masked, scores, jnp.float32(-1e30)), axis=-1), new_score)
    weights = jnp.where(masked, jnp.exp(scores - top[..., None]), jnp.float32(0.0))
    new_weight = jnp.exp(new_score - top)
    total = jnp.sum(weights, axis=-1) + new_weight
    summed = jnp.einsum(
        "bht,bte->bhe",
        weights.astype(jnp.bfloat16),
        value_cache[0],
        preferred_element_type=jnp.float32,
    )
    new_rounded = lax.optimization_barrier(new_weight.astype(jnp.bfloat16)).astype(jnp.float32)
    summed = summed + new_rounded[..., None] * value_new.astype(jnp.float32)[:, None, :]
    top_split = top.reshape(ROWS, 2, GR)
    total_split = total.reshape(ROWS, 2, GR)
    summed_split = summed.reshape(ROWS, 2, GR, HD)
    first_half = my_half == 0
    own_top = jnp.where(first_half, top_split[:, 0], top_split[:, 1])
    own_total = jnp.where(first_half, total_split[:, 0], total_split[:, 1])
    own_summed = jnp.where(first_half, summed_split[:, 0], summed_split[:, 1])
    give_top = jnp.where(first_half, top_split[:, 1], top_split[:, 0])
    give_total = jnp.where(first_half, total_split[:, 1], total_split[:, 0])
    give_summed = jnp.where(first_half, summed_split[:, 1], summed_split[:, 0])
    stats = jnp.concatenate([give_top, give_total], -1)
    stats = jnp.pad(stats, ((0, 0), (0, HD - stats.shape[-1])))[:, None, :]
    got = from_partner(jnp.concatenate([give_summed, stats], 1), "tp", 0)
    got_summed = got[:, :GR]
    got_top, got_total = got[:, GR, :GR], got[:, GR, GR : 2 * GR]
    joint = jnp.maximum(own_top, got_top)
    factor_own = jnp.exp(own_top - joint)
    factor_got = jnp.exp(got_top - joint)
    numer = own_summed * factor_own[..., None] + got_summed * factor_got[..., None]
    denom = own_total * factor_own + got_total * factor_got
    attention = (numer / denom[..., None]).astype(jnp.bfloat16)
    from_rows = [lax.dynamic_index_in_dim(attention, grid_row, 1, keepdims=False)]
    for s in range(1, GR):
        piece = lax.dynamic_index_in_dim(attention, grid_row ^ s, 1, keepdims=False)
        from_rows.append(swap_rows(piece, "tp", col_bits, s))
    by_row = pick(jnp.stack(from_rows), row_order)
    if direct_cols:
        from_cols = [by_row] + [swap_cols(by_row, "tp", s) for s in range(1, grid_cols)]
        every_slot = pick(jnp.stack(from_cols), col_order)
    else:
        every_slot = gather_rounds(by_row[None], "tp", range(col_bits))
    every_slot = every_slot.transpose(1, 0, 2, 3).reshape(group_count, ROLL, ROWS, HD)
    head_ids = jnp.arange(KVH, dtype=jnp.int32)
    pair_heads = kv_assign[0::2]
    inverse = jnp.sum(
        head_ids[None, :] * (pair_heads[None, :] == head_ids[:, None]).astype(jnp.int32), axis=1
    )
    slot_ids = jnp.arange(QG, dtype=jnp.int32)
    rank_of_slot = 2 * inverse[slot_ids // 2] + slot_ids % 2
    chosen = jax.vmap(lambda per_group: pick(per_group, rank_of_slot))(every_slot)
    out_part = jnp.einsum("gabe,cae->gbc", chosen, o_blocks[0], preferred_element_type=jnp.float32)
    if group_count == 1 and grid_cols == GR and col_width == GR * DS:
        pieces = out_part[0].reshape(ROWS, GR, DS)
        my_cols = None
        for s in range(GR):
            piece = lax.dynamic_index_in_dim(pieces, grid_row ^ s, 1, keepdims=False)
            pairs = [(i * grid_cols + j, j * grid_cols + (i ^ s)) for i in range(GR) for j in range(grid_cols)]
            got = lax.ppermute(piece, "tp", pairs)
            my_cols = got if my_cols is None else my_cols + got
    else:
        placed = jnp.zeros((group_count, ROWS, D), jnp.float32)
        placed = lax.dynamic_update_slice_in_dim(placed, out_part, grid_col * col_width, 2)
        out_term = (
            placed.reshape(group_count, ROWS, ROLL, DS).transpose(0, 2, 1, 3).reshape(ranks * ROWS, DS)
        )
        my_cols = scatter_sum_xor(out_term.reshape(ranks, ROWS, DS), "tp")[0]
    return my_cols.astype(jnp.bfloat16)[None]


def solution(mesh):
    return jax.shard_map(
        local,
        mesh=mesh,
        in_specs=(
            P(("groups", "tp"), None, None),
            P(),
            P("tp", None, None, None),
            P("tp", None, None, None),
            P(None, None, "tp"),
            P(),
            P(("groups", "tp"), None, None, None),
            P(("groups", "tp"), None, None, None),
            P(("groups", "tp"), None),
        ),
        out_specs=P(("groups", "tp"), None, None),
        check_vma=False,
    )
```

```python
import jax
import jax.numpy as jnp
from jax import lax
from jax.sharding import PartitionSpec as P

D = 8192
KVH = 8
HD = 128
ROLL = 16
ROWS = 8
GR = 4
QG = 16
DS = 512


def from_partner(value, axis, bit):
    mask = 2**bit
    pairs = [(source, source ^ mask) for source in range(lax.axis_size(axis))]
    return lax.ppermute(value, axis, pairs)


def xor_swap(value, axis, bit):
    return from_partner(value, axis, bit)


def gather_xor(value, axis):
    n = lax.axis_size(axis)
    me = lax.axis_index(axis)
    held = value
    for bit in range(n.bit_length() - 1):
        other = xor_swap(held, axis, bit)
        low = ((me >> bit) & 1) == 0
        held = jnp.where(low, jnp.concatenate([held, other], 0), jnp.concatenate([other, held], 0))
    return held


def scatter_rounds(held, order, axis, bits):
    me = lax.axis_index(axis)
    for bit in bits:
        pos = order.index(bit)
        order = order[:pos] + order[pos + 1 :]
        low = ((me >> bit) & 1) == 0
        first = lax.index_in_dim(held, 0, pos, keepdims=False)
        second = lax.index_in_dim(held, 1, pos, keepdims=False)
        keep = jnp.where(low, first, second)
        give = jnp.where(low, second, first)
        held = keep + xor_swap(give, axis, bit)
    return held, order


def scatter_sum_xor(pieces, axis):
    n = lax.axis_size(axis)
    bits = n.bit_length() - 1
    me = lax.axis_index(axis)
    held = pieces.reshape((2,) * bits + pieces.shape[1:])
    order = list(range(bits - 1, -1, -1))
    for bit in range(bits):
        pos = order.index(bit)
        order.pop(pos)
        low = ((me >> bit) & 1) == 0
        first = lax.index_in_dim(held, 0, pos, keepdims=False)
        second = lax.index_in_dim(held, 1, pos, keepdims=False)
        keep = jnp.where(low, first, second)
        give = jnp.where(low, second, first)
        held = keep + xor_swap(give, axis, bit)
    return held[None]


def pick(table, idx):
    hit = idx[:, None] == jnp.arange(table.shape[0], dtype=idx.dtype)[None, :]
    hit = hit.reshape(hit.shape + (1,) * (table.ndim - 1))
    return jnp.sum(jnp.where(hit, table[None], jnp.zeros((), table.dtype)), axis=1)


def gather_rounds(held, axis, bits):
    me = lax.axis_index(axis)
    for bit in bits:
        other = xor_swap(held, axis, bit)
        low = ((me >> bit) & 1) == 0
        held = jnp.where(low, jnp.concatenate([held, other], 0), jnp.concatenate([other, held], 0))
    return held


def exchange_rounds(held, axis, bits):
    me = lax.axis_index(axis)
    count = len(bits)
    for done, bit in enumerate(bits):
        low = ((me >> bit) & 1) == 0
        first = lax.index_in_dim(held, 0, 0, keepdims=False)
        second = lax.index_in_dim(held, 1, 0, keepdims=False)
        keep = jnp.where(low, first, second)
        give = jnp.where(low, second, first)
        got = xor_swap(give, axis, bit)
        at = count - done - 1 + done
        held = jnp.where(low, jnp.stack([keep, got], at), jnp.stack([got, keep], at))
    return held


def swap_rows(value, axis, col_bits, s):
    shift = s << col_bits
    return lax.ppermute(value, axis, [(t, t ^ shift) for t in range(lax.axis_size(axis))])


def swap_cols(value, axis, s):
    return lax.ppermute(value, axis, [(t, t ^ s) for t in range(lax.axis_size(axis))])


def norm_rows(rows_float, norm_gain):
    mean_square = jnp.mean(rows_float * rows_float, axis=-1, keepdims=True)
    return (rows_float * lax.rsqrt(mean_square + 1e-05) * norm_gain[None, :]).astype(jnp.bfloat16)


def local(
    hidden_in, norm_gain, q_blocks, o_blocks, kv_blocks, kv_assign, key_cache, value_cache, lengths
):
    ranks = lax.axis_size("tp")
    my_index = lax.axis_index("tp")
    my_rank = my_index % ROLL
    my_half = my_rank % 2
    grid_cols = ranks // GR
    group_count = ranks // ROLL
    col_width = q_blocks.shape[3]
    key_width = kv_blocks.shape[2]
    grid_row = my_index // grid_cols
    grid_col = my_index % grid_cols
    dest_ids = jnp.arange(ranks, dtype=jnp.int32)
    dest_rank = dest_ids % ROLL
    dest_head = pick(kv_assign, dest_rank)
    dest_group = 2 * dest_head + dest_rank % 2
    dest_copy = dest_ids // ROLL
    bits = ranks.bit_length() - 1
    col_bits = grid_cols.bit_length() - 1
    row_bits = GR.bit_length() - 1
    row_order = jnp.arange(GR, dtype=jnp.int32) ^ grid_row
    col_order = jnp.arange(grid_cols, dtype=jnp.int32) ^ grid_col
    direct_cols = grid_cols <= 4
    fast_norm = direct_cols and group_count == 1 and GR == grid_cols and col_width == grid_cols * DS
    fast_norm = fast_norm and key_width == DS
    if direct_cols:
        from_cols = [hidden_in[0]] + [swap_cols(hidden_in[0], "tp", s) for s in range(1, grid_cols)]
        in_row = jnp.stack(from_cols)
        if not fast_norm:
            in_row = pick(in_row, col_order)
    else:
        in_row = gather_rounds(hidden_in, "tp", range(col_bits))
    from_rows = [in_row] + [swap_rows(in_row, "tp", col_bits, s) for s in range(1, GR)]
    if fast_norm:
        arrived = jnp.stack(from_rows).astype(jnp.float32)
        mean_square = jnp.sum(arrived * arrived, axis=(0, 1, 3))[:, None] / D
        scale_rows = lax.rsqrt(mean_square + 1e-05)
        col_x = pick(lax.dynamic_index_in_dim(arrived, grid_row ^ grid_col, 0, keepdims=False), col_order)
        col_x = col_x.transpose(1, 0, 2).reshape(ROWS, col_width)
        col_gain = lax.dynamic_slice_in_dim(norm_gain, grid_col * col_width, col_width)
        col_rows = (col_x * scale_rows * col_gain[None, :]).astype(jnp.bfloat16)
        own_gain = lax.dynamic_slice_in_dim(norm_gain, my_index * key_width, key_width)
        key_rows = (hidden_in[0].astype(jnp.float32) * scale_rows * own_gain[None, :]).astype(jnp.bfloat16)
    else:
        every_rows = pick(jnp.stack(from_rows), row_order).reshape(ranks, ROWS, DS)
        rows_float = (
            every_rows.reshape(group_count, ROLL, ROWS, DS)
            .transpose(0, 2, 1, 3)
            .reshape(group_count * ROWS, D)
            .astype(jnp.float32)
        )
        normed_every = norm_rows(rows_float, norm_gain)
        col_rows = lax.dynamic_slice_in_dim(normed_every, grid_col * col_width, col_width, 1)
        key_rows = lax.dynamic_slice_in_dim(normed_every, my_index * key_width, key_width, 1)
    query_part = jnp.einsum(
        "rc,aec->rae", col_rows, q_blocks[0], preferred_element_type=jnp.float32
    )
    query_part = (
        query_part.reshape(group_count, ROWS, QG, HD)
        .transpose(0, 2, 1, 3)
        .reshape(group_count * QG, ROWS, HD)
    )
    query_pairs = pick(query_part.reshape(group_count * KVH, 2, ROWS, HD), dest_copy * KVH + dest_head)
    query_pick = query_pairs.transpose(0, 2, 1, 3).reshape(ranks, ROWS, 2 * HD)
    keyval_part = jnp.einsum("rc,kfc->rkf", key_rows, kv_blocks, preferred_element_type=jnp.float32)
    keyval_part = (
        keyval_part.reshape(group_count, ROWS, 2, KVH, HD)
        .transpose(0, 3, 1, 2, 4)
        .reshape(group_count * KVH, ROWS, 2 * HD)
    )
    keyval_term = pick(keyval_part, dest_copy * KVH + dest_head)
    width = 4 * HD
    compact = jnp.concatenate([query_pick, keyval_term], -1)
    if direct_cols:
        by_col = compact.reshape(GR, grid_cols, ROWS, width)
        held = lax.dynamic_index_in_dim(by_col, grid_col, 1, keepdims=False)
        for s in range(1, grid_cols):
            held = held + swap_cols(lax.dynamic_index_in_dim(by_col, grid_col ^ s, 1, keepdims=False), "tp", s)
    else:
        held, _ = scatter_rounds(
            compact.reshape((2,) * bits + (ROWS, width)), list(range(bits - 1, -1, -1)), "tp", range(col_bits)
        )
        held = held.reshape(GR, ROWS, width)
    from_rows = [lax.dynamic_index_in_dim(held, grid_row, 0, keepdims=False)]
    for s in range(1, GR):
        piece = lax.dynamic_index_in_dim(held, grid_row ^ s, 0, keepdims=False)
        from_rows.append(swap_rows(piece, "tp", col_bits, s))
    halves_q = [
        pick(jnp.stack([got[:, h * HD : (h + 1) * HD] for got in from_rows]), row_order) for h in range(2)
    ]
    both_queries = jnp.stack(halves_q).transpose(2, 0, 1, 3).reshape(ROWS, 2 * GR, HD).astype(jnp.bfloat16)
    keyval_sum = from_rows[0][:, 2 * HD :]
    for got in from_rows[1:]:
        keyval_sum = keyval_sum + got[:, 2 * HD :]
    keyval_new = keyval_sum.astype(jnp.bfloat16)
    key_new = keyval_new[:, :HD]
    value_new = keyval_new[:, HD:]
    scale = 1.0 / HD**0.5
    scores = (
        jnp.einsum("bhe,bte->bht", both_queries, key_cache[0], preferred_element_type=jnp.float32)
        * scale
    )
    positions = jnp.arange(scores.shape[2], dtype=jnp.int32)
    masked = positions[None, None, :] < lengths[0][:, None, None]
    new_score = (
        jnp.einsum("bhe,be->bh", both_queries, key_new, preferred_element_type=jnp.float32) * scale
    )
    new_score = jnp.where(my_half == 0, new_score, jnp.float32(-1e30))
    top = jnp.maximum(jnp.max(jnp.where(masked, scores, jnp.float32(-1e30)), axis=-1), new_score)
    weights = jnp.where(masked, jnp.exp(scores - top[..., None]), jnp.float32(0.0))
    new_weight = jnp.exp(new_score - top)
    total = jnp.sum(weights, axis=-1) + new_weight
    summed = jnp.einsum(
        "bht,bte->bhe",
        weights.astype(jnp.bfloat16),
        value_cache[0],
        preferred_element_type=jnp.float32,
    )
    new_rounded = lax.optimization_barrier(new_weight.astype(jnp.bfloat16)).astype(jnp.float32)
    summed = summed + new_rounded[..., None] * value_new.astype(jnp.float32)[:, None, :]
    top_split = top.reshape(ROWS, 2, GR)
    total_split = total.reshape(ROWS, 2, GR)
    summed_split = summed.reshape(ROWS, 2, GR, HD)
    first_half = my_half == 0
    own_top = jnp.where(first_half, top_split[:, 0], top_split[:, 1])
    own_total = jnp.where(first_half, total_split[:, 0], total_split[:, 1])
    own_summed = jnp.where(first_half, summed_split[:, 0], summed_split[:, 1])
    give_top = jnp.where(first_half, top_split[:, 1], top_split[:, 0])
    give_total = jnp.where(first_half, total_split[:, 1], total_split[:, 0])
    give_summed = jnp.where(first_half, summed_split[:, 1], summed_split[:, 0])
    stats = jnp.concatenate([give_top, give_total], -1)
    stats = jnp.pad(stats, ((0, 0), (0, HD - stats.shape[-1])))[:, None, :]
    got = from_partner(jnp.concatenate([give_summed, stats], 1), "tp", 0)
    got_summed = got[:, :GR]
    got_top, got_total = got[:, GR, :GR], got[:, GR, GR : 2 * GR]
    joint = jnp.maximum(own_top, got_top)
    factor_own = jnp.exp(own_top - joint)
    factor_got = jnp.exp(got_top - joint)
    numer = own_summed * factor_own[..., None] + got_summed * factor_got[..., None]
    denom = own_total * factor_own + got_total * factor_got
    attention = (numer / denom[..., None]).astype(jnp.bfloat16)
    from_rows = [lax.dynamic_index_in_dim(attention, grid_row, 1, keepdims=False)]
    for s in range(1, GR):
        piece = lax.dynamic_index_in_dim(attention, grid_row ^ s, 1, keepdims=False)
        from_rows.append(swap_rows(piece, "tp", col_bits, s))
    by_row = pick(jnp.stack(from_rows), row_order)
    if direct_cols:
        from_cols = [by_row] + [swap_cols(by_row, "tp", s) for s in range(1, grid_cols)]
        every_slot = pick(jnp.stack(from_cols), col_order)
    else:
        every_slot = gather_rounds(by_row[None], "tp", range(col_bits))
    every_slot = every_slot.transpose(1, 0, 2, 3).reshape(group_count, ROLL, ROWS, HD)
    head_ids = jnp.arange(KVH, dtype=jnp.int32)
    pair_heads = kv_assign.reshape(KVH, 2)[:, 0]
    inverse = jnp.sum(
        head_ids[None, :] * (pair_heads[None, :] == head_ids[:, None]).astype(jnp.int32), axis=1
    )
    slot_ids = jnp.arange(QG, dtype=jnp.int32)
    rank_of_slot = 2 * jnp.broadcast_to(inverse[:, None], (KVH, 2)).reshape(QG) + slot_ids % 2
    chosen = jax.vmap(lambda per_group: pick(per_group, rank_of_slot))(every_slot)
    out_part = jnp.einsum("gabe,cae->gbc", chosen, o_blocks[0], preferred_element_type=jnp.float32)
    if group_count == 1 and grid_cols == GR and col_width == GR * DS:
        pieces = out_part[0].reshape(ROWS, GR, DS)
        my_cols = None
        for s in range(GR):
            piece = lax.dynamic_index_in_dim(pieces, grid_row ^ s, 1, keepdims=False)
            pairs = [(i * grid_cols + j, j * grid_cols + (i ^ s)) for i in range(GR) for j in range(grid_cols)]
            got = lax.ppermute(piece, "tp", pairs)
            my_cols = got if my_cols is None else my_cols + got
    else:
        placed = jnp.zeros((group_count, ROWS, D), jnp.float32)
        placed = lax.dynamic_update_slice_in_dim(placed, out_part, grid_col * col_width, 2)
        out_term = (
            placed.reshape(group_count, ROWS, ROLL, DS).transpose(0, 2, 1, 3).reshape(ranks * ROWS, DS)
        )
        my_cols = scatter_sum_xor(out_term.reshape(ranks, ROWS, DS), "tp")[0]
    return my_cols.astype(jnp.bfloat16)[None]


def solution(mesh):
    return jax.shard_map(
        local,
        mesh=mesh,
        in_specs=(
            P(("groups", "tp"), None, None),
            P(),
            P("tp", None, None, None),
            P("tp", None, None, None),
            P(None, None, "tp"),
            P(),
            P(("groups", "tp"), None, None, None),
            P(("groups", "tp"), None, None, None),
            P(("groups", "tp"), None),
        ),
        out_specs=P(("groups", "tp"), None, None),
        check_vma=False,
    )
```

```python
import jax
import jax.numpy as jnp
from jax import lax
from jax.sharding import PartitionSpec as P

D = 8192
KVH = 8
HD = 128
ROLL = 16
ROWS = 8
GR = 4
QG = 16
DS = 512


def from_partner(value, axis, bit):
    mask = 2**bit
    pairs = [(source, source ^ mask) for source in range(lax.axis_size(axis))]
    return lax.ppermute(value, axis, pairs)


def xor_swap(value, axis, bit):
    return from_partner(value, axis, bit)


def gather_xor(value, axis):
    n = lax.axis_size(axis)
    me = lax.axis_index(axis)
    held = value
    for bit in range(n.bit_length() - 1):
        other = xor_swap(held, axis, bit)
        low = ((me >> bit) & 1) == 0
        held = jnp.where(low, jnp.concatenate([held, other], 0), jnp.concatenate([other, held], 0))
    return held


def scatter_rounds(held, order, axis, bits):
    me = lax.axis_index(axis)
    for bit in bits:
        pos = order.index(bit)
        order = order[:pos] + order[pos + 1 :]
        low = ((me >> bit) & 1) == 0
        first = lax.index_in_dim(held, 0, pos, keepdims=False)
        second = lax.index_in_dim(held, 1, pos, keepdims=False)
        keep = jnp.where(low, first, second)
        give = jnp.where(low, second, first)
        held = keep + xor_swap(give, axis, bit)
    return held, order


def scatter_sum_xor(pieces, axis):
    n = lax.axis_size(axis)
    bits = n.bit_length() - 1
    me = lax.axis_index(axis)
    held = pieces.reshape((2,) * bits + pieces.shape[1:])
    order = list(range(bits - 1, -1, -1))
    for bit in range(bits):
        pos = order.index(bit)
        order.pop(pos)
        low = ((me >> bit) & 1) == 0
        first = lax.index_in_dim(held, 0, pos, keepdims=False)
        second = lax.index_in_dim(held, 1, pos, keepdims=False)
        keep = jnp.where(low, first, second)
        give = jnp.where(low, second, first)
        held = keep + xor_swap(give, axis, bit)
    return held[None]


def pick(table, idx):
    hit = idx[:, None] == jnp.arange(table.shape[0], dtype=idx.dtype)[None, :]
    hit = hit.reshape(hit.shape + (1,) * (table.ndim - 1))
    return jnp.sum(jnp.where(hit, table[None], jnp.zeros((), table.dtype)), axis=1)


def gather_rounds(held, axis, bits):
    me = lax.axis_index(axis)
    for bit in bits:
        other = xor_swap(held, axis, bit)
        low = ((me >> bit) & 1) == 0
        held = jnp.where(low, jnp.concatenate([held, other], 0), jnp.concatenate([other, held], 0))
    return held


def exchange_rounds(held, axis, bits):
    me = lax.axis_index(axis)
    count = len(bits)
    for done, bit in enumerate(bits):
        low = ((me >> bit) & 1) == 0
        first = lax.index_in_dim(held, 0, 0, keepdims=False)
        second = lax.index_in_dim(held, 1, 0, keepdims=False)
        keep = jnp.where(low, first, second)
        give = jnp.where(low, second, first)
        got = xor_swap(give, axis, bit)
        at = count - done - 1 + done
        held = jnp.where(low, jnp.stack([keep, got], at), jnp.stack([got, keep], at))
    return held


def swap_rows(value, axis, col_bits, s):
    shift = s << col_bits
    return lax.ppermute(value, axis, [(t, t ^ shift) for t in range(lax.axis_size(axis))])


def swap_cols(value, axis, s):
    return lax.ppermute(value, axis, [(t, t ^ s) for t in range(lax.axis_size(axis))])


def norm_rows(rows_float, norm_gain):
    mean_square = jnp.mean(rows_float * rows_float, axis=-1, keepdims=True)
    return (rows_float * lax.rsqrt(mean_square + 1e-05) * norm_gain[None, :]).astype(jnp.bfloat16)


def local(
    hidden_in, norm_gain, q_blocks, o_blocks, kv_blocks, kv_assign, key_cache, value_cache, lengths
):
    ranks = lax.axis_size("tp")
    my_index = lax.axis_index("tp")
    my_rank = my_index % ROLL
    my_half = my_rank % 2
    grid_cols = ranks // GR
    group_count = ranks // ROLL
    col_width = q_blocks.shape[3]
    key_width = kv_blocks.shape[2]
    grid_row = my_index // grid_cols
    grid_col = my_index % grid_cols
    dest_ids = jnp.arange(ranks, dtype=jnp.int32)
    dest_rank = dest_ids % ROLL
    dest_head = kv_assign[dest_rank]
    dest_group = 2 * dest_head + dest_rank % 2
    dest_copy = dest_ids // ROLL
    bits = ranks.bit_length() - 1
    col_bits = grid_cols.bit_length() - 1
    row_bits = GR.bit_length() - 1
    row_order = jnp.arange(GR, dtype=jnp.int32) ^ grid_row
    col_order = jnp.arange(grid_cols, dtype=jnp.int32) ^ grid_col
    direct_cols = grid_cols <= 4
    if direct_cols:
        from_cols = [hidden_in[0]] + [swap_cols(hidden_in[0], "tp", s) for s in range(1, grid_cols)]
        in_row = pick(jnp.stack(from_cols), col_order)
    else:
        in_row = gather_rounds(hidden_in, "tp", range(col_bits))
    from_rows = [in_row] + [swap_rows(in_row, "tp", col_bits, s) for s in range(1, GR)]
    every_rows = pick(jnp.stack(from_rows), row_order).reshape(ranks, ROWS, DS)
    rows_float = (
        every_rows.reshape(group_count, ROLL, ROWS, DS)
        .transpose(0, 2, 1, 3)
        .reshape(group_count * ROWS, D)
        .astype(jnp.float32)
    )
    normed_every = norm_rows(rows_float, norm_gain)
    col_rows = lax.dynamic_slice_in_dim(normed_every, grid_col * col_width, col_width, 1)
    query_part = jnp.einsum(
        "rc,aec->rae", col_rows, q_blocks[0], preferred_element_type=jnp.float32
    )
    query_part = (
        query_part.reshape(group_count, ROWS, QG, HD)
        .transpose(0, 2, 1, 3)
        .reshape(group_count * QG, ROWS, HD)
    )
    pair_first = dest_copy * QG + 2 * dest_head
    query_pick = jnp.concatenate([pick(query_part, pair_first), pick(query_part, pair_first + 1)], -1)
    key_rows = lax.dynamic_slice_in_dim(normed_every, my_index * key_width, key_width, 1)
    keyval_part = jnp.einsum("rc,kfc->rkf", key_rows, kv_blocks, preferred_element_type=jnp.float32)
    keyval_part = (
        keyval_part.reshape(group_count, ROWS, 2, KVH, HD)
        .transpose(0, 3, 1, 2, 4)
        .reshape(group_count * KVH, ROWS, 2 * HD)
    )
    keyval_term = pick(keyval_part, dest_copy * KVH + dest_head)
    width = 4 * HD
    compact = jnp.concatenate([query_pick, keyval_term], -1)
    if direct_cols:
        by_col = compact.reshape(GR, grid_cols, ROWS, width)
        held = lax.dynamic_index_in_dim(by_col, grid_col, 1, keepdims=False)
        for s in range(1, grid_cols):
            held = held + swap_cols(lax.dynamic_index_in_dim(by_col, grid_col ^ s, 1, keepdims=False), "tp", s)
    else:
        held, _ = scatter_rounds(
            compact.reshape((2,) * bits + (ROWS, width)), list(range(bits - 1, -1, -1)), "tp", range(col_bits)
        )
        held = held.reshape(GR, ROWS, width)
    from_rows = [lax.dynamic_index_in_dim(held, grid_row, 0, keepdims=False)]
    for s in range(1, GR):
        piece = lax.dynamic_index_in_dim(held, grid_row ^ s, 0, keepdims=False)
        from_rows.append(swap_rows(piece, "tp", col_bits, s))
    halves_q = [
        pick(jnp.stack([got[:, h * HD : (h + 1) * HD] for got in from_rows]), row_order) for h in range(2)
    ]
    both_queries = jnp.stack(halves_q).transpose(2, 0, 1, 3).reshape(ROWS, 2 * GR, HD).astype(jnp.bfloat16)
    keyval_sum = from_rows[0][:, 2 * HD :]
    for got in from_rows[1:]:
        keyval_sum = keyval_sum + got[:, 2 * HD :]
    keyval_new = keyval_sum.astype(jnp.bfloat16)
    key_new = keyval_new[:, :HD]
    value_new = keyval_new[:, HD:]
    scale = 1.0 / HD**0.5
    scores = (
        jnp.einsum("bhe,bte->bht", both_queries, key_cache[0], preferred_element_type=jnp.float32)
        * scale
    )
    positions = jnp.arange(scores.shape[2], dtype=jnp.int32)
    masked = positions[None, None, :] < lengths[0][:, None, None]
    new_score = (
        jnp.einsum("bhe,be->bh", both_queries, key_new, preferred_element_type=jnp.float32) * scale
    )
    new_score = jnp.where(my_half == 0, new_score, jnp.float32(-1e30))
    top = jnp.maximum(jnp.max(jnp.where(masked, scores, jnp.float32(-1e30)), axis=-1), new_score)
    weights = jnp.where(masked, jnp.exp(scores - top[..., None]), jnp.float32(0.0))
    new_weight = jnp.exp(new_score - top)
    total = jnp.sum(weights, axis=-1) + new_weight
    summed = jnp.einsum(
        "bht,bte->bhe",
        weights.astype(jnp.bfloat16),
        value_cache[0],
        preferred_element_type=jnp.float32,
    )
    new_rounded = lax.optimization_barrier(new_weight.astype(jnp.bfloat16)).astype(jnp.float32)
    summed = summed + new_rounded[..., None] * value_new.astype(jnp.float32)[:, None, :]
    top_split = top.reshape(ROWS, 2, GR)
    total_split = total.reshape(ROWS, 2, GR)
    summed_split = summed.reshape(ROWS, 2, GR, HD)
    first_half = my_half == 0
    own_top = jnp.where(first_half, top_split[:, 0], top_split[:, 1])
    own_total = jnp.where(first_half, total_split[:, 0], total_split[:, 1])
    own_summed = jnp.where(first_half, summed_split[:, 0], summed_split[:, 1])
    give_top = jnp.where(first_half, top_split[:, 1], top_split[:, 0])
    give_total = jnp.where(first_half, total_split[:, 1], total_split[:, 0])
    give_summed = jnp.where(first_half, summed_split[:, 1], summed_split[:, 0])
    stats = jnp.concatenate([give_top, give_total], -1)
    stats = jnp.pad(stats, ((0, 0), (0, HD - stats.shape[-1])))[:, None, :]
    got = from_partner(jnp.concatenate([give_summed, stats], 1), "tp", 0)
    got_summed = got[:, :GR]
    got_top, got_total = got[:, GR, :GR], got[:, GR, GR : 2 * GR]
    joint = jnp.maximum(own_top, got_top)
    factor_own = jnp.exp(own_top - joint)
    factor_got = jnp.exp(got_top - joint)
    numer = own_summed * factor_own[..., None] + got_summed * factor_got[..., None]
    denom = own_total * factor_own + got_total * factor_got
    attention = (numer / denom[..., None]).astype(jnp.bfloat16)
    attention = attention.astype(jnp.float32)
    from_rows = [lax.dynamic_index_in_dim(attention, grid_row, 1, keepdims=False)]
    for s in range(1, GR):
        piece = lax.dynamic_index_in_dim(attention, grid_row ^ s, 1, keepdims=False)
        from_rows.append(swap_rows(piece, "tp", col_bits, s))
    by_row = pick(jnp.stack(from_rows), row_order)
    if direct_cols:
        from_cols = [by_row] + [swap_cols(by_row, "tp", s) for s in range(1, grid_cols)]
        every_slot = pick(jnp.stack(from_cols), col_order)
    else:
        every_slot = gather_rounds(by_row[None], "tp", range(col_bits))
    every_slot = every_slot.transpose(1, 0, 2, 3).reshape(group_count, ROLL, ROWS, HD)
    head_ids = jnp.arange(KVH, dtype=jnp.int32)
    pair_heads = kv_assign[0::2]
    inverse = jnp.sum(
        head_ids[None, :] * (pair_heads[None, :] == head_ids[:, None]).astype(jnp.int32), axis=1
    )
    slot_ids = jnp.arange(QG, dtype=jnp.int32)
    rank_of_slot = 2 * inverse[slot_ids // 2] + slot_ids % 2
    chosen = jax.vmap(lambda per_group: pick(per_group, rank_of_slot))(every_slot).astype(jnp.bfloat16)
    out_part = jnp.einsum("gabe,cae->gbc", chosen, o_blocks[0], preferred_element_type=jnp.float32)
    if group_count == 1 and grid_cols == GR and col_width == GR * DS:
        pieces = out_part[0].reshape(ROWS, GR, DS)
        my_cols = None
        for s in range(GR):
            piece = lax.dynamic_index_in_dim(pieces, grid_row ^ s, 1, keepdims=False)
            pairs = [(i * grid_cols + j, j * grid_cols + (i ^ s)) for i in range(GR) for j in range(grid_cols)]
            got = lax.ppermute(piece, "tp", pairs)
            my_cols = got if my_cols is None else my_cols + got
    else:
        placed = jnp.zeros((group_count, ROWS, D), jnp.float32)
        placed = lax.dynamic_update_slice_in_dim(placed, out_part, grid_col * col_width, 2)
        out_term = (
            placed.reshape(group_count, ROWS, ROLL, DS).transpose(0, 2, 1, 3).reshape(ranks * ROWS, DS)
        )
        my_cols = scatter_sum_xor(out_term.reshape(ranks, ROWS, DS), "tp")[0]
    return my_cols.astype(jnp.bfloat16)[None]


def solution(mesh):
    return jax.shard_map(
        local,
        mesh=mesh,
        in_specs=(
            P(("groups", "tp"), None, None),
            P(),
            P("tp", None, None, None),
            P("tp", None, None, None),
            P(None, None, "tp"),
            P(),
            P(("groups", "tp"), None, None, None),
            P(("groups", "tp"), None, None, None),
            P(("groups", "tp"), None),
        ),
        out_specs=P(("groups", "tp"), None, None),
        check_vma=False,
    )
```
